128 devices in a mesh: outer: 16 (over z, x), inner: 8 (over y, core).
Axes of the slice: x: 4, y: 4, z: 4, core: 2. Of those that a mesh axis runs over, the one named last changes fastest.
Arguments:
- features: bfloat16 [4194304, 64], P(('outer', 'inner')), may hold values from -6 to 6
- block_offset: int32 [32768], P(('outer', 'inner')), may hold values from 0 to 7
- parent_entry: int32 [4194304], P(('outer', 'inner')), may hold values from 0 to 8191, as said below
- owner_cell: int32 [128, 8192], P(('outer', 'inner')), may hold values from 0 to 4096, as said below
- w_down: bfloat16 [8, 64, 128], replicated, may hold values from -0.25 to 0.25
- b_down: float32 [128], replicated, may hold values from -3 to 3
- w_up: bfloat16 [8, 128, 64], replicated, may hold values from -0.5 to 0.5
Outputs:
- refined: bfloat16 [4194304, 64], P(('outer', 'inner'))
The draws below stay inside these ranges and needn't reach their ends.
Inputs may be any that keep to these rules, and one draw needn't show every extreme that they name: `parent_entry`: each device's parent list has 4096 entries for cells it owns, then 8 groups of 512 slots, group g for the neighbour at step g as in the reference program. In each group the first c slots are used (1 <= c <= 512), the rest empty; group 7 and one more group have all 512 slots used on every device. A voxel names a used entry of its own device; all voxels of one brick of 128 name entries of one aligned window of 128 entries (entries k * 128 to k * 128 + 127), lying in one group or among the device's own entries, and every neighbour group is named by some brick of every device. owner_cell[d, e] for e < 4096 is the cell of d's own entry e; for e >= 4096 it is the cell named by that entry of the device at d's position minus the step of group (e - 4096) // 512, or 4096 where that slot is empty. The used entries of one aligned window of 128 entries name cells of one aligned window of 128 cells.
All inputs are finite; a program needn't handle non-finite values.
Results may differ from the reference program's by a relative error of at most 0.017.
Values may be sent and summed in bfloat16 or wider, within the bound.
No kernel may reach another device: no remote copies, remote signals or barrier semaphores. Data moves between devices by JAX's collectives and lax.ppermute only.
A program may use at most 128 MiB of HBM per device.

```python
import jax
import jax.numpy as jnp
from jax import lax

C_IN = 64
C_OUT = 128
KERNEL = 8
BLK = 128
NEIGH = 8
F_DEV = 32768
C_DEV = 4096
SELF_CAP = 4096
CAP = 512
WIN = 128
ENTRIES = 8192
OWNERS = 128
FINE = 4194304
N_OUTER = 16
N_INNER = 8


step_table = ((-1, -1), (-1, 0), (-1, 1), (0, -1), (0, 1), (1, -1), (1, 0), (1, 1))


def routing_tables(key):
    keys = jax.random.split(jax.random.fold_in(key, 7), 10)
    counts = jax.random.randint(keys[0], (OWNERS, NEIGH), 1, CAP + 1)
    extra = jax.random.randint(keys[1], (OWNERS, 1), 0, NEIGH - 1)
    groups = jnp.arange(NEIGH)[None, :]
    counts = jnp.where((groups == NEIGH - 1) | (groups == extra), CAP, counts)
    return (counts, keys)


def draw_parent_entry(key, part):
    counts, keys = routing_tables(key)
    blocks = F_DEV // BLK
    rotation = jax.random.randint(keys[3], (OWNERS, 1), 0, NEIGH)
    block_ids = jnp.arange(blocks)[None, :]
    first_groups = (block_ids + rotation) % NEIGH
    choice_bits = jax.random.randint(keys[2], (OWNERS, blocks, 2), 0, 1 << 20)
    later_groups = jnp.where(choice_bits[:, :, 0] % 2 == 0, NEIGH, choice_bits[:, :, 1] % NEIGH)
    block_group = jnp.where(block_ids < NEIGH, first_groups, later_groups)
    safe_group = jnp.minimum(block_group, NEIGH - 1)
    group_count = jnp.take_along_axis(counts, safe_group, axis=1)
    live_windows = (group_count + WIN - 1) // WIN
    window_raw = jax.random.randint(keys[8], (OWNERS, blocks), 0, 1 << 20)
    last_block = (NEIGH - 1 - rotation) % NEIGH
    is_last = block_ids == last_block
    far_window = jnp.where(is_last, live_windows - 1, window_raw % live_windows)
    self_window = window_raw % (SELF_CAP // WIN)
    live_slots = jnp.minimum(WIN, group_count - far_window * WIN)
    far_base = SELF_CAP + safe_group * CAP + far_window * WIN
    self_base = self_window * WIN
    is_self = block_group == NEIGH
    base = jnp.where(is_self, self_base, far_base)
    limit = jnp.where(is_self, WIN, live_slots)
    base_v = jnp.repeat(base, BLK, axis=1)
    limit_v = jnp.repeat(limit, BLK, axis=1)
    raw_slots = jax.random.randint(keys[4], (OWNERS, F_DEV), 0, 1 << 20)
    entry_ids = base_v + raw_slots % limit_v
    forced = jnp.arange(F_DEV)[None, :] == last_block * BLK + BLK - 1
    entry_ids = jnp.where(forced, ENTRIES - 1, entry_ids)
    return entry_ids.reshape(OWNERS * F_DEV).astype(jnp.int32)


def draw_owner_cell(key, part):
    counts, keys = routing_tables(key)
    cell_windows = C_DEV // WIN
    far_window = jax.random.randint(keys[9], (OWNERS, NEIGH, CAP // WIN), 0, cell_windows)
    far_inside = jax.random.randint(keys[5], (OWNERS, NEIGH, CAP), 0, WIN)
    slot_cells = jnp.repeat(far_window, WIN, axis=2) * WIN + far_inside
    live = jnp.arange(CAP)[None, None, :] < counts[:, :, None]
    slot_cells = jnp.where(live, slot_cells, C_DEV)
    steps = jnp.array(step_table, dtype=jnp.int32)
    owners = jnp.arange(OWNERS, dtype=jnp.int32)[:, None]
    row_pos = owners // N_INNER
    col_pos = owners % N_INNER
    senders = (row_pos - steps[None, :, 0]) % N_OUTER * N_INNER + (col_pos - steps[None, :, 1]) % N_INNER
    far = slot_cells[senders, jnp.arange(NEIGH, dtype=jnp.int32)[None, :]]
    own_window = jax.random.randint(keys[7], (OWNERS, SELF_CAP // WIN), 0, cell_windows)
    own_inside = jax.random.randint(keys[6], (OWNERS, SELF_CAP), 0, WIN)
    own = jnp.repeat(own_window, WIN, axis=1) * WIN + own_inside
    return jnp.concatenate([own, far.reshape(OWNERS, NEIGH * CAP)], axis=1).astype(jnp.int32)


def set_ends(result, rng, smallest, largest):
    shape = result.shape
    place = [jax.random.randint(jax.random.fold_in(rng, axis), (), 0, shape[axis]) for axis in range(len(shape))]
    result = result.at[tuple(place)].set(smallest)
    longest = shape.index(max(shape))
    place[longest] = (place[longest] + 1) % shape[longest]
    return result.at[tuple(place)].set(largest)


def level_of(rng, shape, shards, low, largest):
    level = 1.0
    for dim, blocks in shards:
        draws = jax.random.uniform(jax.random.fold_in(jax.random.fold_in(rng, 6), dim), (blocks,), jnp.float32, low / len(shards), largest / len(shards))
        level = level * jnp.repeat(jnp.exp(draws), shape[dim] // blocks).reshape((-1,) + (1,) * (len(shape) - 1 - dim))
    return level


def gaussian(own_key, extent, spread, reach, cuts=(), kind=jnp.bfloat16):
    factor_of = level_of(own_key, extent, cuts, -0.22, 0.18) if cuts else 1.0
    drawn = jax.random.normal(own_key, extent, jnp.float32) * spread * factor_of
    return jnp.minimum(jnp.maximum(drawn, -reach), reach).astype(kind)


def setup_inputs(seed: int = 0) -> dict:
    arg_keys = jax.random.split(jax.random.key(seed), 8)
    return {
        "features": gaussian(arg_keys[0], (FINE, C_IN), 1.0, 6.0, ((0, 128),)),
        "block_offset": set_ends(jax.random.randint(arg_keys[1], (FINE // BLK,), 0, KERNEL), jax.random.fold_in(arg_keys[1], 1), 0, KERNEL - 1).astype(jnp.int32),
        "parent_entry": draw_parent_entry(jax.random.fold_in(arg_keys[7], 71), 0),
        "owner_cell": draw_owner_cell(jax.random.fold_in(arg_keys[7], 71), 0),
        "w_down": gaussian(arg_keys[4], (KERNEL, C_IN, C_OUT), (8 * C_IN) ** -0.5, 0.25),
        "b_down": gaussian(arg_keys[5], (C_OUT,), 0.5, 3.0, (), jnp.float32),
        "w_up": gaussian(arg_keys[6], (KERNEL, C_OUT, C_IN), C_OUT ** -0.5, 0.5),
    }


step_table = ((-1, -1), (-1, 0), (-1, 1), (0, -1), (0, 1), (1, -1), (1, 0), (1, 1))


def entry_targets(owner_cell, source):
    spare_index = OWNERS * C_DEV
    steps = jnp.array(step_table, dtype=jnp.int32)
    row_pos = source // N_INNER
    col_pos = source % N_INNER
    owners = ((row_pos + steps[:, 0]) % N_OUTER) * N_INNER + (col_pos + steps[:, 1]) % N_INNER
    own_cells = source * C_DEV + owner_cell[source, :SELF_CAP]
    regions = owner_cell[:, SELF_CAP:].reshape(OWNERS, NEIGH, CAP)
    cells = regions[owners, jnp.arange(NEIGH, dtype=jnp.int32)]
    far = jnp.where(cells < C_DEV, owners[:, None] * C_DEV + cells, spare_index)
    return jnp.concatenate([own_cells, far.reshape(NEIGH * CAP)]).astype(jnp.int32)


def reference(features, block_offset, parent_entry, owner_cell, w_down, b_down, w_up):
    spare_index = OWNERS * C_DEV
    fine_blocks = features.reshape(OWNERS, F_DEV // BLK, BLK, C_IN)
    offset_table = block_offset.reshape(OWNERS, F_DEV // BLK)
    parent_table = parent_entry.reshape(OWNERS, F_DEV)
    sources = jnp.arange(OWNERS, dtype=jnp.int32)

    def down_step(coarse_total, item):
        grouped, offset_ids, parent_ids, source = item
        weights = w_down[offset_ids].astype(jnp.float32)
        partial_value = jnp.einsum("bri,bio->bro", grouped.astype(jnp.float32), weights,
                             precision=lax.Precision.HIGHEST).reshape(F_DEV, C_OUT)
        entry_sum = jax.ops.segment_sum(partial_value, parent_ids, num_segments=ENTRIES).astype(jnp.bfloat16)
        target = entry_targets(owner_cell, source)
        coarse_total = coarse_total.at[target].add(entry_sum.astype(jnp.float32))
        return coarse_total, None

    start = jnp.zeros((spare_index + 1, C_OUT), jnp.float32)
    coarse_total, _ = lax.scan(down_step, start, (fine_blocks, offset_table, parent_table, sources))
    coarse = jnp.maximum(coarse_total[:spare_index] + b_down, 0.0).astype(jnp.bfloat16)
    padded = jnp.concatenate([coarse, jnp.zeros((1, C_OUT), jnp.bfloat16)], axis=0)

    def up_step(item):
        grouped, offset_ids, parent_ids, source = item
        target = entry_targets(owner_cell, source)
        parent_rows = padded[target[parent_ids]].astype(jnp.float32).reshape(F_DEV // BLK, BLK, C_OUT)
        lifted = jnp.einsum("bro,boi->bri", parent_rows, w_up[offset_ids].astype(jnp.float32),
                            precision=lax.Precision.HIGHEST)
        return (grouped.astype(jnp.float32) + lifted).astype(jnp.bfloat16).reshape(F_DEV, C_IN)

    refined = lax.map(up_step, (fine_blocks, offset_table, parent_table, sources))
    return refined.reshape(FINE, C_IN)
```

```python
import jax
import jax.numpy as jnp
from jax import lax
from jax.experimental import pallas as pl
from jax.experimental.pallas import tpu as pltpu
from jax.sharding import PartitionSpec as P

BLK = 128
C_DEV = 4096
SELF_CAP = 4096
WIN = 128
BRICKS_PER_STEP = 32

step_table = ((-1, -1), (-1, 0), (-1, 1), (0, -1), (0, 1), (1, -1), (1, 0), (1, 1))

NT = (((1,), (1,)), ((), ()))
TN = (((0,), (0,)), ((), ()))


def split_parts(data):
    high = data.astype(jnp.bfloat16)
    low = (data - high.astype(jnp.float32)).astype(jnp.bfloat16)
    return high, low


def one_hot_rows(index_row):
    span = lax.broadcasted_iota(jnp.int32, (WIN, index_row.shape[1]), 0)
    return (span == index_row).astype(jnp.bfloat16)


def down_kernel(win_ref, off_ref, xt_ref, e_ref, w_ref, *refs):
    n_groups = len(step_table)
    outs = refs[: 1 + n_groups]
    acc = refs[1 + n_groups]
    step = pl.program_id(0)
    per_step = e_ref.shape[0]

    @pl.when(step == 0)
    def _():
        acc[...] = jnp.zeros_like(acc)

    def body(j, carry):
        brick = step * per_step + j
        window = win_ref[brick]
        offset = off_ref[brick]
        inside = jnp.bitwise_and(e_ref[pl.ds(j, 1), :], WIN - 1)
        pick = one_hot_rows(inside)
        cols = pl.ds(pl.multiple_of(j * BLK, BLK), BLK)
        summed = lax.dot_general(pick, xt_ref[:, cols], NT, preferred_element_type=jnp.float32)
        high, low = split_parts(summed)
        weights = w_ref[offset]
        part = jnp.dot(high, weights, preferred_element_type=jnp.float32) + jnp.dot(
            low, weights, preferred_element_type=jnp.float32
        )
        rows = pl.ds(pl.multiple_of(window * WIN, WIN), WIN)
        acc[rows, :] += part
        return carry

    lax.fori_loop(0, per_step, body, 0)

    @pl.when(step == pl.num_programs(0) - 1)
    def _():
        outs[0][...] = acc[0:SELF_CAP, :].astype(jnp.bfloat16)
        cap = outs[1].shape[0]
        for g in range(n_groups):
            start = SELF_CAP + g * cap
            outs[1 + g][...] = acc[start : start + cap, :].astype(jnp.bfloat16)


def coarse_kernel(cw_ref, cells_ref, bias_ref, *refs):
    n_groups = len(step_table)
    sources = refs[: 1 + n_groups]
    outs = refs[1 + n_groups : 2 + 2 * n_groups]
    acc, coarse = refs[2 + 2 * n_groups :]
    cell_windows = acc.shape[0] // WIN
    acc[...] = jnp.zeros_like(acc)

    def pick_of(w):
        window = jnp.minimum(cw_ref[w], cell_windows - 1)
        cells = cells_ref[pl.ds(w, 1), :]
        inside = jnp.where(cells < C_DEV, cells - window * WIN, -1)
        rows = pl.ds(pl.multiple_of(window * WIN, WIN), WIN)
        return one_hot_rows(inside), rows

    base = 0
    for src in sources:
        count = src.shape[0] // WIN

        def gather_body(j, carry, src=src, base=base):
            pick, rows = pick_of(base + j)
            entries = src[pl.ds(pl.multiple_of(j * WIN, WIN), WIN), :]
            acc[rows, :] += jnp.dot(pick, entries, preferred_element_type=jnp.float32)
            return carry

        lax.fori_loop(0, count, gather_body, 0)
        base += count

    coarse[...] = jnp.maximum(acc[...] + bias_ref[...], 0.0).astype(jnp.bfloat16)

    base = 0
    for out in outs:
        count = out.shape[0] // WIN

        def scatter_body(j, carry, out=out, base=base):
            pick, rows = pick_of(base + j)
            chosen = lax.dot_general(pick, coarse[rows, :], TN, preferred_element_type=jnp.float32)
            out[pl.ds(pl.multiple_of(j * WIN, WIN), WIN), :] = chosen.astype(jnp.bfloat16)
            return carry

        lax.fori_loop(0, count, scatter_body, 0)
        base += count


def up_kernel(win_ref, off_ref, xt_ref, e_ref, wt_ref, *refs):
    n_groups = len(step_table)
    sources = refs[: 1 + n_groups]
    out_ref = refs[1 + n_groups]
    stack, sems = refs[2 + n_groups :]
    step = pl.program_id(0)
    per_step = e_ref.shape[0]

    @pl.when(step == 0)
    def _():
        copies = []
        start = 0
        for index, src in enumerate(sources):
            size = src.shape[0]
            copy = pltpu.make_async_copy(src, stack.at[pl.ds(start, size)], sems.at[index])
            copy.start()
            copies.append(copy)
            start += size
        for copy in copies:
            copy.wait()

    def body(j, carry):
        brick = step * per_step + j
        window = win_ref[brick]
        offset = off_ref[brick]
        inside = jnp.bitwise_and(e_ref[pl.ds(j, 1), :], WIN - 1)
        pick = one_hot_rows(inside)
        parents = stack[pl.ds(pl.multiple_of(window * WIN, WIN), WIN), :]
        lifted_t = lax.dot_general(wt_ref[offset], parents, NT, preferred_element_type=jnp.float32)
        high, low = split_parts(lifted_t)
        lifted = jnp.dot(high, pick, preferred_element_type=jnp.float32) + jnp.dot(
            low, pick, preferred_element_type=jnp.float32
        )
        cols = pl.ds(pl.multiple_of(j * BLK, BLK), BLK)
        out_ref[:, cols] = (xt_ref[:, cols].astype(jnp.float32) + lifted).astype(out_ref.dtype)
        return carry

    lax.fori_loop(0, per_step, body, 0)


def group_route(g, sign):
    n_outer = lax.axis_size("outer")
    n_inner = lax.axis_size("inner")
    a, b = step_table[g]
    route = []
    for s in range(n_outer * n_inner):
        row, col = divmod(s, n_inner)
        owner = ((row + a) % n_outer) * n_inner + (col + b) % n_inner
        route.append((s, owner) if sign > 0 else (owner, s))
    return route


def local(features, block_offset, parent_entry, owner_cell, w_down, b_down, w_up):
    n_groups = len(step_table)
    fine_rows, in_width = features.shape
    out_width = w_down.shape[2]
    entries = owner_cell.shape[1]
    cap = (entries - SELF_CAP) // n_groups
    blocks = fine_rows // BLK
    steps = blocks // BRICKS_PER_STEP

    xt = features.T
    entry_rows = parent_entry.reshape(blocks, BLK)
    brick_window = entry_rows[:, 0] // WIN
    cells = owner_cell.reshape(entries // WIN, WIN)
    cell_window = jnp.min(cells, axis=1) // WIN
    w_up_t = jnp.swapaxes(w_up, 1, 2)

    part_shapes = [jax.ShapeDtypeStruct((SELF_CAP, out_width), jnp.bfloat16)] + [
        jax.ShapeDtypeStruct((cap, out_width), jnp.bfloat16)
    ] * n_groups
    whole = lambda shape: pl.BlockSpec(shape, lambda *idx: (0,) * len(shape))

    down = pl.pallas_call(
        down_kernel,
        out_shape=part_shapes,
        grid_spec=pltpu.PrefetchScalarGridSpec(
            num_scalar_prefetch=2,
            grid=(steps,),
            in_specs=[
                pl.BlockSpec((in_width, BRICKS_PER_STEP * BLK), lambda i, *_: (0, i)),
                pl.BlockSpec((BRICKS_PER_STEP, BLK), lambda i, *_: (i, 0)),
                whole(w_down.shape),
            ],
            out_specs=[whole(s.shape) for s in part_shapes],
            scratch_shapes=[pltpu.VMEM((entries, out_width), jnp.float32)],
        ),
        compiler_params=pltpu.CompilerParams(dimension_semantics=("arbitrary",)),
        cost_estimate=pl.CostEstimate(
            flops=6 * fine_rows * in_width * out_width,
            transcendentals=0,
            bytes_accessed=fine_rows * (in_width * 2 + 4) + entries * out_width * 2,
        ),
    )
    parts = down(brick_window, block_offset, xt, entry_rows, w_down)

    arrived = [
        lax.ppermute(parts[1 + g], ("outer", "inner"), group_route(g, 1)) for g in range(n_groups)
    ]

    coarse = pl.pallas_call(
        coarse_kernel,
        out_shape=part_shapes,
        grid_spec=pltpu.PrefetchScalarGridSpec(
            num_scalar_prefetch=1,
            grid=(1,),
            in_specs=[whole(cells.shape), whole((1, out_width))]
            + [whole(s.shape) for s in part_shapes],
            out_specs=[whole(s.shape) for s in part_shapes],
            scratch_shapes=[
                pltpu.VMEM((C_DEV, out_width), jnp.float32),
                pltpu.VMEM((C_DEV, out_width), jnp.bfloat16),
            ],
        ),
        cost_estimate=pl.CostEstimate(
            flops=4 * entries * WIN * out_width,
            transcendentals=0,
            bytes_accessed=4 * entries * out_width,
        ),
    )
    answers = coarse(cell_window, cells, b_down.reshape(1, out_width), parts[0], *arrived)

    returned = [
        lax.ppermute(answers[1 + g], ("outer", "inner"), group_route(g, -1)) for g in range(n_groups)
    ]

    up = pl.pallas_call(
        up_kernel,
        out_shape=jax.ShapeDtypeStruct((in_width, fine_rows), features.dtype),
        grid_spec=pltpu.PrefetchScalarGridSpec(
            num_scalar_prefetch=2,
            grid=(steps,),
            in_specs=[
                pl.BlockSpec((in_width, BRICKS_PER_STEP * BLK), lambda i, *_: (0, i)),
                pl.BlockSpec((BRICKS_PER_STEP, BLK), lambda i, *_: (i, 0)),
                whole(w_up_t.shape),
            ]
            + [pl.BlockSpec(memory_space=pl.ANY)] * (1 + n_groups),
            out_specs=pl.BlockSpec((in_width, BRICKS_PER_STEP * BLK), lambda i, *_: (0, i)),
            scratch_shapes=[
                pltpu.VMEM((entries, out_width), jnp.bfloat16),
                pltpu.SemaphoreType.DMA((1 + n_groups,)),
            ],
        ),
        compiler_params=pltpu.CompilerParams(dimension_semantics=("arbitrary",)),
        cost_estimate=pl.CostEstimate(
            flops=6 * fine_rows * in_width * out_width,
            transcendentals=0,
            bytes_accessed=fine_rows * (in_width * 4 + 4) + entries * out_width * 2,
        ),
    )
    out_t = up(brick_window, block_offset, xt, entry_rows, w_up_t, answers[0], *returned)
    return out_t.T


def solution(mesh):
    in_specs = (
        P(("outer", "inner"), None),
        P(("outer", "inner")),
        P(("outer", "inner")),
        P(("outer", "inner"), None),
        P(),
        P(),
        P(),
    )
    out_specs = P(("outer", "inner"), None)
    return jax.shard_map(local, mesh=mesh, in_specs=in_specs, out_specs=out_specs, check_vma=False)
```

```python
import jax
import jax.numpy as jnp
from jax import lax
from jax.experimental import pallas as pl
from jax.experimental.pallas import tpu as pltpu
from jax.sharding import PartitionSpec as P

BLK = 128
C_DEV = 4096
SELF_CAP = 4096
WIN = 128
BRICKS_PER_STEP = 32
UNROLL = 8
WIN_UNROLL = 4

step_table = ((-1, -1), (-1, 0), (-1, 1), (0, -1), (0, 1), (1, -1), (1, 0), (1, 1))

NT = (((1,), (1,)), ((), ()))
TN = (((0,), (0,)), ((), ()))


def split_parts(data):
    high = data.astype(jnp.bfloat16)
    low = (data - high.astype(jnp.float32)).astype(jnp.bfloat16)
    return high, low


def one_hot_rows(index_row):
    span = lax.broadcasted_iota(jnp.int32, (WIN, index_row.shape[1]), 0)
    return (span == index_row).astype(jnp.bfloat16)


def down_kernel(win_ref, off_ref, xt_ref, e_ref, w_ref, *refs):
    n_groups = len(step_table)
    outs = refs[: 1 + n_groups]
    acc = refs[1 + n_groups]
    step = pl.program_id(0)
    per_step = e_ref.shape[0]

    @pl.when(step == 0)
    def _():
        acc[...] = jnp.zeros_like(acc)

    def body(u, carry):
        results = []
        for t in range(UNROLL):
            j = u * UNROLL + t
            brick = step * per_step + j
            window = win_ref[brick]
            offset = off_ref[brick]
            inside = jnp.bitwise_and(e_ref[pl.ds(j, 1), :], WIN - 1)
            pick = one_hot_rows(inside)
            cols = pl.ds(pl.multiple_of(j * BLK, BLK), BLK)
            summed = lax.dot_general(pick, xt_ref[:, cols], NT, preferred_element_type=jnp.float32)
            high, low = split_parts(summed)
            weights = w_ref[offset]
            part = jnp.dot(high, weights, preferred_element_type=jnp.float32) + jnp.dot(
                low, weights, preferred_element_type=jnp.float32
            )
            results.append((window, part))
        for window, part in results:
            rows = pl.ds(pl.multiple_of(window * WIN, WIN), WIN)
            acc[rows, :] += part
        return carry

    lax.fori_loop(0, per_step // UNROLL, body, 0)

    @pl.when(step == pl.num_programs(0) - 1)
    def _():
        outs[0][...] = acc[0:SELF_CAP, :].astype(jnp.bfloat16)
        cap = outs[1].shape[0]
        for g in range(n_groups):
            start = SELF_CAP + g * cap
            outs[1 + g][...] = acc[start : start + cap, :].astype(jnp.bfloat16)


def coarse_kernel(cw_ref, cells_ref, bias_ref, *refs):
    n_groups = len(step_table)
    sources = refs[: 1 + n_groups]
    outs = refs[1 + n_groups : 2 + 2 * n_groups]
    acc, coarse = refs[2 + 2 * n_groups :]
    cell_windows = acc.shape[0] // WIN
    acc[...] = jnp.zeros_like(acc)

    def pick_of(w):
        window = jnp.minimum(cw_ref[w], cell_windows - 1)
        cells = cells_ref[pl.ds(w, 1), :]
        inside = jnp.where(cells < C_DEV, cells - window * WIN, -1)
        rows = pl.ds(pl.multiple_of(window * WIN, WIN), WIN)
        return one_hot_rows(inside), rows

    base = 0
    for src in sources:
        count = src.shape[0] // WIN

        def gather_body(u, carry, src=src, base=base):
            results = []
            for t in range(WIN_UNROLL):
                j = u * WIN_UNROLL + t
                pick, rows = pick_of(base + j)
                entries = src[pl.ds(pl.multiple_of(j * WIN, WIN), WIN), :]
                results.append((rows, jnp.dot(pick, entries, preferred_element_type=jnp.float32)))
            for rows, value in results:
                acc[rows, :] += value
            return carry

        lax.fori_loop(0, count // WIN_UNROLL, gather_body, 0)
        base += count

    coarse[...] = jnp.maximum(acc[...] + bias_ref[...], 0.0).astype(jnp.bfloat16)

    base = 0
    for out in outs:
        count = out.shape[1] // WIN

        def scatter_body(u, carry, out=out, base=base):
            for t in range(WIN_UNROLL):
                j = u * WIN_UNROLL + t
                pick, rows = pick_of(base + j)
                chosen = lax.dot_general(coarse[rows, :], pick, TN, preferred_element_type=jnp.float32)
                out[:, pl.ds(pl.multiple_of(j * WIN, WIN), WIN)] = chosen.astype(jnp.bfloat16)
            return carry

        lax.fori_loop(0, count // WIN_UNROLL, scatter_body, 0)
        base += count


def up_kernel(win_ref, off_ref, xt_ref, e_ref, wt_ref, *refs):
    n_groups = len(step_table)
    sources = refs[: 1 + n_groups]
    out_ref = refs[1 + n_groups]
    stack, sems = refs[2 + n_groups :]
    step = pl.program_id(0)
    per_step = e_ref.shape[0]

    @pl.when(step == 0)
    def _():
        copies = []
        start = 0
        for index, src in enumerate(sources):
            size = src.shape[1]
            copy = pltpu.make_async_copy(src, stack.at[:, pl.ds(start, size)], sems.at[index])
            copy.start()
            copies.append(copy)
            start += size
        for copy in copies:
            copy.wait()

    def body(u, carry):
        for t in range(UNROLL):
            j = u * UNROLL + t
            brick = step * per_step + j
            window = win_ref[brick]
            offset = off_ref[brick]
            inside = jnp.bitwise_and(e_ref[pl.ds(j, 1), :], WIN - 1)
            pick = one_hot_rows(inside)
            parents = stack[:, pl.ds(pl.multiple_of(window * WIN, WIN), WIN)]
            rows_t = jnp.dot(parents, pick, preferred_element_type=jnp.float32).astype(jnp.bfloat16)
            lifted = jnp.dot(wt_ref[offset], rows_t, preferred_element_type=jnp.float32)
            cols = pl.ds(pl.multiple_of(j * BLK, BLK), BLK)
            out_ref[:, cols] = (xt_ref[:, cols].astype(jnp.float32) + lifted).astype(out_ref.dtype)
        return carry

    lax.fori_loop(0, per_step // UNROLL, body, 0)


def group_route(g, sign):
    n_outer = lax.axis_size("outer")
    n_inner = lax.axis_size("inner")
    a, b = step_table[g]
    route = []
    for s in range(n_outer * n_inner):
        row, col = divmod(s, n_inner)
        owner = ((row + a) % n_outer) * n_inner + (col + b) % n_inner
        route.append((s, owner) if sign > 0 else (owner, s))
    return route


def local(features, block_offset, parent_entry, owner_cell, w_down, b_down, w_up):
    n_groups = len(step_table)
    fine_rows, in_width = features.shape
    out_width = w_down.shape[2]
    entries = owner_cell.shape[1]
    cap = (entries - SELF_CAP) // n_groups
    blocks = fine_rows // BLK
    steps = blocks // BRICKS_PER_STEP

    xt = features.T
    entry_rows = parent_entry.reshape(blocks, BLK)
    brick_window = entry_rows[:, 0] // WIN
    cells = owner_cell.reshape(entries // WIN, WIN)
    cell_window = jnp.min(cells, axis=1) // WIN
    w_up_t = jnp.swapaxes(w_up, 1, 2)

    part_shapes = [jax.ShapeDtypeStruct((SELF_CAP, out_width), jnp.bfloat16)] + [
        jax.ShapeDtypeStruct((cap, out_width), jnp.bfloat16)
    ] * n_groups
    answer_shapes = [jax.ShapeDtypeStruct((s.shape[1], s.shape[0]), s.dtype) for s in part_shapes]
    whole = lambda shape: pl.BlockSpec(shape, lambda *idx: (0,) * len(shape))

    down = pl.pallas_call(
        down_kernel,
        out_shape=part_shapes,
        grid_spec=pltpu.PrefetchScalarGridSpec(
            num_scalar_prefetch=2,
            grid=(steps,),
            in_specs=[
                pl.BlockSpec((in_width, BRICKS_PER_STEP * BLK), lambda i, *_: (0, i)),
                pl.BlockSpec((BRICKS_PER_STEP, BLK), lambda i, *_: (i, 0)),
                whole(w_down.shape),
            ],
            out_specs=[whole(s.shape) for s in part_shapes],
            scratch_shapes=[pltpu.VMEM((entries, out_width), jnp.float32)],
        ),
        compiler_params=pltpu.CompilerParams(dimension_semantics=("arbitrary",)),
        cost_estimate=pl.CostEstimate(
            flops=6 * fine_rows * in_width * out_width,
            transcendentals=0,
            bytes_accessed=fine_rows * (in_width * 2 + 4) + entries * out_width * 2,
        ),
    )
    parts = down(brick_window, block_offset, xt, entry_rows, w_down)

    arrived = [
        lax.ppermute(parts[1 + g], ("outer", "inner"), group_route(g, 1)) for g in range(n_groups)
    ]

    coarse = pl.pallas_call(
        coarse_kernel,
        out_shape=answer_shapes,
        grid_spec=pltpu.PrefetchScalarGridSpec(
            num_scalar_prefetch=1,
            grid=(1,),
            in_specs=[whole(cells.shape), whole((1, out_width))]
            + [whole(s.shape) for s in part_shapes],
            out_specs=[whole(s.shape) for s in answer_shapes],
            scratch_shapes=[
                pltpu.VMEM((C_DEV, out_width), jnp.float32),
                pltpu.VMEM((C_DEV, out_width), jnp.bfloat16),
            ],
        ),
        cost_estimate=pl.CostEstimate(
            flops=4 * entries * WIN * out_width,
            transcendentals=0,
            bytes_accessed=4 * entries * out_width,
        ),
    )
    answers = coarse(cell_window, cells, b_down.reshape(1, out_width), parts[0], *arrived)

    returned = [
        lax.ppermute(answers[1 + g], ("outer", "inner"), group_route(g, -1)) for g in range(n_groups)
    ]

    up = pl.pallas_call(
        up_kernel,
        out_shape=jax.ShapeDtypeStruct((in_width, fine_rows), features.dtype),
        grid_spec=pltpu.PrefetchScalarGridSpec(
            num_scalar_prefetch=2,
            grid=(steps,),
            in_specs=[
                pl.BlockSpec((in_width, BRICKS_PER_STEP * BLK), lambda i, *_: (0, i)),
                pl.BlockSpec((BRICKS_PER_STEP, BLK), lambda i, *_: (i, 0)),
                whole(w_up_t.shape),
            ]
            + [pl.BlockSpec(memory_space=pl.ANY)] * (1 + n_groups),
            out_specs=pl.BlockSpec((in_width, BRICKS_PER_STEP * BLK), lambda i, *_: (0, i)),
            scratch_shapes=[
                pltpu.VMEM((out_width, entries), jnp.bfloat16),
                pltpu.SemaphoreType.DMA((1 + n_groups,)),
            ],
        ),
        compiler_params=pltpu.CompilerParams(dimension_semantics=("arbitrary",)),
        cost_estimate=pl.CostEstimate(
            flops=6 * fine_rows * in_width * out_width,
            transcendentals=0,
            bytes_accessed=fine_rows * (in_width * 4 + 4) + entries * out_width * 2,
        ),
    )
    out_t = up(brick_window, block_offset, xt, entry_rows, w_up_t, answers[0], *returned)
    return out_t.T


def solution(mesh):
    in_specs = (
        P(("outer", "inner"), None),
        P(("outer", "inner")),
        P(("outer", "inner")),
        P(("outer", "inner"), None),
        P(),
        P(),
        P(),
    )
    out_specs = P(("outer", "inner"), None)
    return jax.shard_map(local, mesh=mesh, in_specs=in_specs, out_specs=out_specs, check_vma=False)
```

```python
import functools

import jax
import jax.numpy as jnp
from jax import lax
from jax.experimental import pallas as pl
from jax.experimental.pallas import tpu as pltpu
from jax.sharding import PartitionSpec as P

BLK = 128
C_DEV = 4096
SELF_CAP = 4096
WIN = 128
BRICKS_PER_STEP = 32
UNROLL = 8
WIN_UNROLL = 4

step_table = ((-1, -1), (-1, 0), (-1, 1), (0, -1), (0, 1), (1, -1), (1, 0), (1, 1))

NT = (((1,), (1,)), ((), ()))
TN = (((0,), (0,)), ((), ()))


def split_parts(data):
    high = data.astype(jnp.bfloat16)
    low = (data - high.astype(jnp.float32)).astype(jnp.bfloat16)
    return high, low


def one_hot_rows(index_row):
    span = lax.broadcasted_iota(jnp.int32, (WIN, index_row.shape[1]), 0)
    return (span == index_row).astype(jnp.bfloat16)


def down_kernel(first_window, count_ref, order_ref, win_ref, off_ref, xt_ref, e_ref, w_ref, *refs):
    outs = refs[:-1]
    acc = refs[-1]
    bricks = e_ref.shape[0]
    trash = acc.shape[0] // WIN - 1
    acc[...] = jnp.zeros_like(acc)
    neighbours = count_ref[0]
    if first_window == 0:
        start, stop = neighbours, bricks
    else:
        start, stop = 0, neighbours

    def body(u, carry):
        results = []
        for t in range(UNROLL):
            position = start + u * UNROLL + t
            brick = order_ref[jnp.minimum(position, bricks - 1)]
            window = jnp.where(position < stop, win_ref[brick] - first_window, trash)
            offset = off_ref[brick]
            inside = jnp.bitwise_and(e_ref[pl.ds(brick, 1), :], WIN - 1)
            pick = one_hot_rows(inside)
            cols = pl.ds(pl.multiple_of(brick * BLK, BLK), BLK)
            summed = lax.dot_general(pick, xt_ref[:, cols], NT, preferred_element_type=jnp.float32)
            high, low = split_parts(summed)
            weights = w_ref[offset]
            part = jnp.dot(high, weights, preferred_element_type=jnp.float32) + jnp.dot(
                low, weights, preferred_element_type=jnp.float32
            )
            results.append((window, part))
        for window, part in results:
            rows = pl.ds(pl.multiple_of(window * WIN, WIN), WIN)
            acc[rows, :] += part
        return carry

    lax.fori_loop(0, (stop - start + UNROLL - 1) // UNROLL, body, 0)
    size = outs[0].shape[0]
    for g, out in enumerate(outs):
        out[...] = acc[g * size : (g + 1) * size, :].astype(out.dtype)


def coarse_kernel(cw_ref, cells_ref, bias_ref, *refs):
    n_groups = len(step_table)
    sources = refs[: 1 + n_groups]
    outs = refs[1 + n_groups : 2 + 2 * n_groups]
    acc, coarse = refs[2 + 2 * n_groups :]
    cell_windows = acc.shape[0] // WIN
    acc[...] = jnp.zeros_like(acc)

    def pick_of(w):
        window = jnp.minimum(cw_ref[w], cell_windows - 1)
        cells = cells_ref[pl.ds(w, 1), :]
        inside = jnp.where(cells < C_DEV, cells - window * WIN, -1)
        rows = pl.ds(pl.multiple_of(window * WIN, WIN), WIN)
        return one_hot_rows(inside), rows

    base = 0
    for src in sources:
        count = src.shape[0] // WIN

        def gather_body(u, carry, src=src, base=base):
            results = []
            for t in range(WIN_UNROLL):
                j = u * WIN_UNROLL + t
                pick, rows = pick_of(base + j)
                entries = src[pl.ds(pl.multiple_of(j * WIN, WIN), WIN), :]
                results.append((rows, jnp.dot(pick, entries, preferred_element_type=jnp.float32)))
            for rows, value in results:
                acc[rows, :] += value
            return carry

        lax.fori_loop(0, count // WIN_UNROLL, gather_body, 0)
        base += count

    coarse[...] = jnp.maximum(acc[...] + bias_ref[...], 0.0).astype(jnp.bfloat16)

    base = 0
    for out in outs:
        count = out.shape[1] // WIN

        def scatter_body(u, carry, out=out, base=base):
            for t in range(WIN_UNROLL):
                j = u * WIN_UNROLL + t
                pick, rows = pick_of(base + j)
                chosen = lax.dot_general(coarse[rows, :], pick, TN, preferred_element_type=jnp.float32)
                out[:, pl.ds(pl.multiple_of(j * WIN, WIN), WIN)] = chosen.astype(jnp.bfloat16)
            return carry

        lax.fori_loop(0, count // WIN_UNROLL, scatter_body, 0)
        base += count


def up_kernel(win_ref, off_ref, xt_ref, e_ref, wt_ref, *refs):
    n_groups = len(step_table)
    sources = refs[: 1 + n_groups]
    out_ref = refs[1 + n_groups]
    stack, sems = refs[2 + n_groups :]
    step = pl.program_id(0)
    per_step = e_ref.shape[0]

    @pl.when(step == 0)
    def _():
        copies = []
        start = 0
        for index, src in enumerate(sources):
            size = src.shape[1]
            copy = pltpu.make_async_copy(src, stack.at[:, pl.ds(start, size)], sems.at[index])
            copy.start()
            copies.append(copy)
            start += size
        for copy in copies:
            copy.wait()

    def body(u, carry):
        for t in range(UNROLL):
            j = u * UNROLL + t
            brick = step * per_step + j
            window = win_ref[brick]
            offset = off_ref[brick]
            inside = jnp.bitwise_and(e_ref[pl.ds(j, 1), :], WIN - 1)
            pick = one_hot_rows(inside)
            parents = stack[:, pl.ds(pl.multiple_of(window * WIN, WIN), WIN)]
            rows_t = jnp.dot(parents, pick, preferred_element_type=jnp.float32).astype(jnp.bfloat16)
            lifted = jnp.dot(wt_ref[offset], rows_t, preferred_element_type=jnp.float32)
            cols = pl.ds(pl.multiple_of(j * BLK, BLK), BLK)
            out_ref[:, cols] = (xt_ref[:, cols].astype(jnp.float32) + lifted).astype(out_ref.dtype)
        return carry

    lax.fori_loop(0, per_step // UNROLL, body, 0)


def group_route(g, sign):
    n_outer = lax.axis_size("outer")
    n_inner = lax.axis_size("inner")
    a, b = step_table[g]
    route = []
    for s in range(n_outer * n_inner):
        row, col = divmod(s, n_inner)
        owner = ((row + a) % n_outer) * n_inner + (col + b) % n_inner
        route.append((s, owner) if sign > 0 else (owner, s))
    return route


def local(features, block_offset, parent_entry, owner_cell, w_down, b_down, w_up):
    n_groups = len(step_table)
    fine_rows, in_width = features.shape
    out_width = w_down.shape[2]
    entries = owner_cell.shape[1]
    cap = (entries - SELF_CAP) // n_groups
    blocks = fine_rows // BLK
    steps = blocks // BRICKS_PER_STEP

    xt = features.T
    entry_rows = parent_entry.reshape(blocks, BLK)
    brick_window = entry_rows[:, 0] // WIN
    cells = owner_cell.reshape(entries // WIN, WIN)
    cell_window = jnp.min(cells, axis=1) // WIN
    w_up_t = jnp.swapaxes(w_up, 1, 2)

    part_shapes = [jax.ShapeDtypeStruct((SELF_CAP, out_width), jnp.bfloat16)] + [
        jax.ShapeDtypeStruct((cap, out_width), jnp.bfloat16)
    ] * n_groups
    answer_shapes = [jax.ShapeDtypeStruct((s.shape[1], s.shape[0]), s.dtype) for s in part_shapes]
    whole = lambda shape: pl.BlockSpec(shape, lambda *idx: (0,) * len(shape))

    is_far = (brick_window >= SELF_CAP // WIN).astype(jnp.int32)
    far_count = jnp.sum(is_far)
    far_rank = jnp.cumsum(is_far) - is_far
    own_rank = jnp.cumsum(1 - is_far) - (1 - is_far)
    position = jnp.where(is_far == 1, far_rank, far_count + own_rank)
    brick_ids = jnp.arange(blocks, dtype=jnp.int32)
    order = jnp.sum(
        jnp.where(position[None, :] == brick_ids[:, None], brick_ids[None, :], 0), axis=1
    ).astype(jnp.int32)
    counts = far_count.reshape(1).astype(jnp.int32)

    def down_call(first_window, shapes):
        rows = sum(s.shape[0] for s in shapes)
        return pl.pallas_call(
            functools.partial(down_kernel, first_window),
            out_shape=shapes,
            grid_spec=pltpu.PrefetchScalarGridSpec(
                num_scalar_prefetch=4,
                grid=(1,),
                in_specs=[whole(xt.shape), whole(entry_rows.shape), whole(w_down.shape)],
                out_specs=[whole(s.shape) for s in shapes],
                scratch_shapes=[pltpu.VMEM((rows + WIN, out_width), jnp.float32)],
            ),
            compiler_params=pltpu.CompilerParams(vmem_limit_bytes=48 * 1024 * 1024),
            cost_estimate=pl.CostEstimate(
                flops=3 * fine_rows * in_width * out_width,
                transcendentals=0,
                bytes_accessed=fine_rows * (in_width * 2 + 4) + rows * out_width * 2,
            ),
        )(counts, order, brick_window, block_offset, xt, entry_rows, w_down)

    parts = [None] + list(down_call(SELF_CAP // WIN, part_shapes[1:]))
    parts[0] = down_call(0, part_shapes[:1])[0]

    arrived = [
        lax.ppermute(parts[1 + g], ("outer", "inner"), group_route(g, 1)) for g in range(n_groups)
    ]

    coarse = pl.pallas_call(
        coarse_kernel,
        out_shape=answer_shapes,
        grid_spec=pltpu.PrefetchScalarGridSpec(
            num_scalar_prefetch=1,
            grid=(1,),
            in_specs=[whole(cells.shape), whole((1, out_width))]
            + [whole(s.shape) for s in part_shapes],
            out_specs=[whole(s.shape) for s in answer_shapes],
            scratch_shapes=[
                pltpu.VMEM((C_DEV, out_width), jnp.float32),
                pltpu.VMEM((C_DEV, out_width), jnp.bfloat16),
            ],
        ),
        cost_estimate=pl.CostEstimate(
            flops=4 * entries * WIN * out_width,
            transcendentals=0,
            bytes_accessed=4 * entries * out_width,
        ),
    )
    answers = coarse(cell_window, cells, b_down.reshape(1, out_width), parts[0], *arrived)

    returned = [
        lax.ppermute(answers[1 + g], ("outer", "inner"), group_route(g, -1)) for g in range(n_groups)
    ]

    up = pl.pallas_call(
        up_kernel,
        out_shape=jax.ShapeDtypeStruct((in_width, fine_rows), features.dtype),
        grid_spec=pltpu.PrefetchScalarGridSpec(
            num_scalar_prefetch=2,
            grid=(steps,),
            in_specs=[
                pl.BlockSpec((in_width, BRICKS_PER_STEP * BLK), lambda i, *_: (0, i)),
                pl.BlockSpec((BRICKS_PER_STEP, BLK), lambda i, *_: (i, 0)),
                whole(w_up_t.shape),
            ]
            + [pl.BlockSpec(memory_space=pl.ANY)] * (1 + n_groups),
            out_specs=pl.BlockSpec((in_width, BRICKS_PER_STEP * BLK), lambda i, *_: (0, i)),
            scratch_shapes=[
                pltpu.VMEM((out_width, entries), jnp.bfloat16),
                pltpu.SemaphoreType.DMA((1 + n_groups,)),
            ],
        ),
        compiler_params=pltpu.CompilerParams(dimension_semantics=("arbitrary",)),
        cost_estimate=pl.CostEstimate(
            flops=6 * fine_rows * in_width * out_width,
            transcendentals=0,
            bytes_accessed=fine_rows * (in_width * 4 + 4) + entries * out_width * 2,
        ),
    )
    out_t = up(brick_window, block_offset, xt, entry_rows, w_up_t, answers[0], *returned)
    return out_t.T


def solution(mesh):
    in_specs = (
        P(("outer", "inner"), None),
        P(("outer", "inner")),
        P(("outer", "inner")),
        P(("outer", "inner"), None),
        P(),
        P(),
        P(),
    )
    out_specs = P(("outer", "inner"), None)
    return jax.shard_map(local, mesh=mesh, in_specs=in_specs, out_specs=out_specs, check_vma=False)
```

```python
import functools

import jax
import jax.numpy as jnp
from jax import lax
from jax.experimental import pallas as pl
from jax.experimental.pallas import tpu as pltpu
from jax.sharding import PartitionSpec as P

BLK = 128
C_DEV = 4096
SELF_CAP = 4096
WIN = 128
BRICKS_PER_STEP = 32
UNROLL = 8
WIN_UNROLL = 4

step_table = ((-1, -1), (-1, 0), (-1, 1), (0, -1), (0, 1), (1, -1), (1, 0), (1, 1))

NT = (((1,), (1,)), ((), ()))
TN = (((0,), (0,)), ((), ()))


def split_parts(data):
    high = data.astype(jnp.bfloat16)
    low = (data - high.astype(jnp.float32)).astype(jnp.bfloat16)
    return high, low


def one_hot_rows(index_row):
    span = lax.broadcasted_iota(jnp.int32, (WIN, index_row.shape[1]), 0)
    return (span == index_row).astype(jnp.bfloat16)


def down_kernel(first_window, count_ref, order_ref, win_ref, off_ref, xt_ref, e_ref, w_ref, *refs):
    outs = refs[:-1]
    acc = refs[-1]
    step = pl.program_id(0)
    per_step = e_ref.shape[0]
    trash = acc.shape[0] // WIN - 1

    @pl.when(step == 0)
    def _():
        acc[...] = jnp.zeros_like(acc)

    neighbours = count_ref[step]
    if first_window == 0:
        start, stop = neighbours, per_step
    else:
        start, stop = 0, neighbours

    def body(u, carry):
        results = []
        for t in range(UNROLL):
            position = start + u * UNROLL + t
            j = order_ref[step * per_step + jnp.minimum(position, per_step - 1)]
            brick = step * per_step + j
            window = jnp.where(position < stop, win_ref[brick] - first_window, trash)
            offset = off_ref[brick]
            inside = jnp.bitwise_and(e_ref[pl.ds(j, 1), :], WIN - 1)
            pick = one_hot_rows(inside)
            cols = pl.ds(pl.multiple_of(j * BLK, BLK), BLK)
            summed = lax.dot_general(pick, xt_ref[:, cols], NT, preferred_element_type=jnp.float32)
            part = jnp.dot(summed.astype(jnp.bfloat16), w_ref[offset], preferred_element_type=jnp.float32)
            results.append((window, part))
        for window, part in results:
            rows = pl.ds(pl.multiple_of(window * WIN, WIN), WIN)
            acc[rows, :] += part
        return carry

    lax.fori_loop(0, (stop - start + UNROLL - 1) // UNROLL, body, 0)

    @pl.when(step == pl.num_programs(0) - 1)
    def _():
        size = outs[0].shape[0]
        for g, out in enumerate(outs):
            out[...] = acc[g * size : (g + 1) * size, :].astype(out.dtype)


def coarse_kernel(cw_ref, cells_ref, bias_ref, *refs):
    n_groups = len(step_table)
    sources = refs[: 1 + n_groups]
    outs = refs[1 + n_groups : 2 + 2 * n_groups]
    acc, coarse = refs[2 + 2 * n_groups :]
    cell_windows = acc.shape[0] // WIN
    acc[...] = jnp.zeros_like(acc)

    def pick_of(w):
        window = jnp.minimum(cw_ref[w], cell_windows - 1)
        cells = cells_ref[pl.ds(w, 1), :]
        inside = jnp.where(cells < C_DEV, cells - window * WIN, -1)
        rows = pl.ds(pl.multiple_of(window * WIN, WIN), WIN)
        return one_hot_rows(inside), rows

    base = 0
    for src in sources:
        count = src.shape[0] // WIN

        def gather_body(u, carry, src=src, base=base):
            results = []
            for t in range(WIN_UNROLL):
                j = u * WIN_UNROLL + t
                pick, rows = pick_of(base + j)
                entries = src[pl.ds(pl.multiple_of(j * WIN, WIN), WIN), :]
                results.append((rows, jnp.dot(pick, entries, preferred_element_type=jnp.float32)))
            for rows, value in results:
                acc[rows, :] += value
            return carry

        lax.fori_loop(0, count // WIN_UNROLL, gather_body, 0)
        base += count

    coarse[...] = jnp.maximum(acc[...] + bias_ref[...], 0.0).astype(jnp.bfloat16)

    base = 0
    for out in outs:
        count = out.shape[1] // WIN

        def scatter_body(u, carry, out=out, base=base):
            for t in range(WIN_UNROLL):
                j = u * WIN_UNROLL + t
                pick, rows = pick_of(base + j)
                chosen = lax.dot_general(coarse[rows, :], pick, TN, preferred_element_type=jnp.float32)
                out[:, pl.ds(pl.multiple_of(j * WIN, WIN), WIN)] = chosen.astype(jnp.bfloat16)
            return carry

        lax.fori_loop(0, count // WIN_UNROLL, scatter_body, 0)
        base += count


def up_kernel(win_ref, off_ref, xt_ref, e_ref, wt_ref, *refs):
    n_groups = len(step_table)
    sources = refs[: 1 + n_groups]
    out_ref = refs[1 + n_groups]
    stack, sems = refs[2 + n_groups :]
    step = pl.program_id(0)
    per_step = e_ref.shape[0]

    @pl.when(step == 0)
    def _():
        copies = []
        start = 0
        for index, src in enumerate(sources):
            size = src.shape[1]
            copy = pltpu.make_async_copy(src, stack.at[:, pl.ds(start, size)], sems.at[index])
            copy.start()
            copies.append(copy)
            start += size
        for copy in copies:
            copy.wait()

    def body(u, carry):
        for t in range(UNROLL):
            j = u * UNROLL + t
            brick = step * per_step + j
            window = win_ref[brick]
            offset = off_ref[brick]
            inside = jnp.bitwise_and(e_ref[pl.ds(j, 1), :], WIN - 1)
            pick = one_hot_rows(inside)
            parents = stack[:, pl.ds(pl.multiple_of(window * WIN, WIN), WIN)]
            rows_t = jnp.dot(parents, pick, preferred_element_type=jnp.float32).astype(jnp.bfloat16)
            lifted = jnp.dot(wt_ref[offset], rows_t, preferred_element_type=jnp.float32)
            cols = pl.ds(pl.multiple_of(j * BLK, BLK), BLK)
            out_ref[:, cols] = (xt_ref[:, cols].astype(jnp.float32) + lifted).astype(out_ref.dtype)
        return carry

    lax.fori_loop(0, per_step // UNROLL, body, 0)


def group_route(g, sign):
    n_outer = lax.axis_size("outer")
    n_inner = lax.axis_size("inner")
    a, b = step_table[g]
    route = []
    for s in range(n_outer * n_inner):
        row, col = divmod(s, n_inner)
        owner = ((row + a) % n_outer) * n_inner + (col + b) % n_inner
        route.append((s, owner) if sign > 0 else (owner, s))
    return route


def local(features, block_offset, parent_entry, owner_cell, w_down, b_down, w_up):
    n_groups = len(step_table)
    fine_rows, in_width = features.shape
    out_width = w_down.shape[2]
    entries = owner_cell.shape[1]
    cap = (entries - SELF_CAP) // n_groups
    blocks = fine_rows // BLK
    steps = blocks // BRICKS_PER_STEP

    xt = features.T
    entry_rows = parent_entry.reshape(blocks, BLK)
    brick_window = entry_rows[:, 0] // WIN
    cells = owner_cell.reshape(entries // WIN, WIN)
    cell_window = jnp.min(cells, axis=1) // WIN
    w_up_t = jnp.swapaxes(w_up, 1, 2)

    part_shapes = [jax.ShapeDtypeStruct((SELF_CAP, out_width), jnp.bfloat16)] + [
        jax.ShapeDtypeStruct((cap, out_width), jnp.bfloat16)
    ] * n_groups
    answer_shapes = [jax.ShapeDtypeStruct((s.shape[1], s.shape[0]), s.dtype) for s in part_shapes]
    whole = lambda shape: pl.BlockSpec(shape, lambda *idx: (0,) * len(shape))

    is_far = (brick_window >= SELF_CAP // WIN).astype(jnp.int32).reshape(steps, BRICKS_PER_STEP)
    far_count = jnp.sum(is_far, axis=1)
    far_rank = jnp.cumsum(is_far, axis=1) - is_far
    own_rank = jnp.cumsum(1 - is_far, axis=1) - (1 - is_far)
    position = jnp.where(is_far == 1, far_rank, far_count[:, None] + own_rank)
    local_ids = jnp.arange(BRICKS_PER_STEP, dtype=jnp.int32)
    order = jnp.sum(
        jnp.where(position[:, None, :] == local_ids[None, :, None], local_ids[None, None, :], 0), axis=2
    )
    order = order.reshape(blocks).astype(jnp.int32)
    counts = far_count.astype(jnp.int32)

    def down_call(first_window, shapes):
        rows = sum(s.shape[0] for s in shapes)
        return pl.pallas_call(
            functools.partial(down_kernel, first_window),
            out_shape=shapes,
            grid_spec=pltpu.PrefetchScalarGridSpec(
                num_scalar_prefetch=4,
                grid=(steps,),
                in_specs=[
                    pl.BlockSpec((in_width, BRICKS_PER_STEP * BLK), lambda i, *_: (0, i)),
                    pl.BlockSpec((BRICKS_PER_STEP, BLK), lambda i, *_: (i, 0)),
                    whole(w_down.shape),
                ],
                out_specs=[whole(s.shape) for s in shapes],
                scratch_shapes=[pltpu.VMEM((rows + WIN, out_width), jnp.float32)],
            ),
            compiler_params=pltpu.CompilerParams(dimension_semantics=("arbitrary",)),
            cost_estimate=pl.CostEstimate(
                flops=2 * fine_rows * in_width * out_width,
                transcendentals=0,
                bytes_accessed=fine_rows * (in_width * 2 + 4) + rows * out_width * 2,
            ),
        )(counts, order, brick_window, block_offset, xt, entry_rows, w_down)

    parts = [None] + list(down_call(SELF_CAP // WIN, part_shapes[1:]))
    parts[0] = down_call(0, part_shapes[:1])[0]

    arrived = [
        lax.ppermute(parts[1 + g], ("outer", "inner"), group_route(g, 1)) for g in range(n_groups)
    ]

    coarse = pl.pallas_call(
        coarse_kernel,
        out_shape=answer_shapes,
        grid_spec=pltpu.PrefetchScalarGridSpec(
            num_scalar_prefetch=1,
            grid=(1,),
            in_specs=[whole(cells.shape), whole((1, out_width))]
            + [whole(s.shape) for s in part_shapes],
            out_specs=[whole(s.shape) for s in answer_shapes],
            scratch_shapes=[
                pltpu.VMEM((C_DEV, out_width), jnp.float32),
                pltpu.VMEM((C_DEV, out_width), jnp.bfloat16),
            ],
        ),
        cost_estimate=pl.CostEstimate(
            flops=4 * entries * WIN * out_width,
            transcendentals=0,
            bytes_accessed=4 * entries * out_width,
        ),
    )
    answers = coarse(cell_window, cells, b_down.reshape(1, out_width), parts[0], *arrived)

    returned = [
        lax.ppermute(answers[1 + g], ("outer", "inner"), group_route(g, -1)) for g in range(n_groups)
    ]

    up = pl.pallas_call(
        up_kernel,
        out_shape=jax.ShapeDtypeStruct((in_width, fine_rows), features.dtype),
        grid_spec=pltpu.PrefetchScalarGridSpec(
            num_scalar_prefetch=2,
            grid=(steps,),
            in_specs=[
                pl.BlockSpec((in_width, BRICKS_PER_STEP * BLK), lambda i, *_: (0, i)),
                pl.BlockSpec((BRICKS_PER_STEP, BLK), lambda i, *_: (i, 0)),
                whole(w_up_t.shape),
            ]
            + [pl.BlockSpec(memory_space=pl.ANY)] * (1 + n_groups),
            out_specs=pl.BlockSpec((in_width, BRICKS_PER_STEP * BLK), lambda i, *_: (0, i)),
            scratch_shapes=[
                pltpu.VMEM((out_width, entries), jnp.bfloat16),
                pltpu.SemaphoreType.DMA((1 + n_groups,)),
            ],
        ),
        compiler_params=pltpu.CompilerParams(dimension_semantics=("arbitrary",)),
        cost_estimate=pl.CostEstimate(
            flops=6 * fine_rows * in_width * out_width,
            transcendentals=0,
            bytes_accessed=fine_rows * (in_width * 4 + 4) + entries * out_width * 2,
        ),
    )
    out_t = up(brick_window, block_offset, xt, entry_rows, w_up_t, answers[0], *returned)
    return out_t.T


def solution(mesh):
    in_specs = (
        P(("outer", "inner"), None),
        P(("outer", "inner")),
        P(("outer", "inner")),
        P(("outer", "inner"), None),
        P(),
        P(),
        P(),
    )
    out_specs = P(("outer", "inner"), None)
    return jax.shard_map(local, mesh=mesh, in_specs=in_specs, out_specs=out_specs, check_vma=False)
```

```python
import functools

import jax
import jax.numpy as jnp
from jax import lax
from jax.experimental import pallas as pl
from jax.experimental.pallas import tpu as pltpu
from jax.sharding import PartitionSpec as P

BLK = 128
C_DEV = 4096
SELF_CAP = 4096
WIN = 128
BRICKS_PER_STEP = 32
UNROLL = 8
WIN_UNROLL = 4

step_table = ((-1, -1), (-1, 0), (-1, 1), (0, -1), (0, 1), (1, -1), (1, 0), (1, 1))

NT = (((1,), (1,)), ((), ()))
TN = (((0,), (0,)), ((), ()))


def split_parts(data):
    high = data.astype(jnp.bfloat16)
    low = (data - high.astype(jnp.float32)).astype(jnp.bfloat16)
    return high, low


def one_hot_rows(index_row):
    span = lax.broadcasted_iota(jnp.int32, (WIN, index_row.shape[1]), 0)
    return (span == index_row).astype(jnp.bfloat16)


def down_kernel(first_window, count_ref, order_ref, win_ref, off_ref, xt_ref, e_ref, w_ref, *refs):
    outs = refs[:-1]
    acc = refs[-1]
    step = pl.program_id(0)
    per_step = e_ref.shape[0]
    trash = acc.shape[0] // WIN - 1

    @pl.when(step == 0)
    def _():
        acc[...] = jnp.zeros_like(acc)

    neighbours = count_ref[step]
    if first_window == 0:
        start, stop = neighbours, per_step
    else:
        start, stop = 0, neighbours

    def body(u, carry):
        results = []
        for t in range(UNROLL):
            position = start + u * UNROLL + t
            j = order_ref[step * per_step + jnp.minimum(position, per_step - 1)]
            brick = step * per_step + j
            window = jnp.where(position < stop, win_ref[brick] - first_window, trash)
            offset = off_ref[brick]
            inside = jnp.bitwise_and(e_ref[pl.ds(j, 1), :], WIN - 1)
            pick = one_hot_rows(inside)
            cols = pl.ds(pl.multiple_of(j * BLK, BLK), BLK)
            summed = lax.dot_general(pick, xt_ref[:, cols], NT, preferred_element_type=jnp.float32)
            part = jnp.dot(summed.astype(jnp.bfloat16), w_ref[offset], preferred_element_type=jnp.float32)
            results.append((window, part))
        for window, part in results:
            rows = pl.ds(pl.multiple_of(window * WIN, WIN), WIN)
            acc[rows, :] += part
        return carry

    lax.fori_loop(0, (stop - start + UNROLL - 1) // UNROLL, body, 0)

    @pl.when(step == pl.num_programs(0) - 1)
    def _():
        size = outs[0].shape[0]
        for g, out in enumerate(outs):
            out[...] = acc[g * size : (g + 1) * size, :].astype(out.dtype)


def coarse_kernel(cw_ref, cells_ref, bias_ref, *refs):
    n_groups = len(step_table)
    sources = refs[: 1 + n_groups]
    outs = refs[1 + n_groups : 2 + 2 * n_groups]
    acc, coarse = refs[2 + 2 * n_groups :]
    cell_windows = acc.shape[0] // WIN
    acc[...] = jnp.zeros_like(acc)

    def pick_of(w):
        window = jnp.minimum(cw_ref[w], cell_windows - 1)
        cells = cells_ref[pl.ds(w, 1), :]
        inside = jnp.where(cells < C_DEV, cells - window * WIN, -1)
        rows = pl.ds(pl.multiple_of(window * WIN, WIN), WIN)
        return one_hot_rows(inside), rows

    base = 0
    for src in sources:
        count = src.shape[0] // WIN

        def gather_body(u, carry, src=src, base=base):
            results = []
            for t in range(WIN_UNROLL):
                j = u * WIN_UNROLL + t
                pick, rows = pick_of(base + j)
                entries = src[pl.ds(pl.multiple_of(j * WIN, WIN), WIN), :]
                results.append((rows, jnp.dot(pick, entries, preferred_element_type=jnp.float32)))
            for rows, value in results:
                acc[rows, :] += value
            return carry

        lax.fori_loop(0, count // WIN_UNROLL, gather_body, 0)
        base += count

    coarse[...] = jnp.maximum(acc[...] + bias_ref[...], 0.0).astype(jnp.bfloat16)

    base = 0
    for out in outs:
        count = out.shape[1] // WIN

        def scatter_body(u, carry, out=out, base=base):
            for t in range(WIN_UNROLL):
                j = u * WIN_UNROLL + t
                pick, rows = pick_of(base + j)
                chosen = lax.dot_general(coarse[rows, :], pick, TN, preferred_element_type=jnp.float32)
                out[:, pl.ds(pl.multiple_of(j * WIN, WIN), WIN)] = chosen.astype(jnp.bfloat16)
            return carry

        lax.fori_loop(0, count // WIN_UNROLL, scatter_body, 0)
        base += count


def up_kernel(own_mode, count_ref, order_ref, win_ref, off_ref, xt_ref, e_ref, wt_ref, *refs):
    step = pl.program_id(0)
    per_step = e_ref.shape[0]
    neighbours = count_ref[step]
    if own_mode:
        parents_ref, out_ref = refs
        first_window = 0
        start, stop = neighbours, per_step
    else:
        n_groups = len(step_table)
        sources = refs[:n_groups]
        out_ref = refs[n_groups + 1]
        parents_ref, stage, sems = refs[n_groups + 2 :]
        first_window = SELF_CAP // WIN
        start, stop = 0, neighbours

        @pl.when(step == 0)
        def _():
            copies = []
            offset = 0
            for index, src in enumerate(sources):
                size = src.shape[1]
                copy = pltpu.make_async_copy(src, parents_ref.at[:, pl.ds(offset, size)], sems.at[index])
                copy.start()
                copies.append(copy)
                offset += size
            for copy in copies:
                copy.wait()

    def brick_of(position):
        j = order_ref[step * per_step + jnp.minimum(position, per_step - 1)]
        return j, step * per_step + j

    def write_copy(j, brick):
        cols = pl.ds(pl.multiple_of(j * BLK, BLK), BLK)
        dest = pl.ds(pl.multiple_of(brick * BLK, BLK), BLK)
        return pltpu.make_async_copy(stage.at[:, cols], out_ref.at[:, dest], sems.at[len(step_table) + j])

    def body(u, carry):
        for t in range(UNROLL):
            position = start + u * UNROLL + t
            j, brick = brick_of(position)
            valid = position < stop
            window = win_ref[brick] - first_window if own_mode else jnp.where(valid, win_ref[brick] - first_window, 0)
            offset = off_ref[brick]
            inside = jnp.bitwise_and(e_ref[pl.ds(j, 1), :], WIN - 1)
            pick = one_hot_rows(inside)
            parents = parents_ref[:, pl.ds(pl.multiple_of(window * WIN, WIN), WIN)]
            rows_t = jnp.dot(parents, pick, preferred_element_type=jnp.float32).astype(jnp.bfloat16)
            lifted = jnp.dot(wt_ref[offset], rows_t, preferred_element_type=jnp.float32)
            cols = pl.ds(pl.multiple_of(j * BLK, BLK), BLK)
            result = (xt_ref[:, cols].astype(jnp.float32) + lifted).astype(out_ref.dtype)
            if own_mode:
                out_ref[:, cols] = result
            else:

                @pl.when(valid)
                def _():
                    stage[:, cols] = result
                    write_copy(j, brick).start()

        return carry

    lax.fori_loop(0, (stop - start + UNROLL - 1) // UNROLL, body, 0)

    if not own_mode:

        def drain(position, carry):
            j, brick = brick_of(position)
            write_copy(j, brick).wait()
            return carry

        lax.fori_loop(start, stop, drain, 0)


def group_route(g, sign):
    n_outer = lax.axis_size("outer")
    n_inner = lax.axis_size("inner")
    a, b = step_table[g]
    route = []
    for s in range(n_outer * n_inner):
        row, col = divmod(s, n_inner)
        owner = ((row + a) % n_outer) * n_inner + (col + b) % n_inner
        route.append((s, owner) if sign > 0 else (owner, s))
    return route


def local(features, block_offset, parent_entry, owner_cell, w_down, b_down, w_up):
    n_groups = len(step_table)
    fine_rows, in_width = features.shape
    out_width = w_down.shape[2]
    entries = owner_cell.shape[1]
    cap = (entries - SELF_CAP) // n_groups
    blocks = fine_rows // BLK
    steps = blocks // BRICKS_PER_STEP

    xt = features.T
    entry_rows = parent_entry.reshape(blocks, BLK)
    brick_window = entry_rows[:, 0] // WIN
    cells = owner_cell.reshape(entries // WIN, WIN)
    cell_window = jnp.min(cells, axis=1) // WIN
    w_up_t = jnp.swapaxes(w_up, 1, 2)

    part_shapes = [jax.ShapeDtypeStruct((SELF_CAP, out_width), jnp.bfloat16)] + [
        jax.ShapeDtypeStruct((cap, out_width), jnp.bfloat16)
    ] * n_groups
    answer_shapes = [jax.ShapeDtypeStruct((s.shape[1], s.shape[0]), s.dtype) for s in part_shapes]
    whole = lambda shape: pl.BlockSpec(shape, lambda *idx: (0,) * len(shape))

    is_far = (brick_window >= SELF_CAP // WIN).astype(jnp.int32).reshape(steps, BRICKS_PER_STEP)
    far_count = jnp.sum(is_far, axis=1)
    far_rank = jnp.cumsum(is_far, axis=1) - is_far
    own_rank = jnp.cumsum(1 - is_far, axis=1) - (1 - is_far)
    position = jnp.where(is_far == 1, far_rank, far_count[:, None] + own_rank)
    local_ids = jnp.arange(BRICKS_PER_STEP, dtype=jnp.int32)
    order = jnp.sum(
        jnp.where(position[:, None, :] == local_ids[None, :, None], local_ids[None, None, :], 0), axis=2
    )
    order = order.reshape(blocks).astype(jnp.int32)
    counts = far_count.astype(jnp.int32)

    def down_call(first_window, shapes):
        rows = sum(s.shape[0] for s in shapes)
        return pl.pallas_call(
            functools.partial(down_kernel, first_window),
            out_shape=shapes,
            grid_spec=pltpu.PrefetchScalarGridSpec(
                num_scalar_prefetch=4,
                grid=(steps,),
                in_specs=[
                    pl.BlockSpec((in_width, BRICKS_PER_STEP * BLK), lambda i, *_: (0, i)),
                    pl.BlockSpec((BRICKS_PER_STEP, BLK), lambda i, *_: (i, 0)),
                    whole(w_down.shape),
                ],
                out_specs=[whole(s.shape) for s in shapes],
                scratch_shapes=[pltpu.VMEM((rows + WIN, out_width), jnp.float32)],
            ),
            compiler_params=pltpu.CompilerParams(dimension_semantics=("arbitrary",)),
            cost_estimate=pl.CostEstimate(
                flops=2 * fine_rows * in_width * out_width,
                transcendentals=0,
                bytes_accessed=fine_rows * (in_width * 2 + 4) + rows * out_width * 2,
            ),
        )(counts, order, brick_window, block_offset, xt, entry_rows, w_down)

    parts = [None] + list(down_call(SELF_CAP // WIN, part_shapes[1:]))
    parts[0] = down_call(0, part_shapes[:1])[0]

    arrived = [
        lax.ppermute(parts[1 + g], ("outer", "inner"), group_route(g, 1)) for g in range(n_groups)
    ]

    coarse = pl.pallas_call(
        coarse_kernel,
        out_shape=answer_shapes,
        grid_spec=pltpu.PrefetchScalarGridSpec(
            num_scalar_prefetch=1,
            grid=(1,),
            in_specs=[whole(cells.shape), whole((1, out_width))]
            + [whole(s.shape) for s in part_shapes],
            out_specs=[whole(s.shape) for s in answer_shapes],
            scratch_shapes=[
                pltpu.VMEM((C_DEV, out_width), jnp.float32),
                pltpu.VMEM((C_DEV, out_width), jnp.bfloat16),
            ],
        ),
        cost_estimate=pl.CostEstimate(
            flops=4 * entries * WIN * out_width,
            transcendentals=0,
            bytes_accessed=4 * entries * out_width,
        ),
    )
    answers = coarse(cell_window, cells, b_down.reshape(1, out_width), parts[0], *arrived)

    returned = [
        lax.ppermute(answers[1 + g], ("outer", "inner"), group_route(g, -1)) for g in range(n_groups)
    ]

    chunk = pl.BlockSpec((in_width, BRICKS_PER_STEP * BLK), lambda i, *_: (0, i))
    rows_spec = pl.BlockSpec((BRICKS_PER_STEP, BLK), lambda i, *_: (i, 0))
    out_shape = jax.ShapeDtypeStruct((in_width, fine_rows), features.dtype)
    up_cost = pl.CostEstimate(
        flops=2 * fine_rows * in_width * out_width,
        transcendentals=0,
        bytes_accessed=fine_rows * (in_width * 2 + 2),
    )
    own_up = pl.pallas_call(
        functools.partial(up_kernel, True),
        out_shape=out_shape,
        grid_spec=pltpu.PrefetchScalarGridSpec(
            num_scalar_prefetch=4,
            grid=(steps,),
            in_specs=[chunk, rows_spec, whole(w_up_t.shape), whole(answer_shapes[0].shape)],
            out_specs=chunk,
        ),
        compiler_params=pltpu.CompilerParams(dimension_semantics=("arbitrary",)),
        cost_estimate=up_cost,
    )
    partial_out = own_up(counts, order, brick_window, block_offset, xt, entry_rows, w_up_t, answers[0])

    far_up = pl.pallas_call(
        functools.partial(up_kernel, False),
        out_shape=out_shape,
        grid_spec=pltpu.PrefetchScalarGridSpec(
            num_scalar_prefetch=4,
            grid=(steps,),
            in_specs=[chunk, rows_spec, whole(w_up_t.shape)]
            + [pl.BlockSpec(memory_space=pl.ANY)] * (n_groups + 1),
            out_specs=pl.BlockSpec(memory_space=pl.ANY),
            scratch_shapes=[
                pltpu.VMEM((out_width, entries - SELF_CAP), jnp.bfloat16),
                pltpu.VMEM((in_width, BRICKS_PER_STEP * BLK), features.dtype),
                pltpu.SemaphoreType.DMA((n_groups + BRICKS_PER_STEP,)),
            ],
        ),
        input_output_aliases={4 + 3 + n_groups: 0},
        compiler_params=pltpu.CompilerParams(dimension_semantics=("arbitrary",)),
        cost_estimate=up_cost,
    )
    out_t = far_up(counts, order, brick_window, block_offset, xt, entry_rows, w_up_t, *returned, partial_out)
    return out_t.T


def solution(mesh):
    in_specs = (
        P(("outer", "inner"), None),
        P(("outer", "inner")),
        P(("outer", "inner")),
        P(("outer", "inner"), None),
        P(),
        P(),
        P(),
    )
    out_specs = P(("outer", "inner"), None)
    return jax.shard_map(local, mesh=mesh, in_specs=in_specs, out_specs=out_specs, check_vma=False)
```

```python
import functools

import jax
import jax.numpy as jnp
from jax import lax
from jax.experimental import pallas as pl
from jax.experimental.pallas import tpu as pltpu
from jax.sharding import PartitionSpec as P

BLK = 128
C_DEV = 4096
SELF_CAP = 4096
WIN = 128
BRICKS_PER_STEP = 32
UNROLL = 8
WIN_UNROLL = 4

step_table = ((-1, -1), (-1, 0), (-1, 1), (0, -1), (0, 1), (1, -1), (1, 0), (1, 1))

NT = (((1,), (1,)), ((), ()))
TN = (((0,), (0,)), ((), ()))


def split_parts(data):
    high = data.astype(jnp.bfloat16)
    low = (data - high.astype(jnp.float32)).astype(jnp.bfloat16)
    return high, low


def one_hot_rows(index_row):
    span = lax.broadcasted_iota(jnp.int32, (WIN, index_row.shape[1]), 0)
    return (span == index_row).astype(jnp.bfloat16)


def down_kernel(first_window, count_ref, order_ref, win_ref, off_ref, xt_ref, e_ref, w_ref, *refs):
    outs = refs[:-1]
    acc = refs[-1]
    step = pl.program_id(0)
    per_step = e_ref.shape[0]
    trash = acc.shape[0] // WIN - 1

    @pl.when(step == 0)
    def _():
        acc[...] = jnp.zeros_like(acc)

    neighbours = count_ref[step]
    if first_window == 0:
        start, stop = neighbours, per_step
    else:
        start, stop = 0, neighbours

    def body(u, carry):
        results = []
        for t in range(UNROLL):
            position = start + u * UNROLL + t
            j = order_ref[step * per_step + jnp.minimum(position, per_step - 1)]
            brick = step * per_step + j
            window = jnp.where(position < stop, win_ref[brick] - first_window, trash)
            offset = off_ref[brick]
            inside = jnp.bitwise_and(e_ref[pl.ds(j, 1), :], WIN - 1)
            pick = one_hot_rows(inside)
            cols = pl.ds(pl.multiple_of(j * BLK, BLK), BLK)
            summed = lax.dot_general(pick, xt_ref[:, cols], NT, preferred_element_type=jnp.float32)
            part = jnp.dot(summed.astype(jnp.bfloat16), w_ref[offset], preferred_element_type=jnp.float32)
            results.append((window, part))
        for window, part in results:
            rows = pl.ds(pl.multiple_of(window * WIN, WIN), WIN)
            acc[rows, :] += part
        return carry

    lax.fori_loop(0, (stop - start + UNROLL - 1) // UNROLL, body, 0)

    @pl.when(step == pl.num_programs(0) - 1)
    def _():
        size = outs[0].shape[0]
        for g, out in enumerate(outs):
            out[...] = acc[g * size : (g + 1) * size, :].astype(out.dtype)


def coarse_kernel(cw_ref, cells_ref, bias_ref, *refs):
    n_groups = len(step_table)
    sources = refs[: 1 + n_groups]
    outs = refs[1 + n_groups : 2 + 2 * n_groups]
    acc, coarse = refs[2 + 2 * n_groups :]
    cell_windows = acc.shape[0] // WIN
    acc[...] = jnp.zeros_like(acc)

    def pick_of(w):
        window = jnp.minimum(cw_ref[w], cell_windows - 1)
        cells = cells_ref[pl.ds(w, 1), :]
        inside = jnp.where(cells < C_DEV, cells - window * WIN, -1)
        rows = pl.ds(pl.multiple_of(window * WIN, WIN), WIN)
        return one_hot_rows(inside), rows

    base = 0
    for src in sources:
        count = src.shape[0] // WIN

        def gather_body(u, carry, src=src, base=base):
            results = []
            for t in range(WIN_UNROLL):
                j = u * WIN_UNROLL + t
                pick, rows = pick_of(base + j)
                entries = src[pl.ds(pl.multiple_of(j * WIN, WIN), WIN), :]
                results.append((rows, jnp.dot(pick, entries, preferred_element_type=jnp.float32)))
            for rows, value in results:
                acc[rows, :] += value
            return carry

        lax.fori_loop(0, count // WIN_UNROLL, gather_body, 0)
        base += count

    coarse[...] = jnp.maximum(acc[...] + bias_ref[...], 0.0).astype(jnp.bfloat16)

    base = 0
    for out in outs:
        count = out.shape[1] // WIN

        def scatter_body(u, carry, out=out, base=base):
            for t in range(WIN_UNROLL):
                j = u * WIN_UNROLL + t
                pick, rows = pick_of(base + j)
                chosen = lax.dot_general(coarse[rows, :], pick, TN, preferred_element_type=jnp.float32)
                out[:, pl.ds(pl.multiple_of(j * WIN, WIN), WIN)] = chosen.astype(jnp.bfloat16)
            return carry

        lax.fori_loop(0, count // WIN_UNROLL, scatter_body, 0)
        base += count


def up_kernel(own_mode, count_ref, order_ref, win_ref, off_ref, xt_ref, e_ref, wt_ref, *refs):
    step = pl.program_id(0)
    per_step = e_ref.shape[0]
    neighbours = count_ref[step]
    if own_mode:
        parents_ref, out_ref = refs
        first_window = 0
        start, stop = neighbours, per_step
    else:
        n_groups = len(step_table)
        sources = refs[:n_groups]
        prev_ref, out_ref, parents_ref, sems = refs[n_groups:]
        first_window = SELF_CAP // WIN
        start, stop = 0, neighbours

        @pl.when(step == 0)
        def _():
            copies = []
            offset = 0
            for index, src in enumerate(sources):
                size = src.shape[1]
                copy = pltpu.make_async_copy(src, parents_ref.at[:, pl.ds(offset, size)], sems.at[index])
                copy.start()
                copies.append(copy)
                offset += size
            for copy in copies:
                copy.wait()

        out_ref[...] = prev_ref[...]

    def body(u, carry):
        for t in range(UNROLL):
            position = jnp.minimum(start + u * UNROLL + t, stop - 1)
            j = order_ref[step * per_step + position]
            brick = step * per_step + j
            window = win_ref[brick] - first_window
            offset = off_ref[brick]
            inside = jnp.bitwise_and(e_ref[pl.ds(j, 1), :], WIN - 1)
            pick = one_hot_rows(inside)
            parents = parents_ref[:, pl.ds(pl.multiple_of(window * WIN, WIN), WIN)]
            rows_t = jnp.dot(parents, pick, preferred_element_type=jnp.float32).astype(jnp.bfloat16)
            lifted = jnp.dot(wt_ref[offset], rows_t, preferred_element_type=jnp.float32)
            cols = pl.ds(pl.multiple_of(j * BLK, BLK), BLK)
            out_ref[:, cols] = (xt_ref[:, cols].astype(jnp.float32) + lifted).astype(out_ref.dtype)
        return carry

    lax.fori_loop(0, (stop - start + UNROLL - 1) // UNROLL, body, 0)


def group_route(g, sign):
    n_outer = lax.axis_size("outer")
    n_inner = lax.axis_size("inner")
    a, b = step_table[g]
    route = []
    for s in range(n_outer * n_inner):
        row, col = divmod(s, n_inner)
        owner = ((row + a) % n_outer) * n_inner + (col + b) % n_inner
        route.append((s, owner) if sign > 0 else (owner, s))
    return route


def local(features, block_offset, parent_entry, owner_cell, w_down, b_down, w_up):
    n_groups = len(step_table)
    fine_rows, in_width = features.shape
    out_width = w_down.shape[2]
    entries = owner_cell.shape[1]
    cap = (entries - SELF_CAP) // n_groups
    blocks = fine_rows // BLK
    steps = blocks // BRICKS_PER_STEP

    xt = features.T
    entry_rows = parent_entry.reshape(blocks, BLK)
    brick_window = entry_rows[:, 0] // WIN
    cells = owner_cell.reshape(entries // WIN, WIN)
    cell_window = jnp.min(cells, axis=1) // WIN
    w_up_t = jnp.swapaxes(w_up, 1, 2)

    part_shapes = [jax.ShapeDtypeStruct((SELF_CAP, out_width), jnp.bfloat16)] + [
        jax.ShapeDtypeStruct((cap, out_width), jnp.bfloat16)
    ] * n_groups
    answer_shapes = [jax.ShapeDtypeStruct((s.shape[1], s.shape[0]), s.dtype) for s in part_shapes]
    whole = lambda shape: pl.BlockSpec(shape, lambda *idx: (0,) * len(shape))

    is_far = (brick_window >= SELF_CAP // WIN).astype(jnp.int32).reshape(steps, BRICKS_PER_STEP)
    far_count = jnp.sum(is_far, axis=1)
    far_rank = jnp.cumsum(is_far, axis=1) - is_far
    own_rank = jnp.cumsum(1 - is_far, axis=1) - (1 - is_far)
    position = jnp.where(is_far == 1, far_rank, far_count[:, None] + own_rank)
    local_ids = jnp.arange(BRICKS_PER_STEP, dtype=jnp.int32)
    order = jnp.sum(
        jnp.where(position[:, None, :] == local_ids[None, :, None], local_ids[None, None, :], 0), axis=2
    )
    order = order.reshape(blocks).astype(jnp.int32)
    counts = far_count.astype(jnp.int32)

    def down_call(first_window, shapes):
        rows = sum(s.shape[0] for s in shapes)
        return pl.pallas_call(
            functools.partial(down_kernel, first_window),
            out_shape=shapes,
            grid_spec=pltpu.PrefetchScalarGridSpec(
                num_scalar_prefetch=4,
                grid=(steps,),
                in_specs=[
                    pl.BlockSpec((in_width, BRICKS_PER_STEP * BLK), lambda i, *_: (0, i)),
                    pl.BlockSpec((BRICKS_PER_STEP, BLK), lambda i, *_: (i, 0)),
                    whole(w_down.shape),
                ],
                out_specs=[whole(s.shape) for s in shapes],
                scratch_shapes=[pltpu.VMEM((rows + WIN, out_width), jnp.float32)],
            ),
            compiler_params=pltpu.CompilerParams(dimension_semantics=("arbitrary",)),
            cost_estimate=pl.CostEstimate(
                flops=2 * fine_rows * in_width * out_width,
                transcendentals=0,
                bytes_accessed=fine_rows * (in_width * 2 + 4) + rows * out_width * 2,
            ),
        )(counts, order, brick_window, block_offset, xt, entry_rows, w_down)

    parts = [None] + list(down_call(SELF_CAP // WIN, part_shapes[1:]))
    parts[0] = down_call(0, part_shapes[:1])[0]

    arrived = [
        lax.ppermute(parts[1 + g], ("outer", "inner"), group_route(g, 1)) for g in range(n_groups)
    ]

    coarse = pl.pallas_call(
        coarse_kernel,
        out_shape=answer_shapes,
        grid_spec=pltpu.PrefetchScalarGridSpec(
            num_scalar_prefetch=1,
            grid=(1,),
            in_specs=[whole(cells.shape), whole((1, out_width))]
            + [whole(s.shape) for s in part_shapes],
            out_specs=[whole(s.shape) for s in answer_shapes],
            scratch_shapes=[
                pltpu.VMEM((C_DEV, out_width), jnp.float32),
                pltpu.VMEM((C_DEV, out_width), jnp.bfloat16),
            ],
        ),
        cost_estimate=pl.CostEstimate(
            flops=4 * entries * WIN * out_width,
            transcendentals=0,
            bytes_accessed=4 * entries * out_width,
        ),
    )
    answers = coarse(cell_window, cells, b_down.reshape(1, out_width), parts[0], *arrived)

    returned = [
        lax.ppermute(answers[1 + g], ("outer", "inner"), group_route(g, -1)) for g in range(n_groups)
    ]

    chunk = pl.BlockSpec((in_width, BRICKS_PER_STEP * BLK), lambda i, *_: (0, i))
    rows_spec = pl.BlockSpec((BRICKS_PER_STEP, BLK), lambda i, *_: (i, 0))
    out_shape = jax.ShapeDtypeStruct((in_width, fine_rows), features.dtype)
    up_cost = pl.CostEstimate(
        flops=2 * fine_rows * in_width * out_width,
        transcendentals=0,
        bytes_accessed=fine_rows * (in_width * 2 + 2),
    )
    own_up = pl.pallas_call(
        functools.partial(up_kernel, True),
        out_shape=out_shape,
        grid_spec=pltpu.PrefetchScalarGridSpec(
            num_scalar_prefetch=4,
            grid=(steps,),
            in_specs=[chunk, rows_spec, whole(w_up_t.shape), whole(answer_shapes[0].shape)],
            out_specs=chunk,
        ),
        compiler_params=pltpu.CompilerParams(dimension_semantics=("arbitrary",)),
        cost_estimate=up_cost,
    )
    partial_out = own_up(counts, order, brick_window, block_offset, xt, entry_rows, w_up_t, answers[0])

    far_up = pl.pallas_call(
        functools.partial(up_kernel, False),
        out_shape=out_shape,
        grid_spec=pltpu.PrefetchScalarGridSpec(
            num_scalar_prefetch=4,
            grid=(steps,),
            in_specs=[chunk, rows_spec, whole(w_up_t.shape)]
            + [pl.BlockSpec(memory_space=pl.ANY)] * n_groups
            + [chunk],
            out_specs=chunk,
            scratch_shapes=[
                pltpu.VMEM((out_width, entries - SELF_CAP), jnp.bfloat16),
                pltpu.SemaphoreType.DMA((n_groups,)),
            ],
        ),
        input_output_aliases={4 + 3 + n_groups: 0},
        compiler_params=pltpu.CompilerParams(dimension_semantics=("arbitrary",)),
        cost_estimate=up_cost,
    )
    out_t = far_up(counts, order, brick_window, block_offset, xt, entry_rows, w_up_t, *returned, partial_out)
    return out_t.T


def solution(mesh):
    in_specs = (
        P(("outer", "inner"), None),
        P(("outer", "inner")),
        P(("outer", "inner")),
        P(("outer", "inner"), None),
        P(),
        P(),
        P(),
    )
    out_specs = P(("outer", "inner"), None)
    return jax.shard_map(local, mesh=mesh, in_specs=in_specs, out_specs=out_specs, check_vma=False)
```

```python
import functools

import jax
import jax.numpy as jnp
from jax import lax
from jax.experimental import pallas as pl
from jax.experimental.pallas import tpu as pltpu
from jax.sharding import PartitionSpec as P

BLK = 128
C_DEV = 4096
SELF_CAP = 4096
WIN = 128
BRICKS_PER_STEP = 64
UNROLL = 8
WIN_UNROLL = 4

step_table = ((-1, -1), (-1, 0), (-1, 1), (0, -1), (0, 1), (1, -1), (1, 0), (1, 1))

NT = (((1,), (1,)), ((), ()))
TN = (((0,), (0,)), ((), ()))


def split_parts(data):
    high = data.astype(jnp.bfloat16)
    low = (data - high.astype(jnp.float32)).astype(jnp.bfloat16)
    return high, low


def one_hot_rows(index_row):
    span = lax.broadcasted_iota(jnp.int32, (WIN, index_row.shape[1]), 0)
    return (span == index_row).astype(jnp.bfloat16)


def down_kernel(first_window, count_ref, order_ref, win_ref, off_ref, xt_ref, e_ref, w_ref, *refs):
    outs = refs[:-1]
    acc = refs[-1]
    step = pl.program_id(0)
    per_step = e_ref.shape[0]
    trash = acc.shape[0] // WIN - 1

    @pl.when(step == 0)
    def _():
        acc[...] = jnp.zeros_like(acc)

    neighbours = count_ref[step]
    if first_window == 0:
        start, stop = neighbours, per_step
    else:
        start, stop = 0, neighbours

    def body(u, carry):
        results = []
        for t in range(UNROLL):
            position = start + u * UNROLL + t
            j = order_ref[step * per_step + jnp.minimum(position, per_step - 1)]
            brick = step * per_step + j
            window = jnp.where(position < stop, win_ref[brick] - first_window, trash)
            offset = off_ref[brick]
            inside = jnp.bitwise_and(e_ref[pl.ds(j, 1), :], WIN - 1)
            pick = one_hot_rows(inside)
            cols = pl.ds(pl.multiple_of(j * BLK, BLK), BLK)
            summed = lax.dot_general(pick, xt_ref[:, cols], NT, preferred_element_type=jnp.float32)
            part = jnp.dot(summed.astype(jnp.bfloat16), w_ref[offset], preferred_element_type=jnp.float32)
            results.append((window, part))
        for window, part in results:
            rows = pl.ds(pl.multiple_of(window * WIN, WIN), WIN)
            acc[rows, :] += part
        return carry

    lax.fori_loop(0, (stop - start + UNROLL - 1) // UNROLL, body, 0)

    @pl.when(step == pl.num_programs(0) - 1)
    def _():
        size = outs[0].shape[0]
        for g, out in enumerate(outs):
            out[...] = acc[g * size : (g + 1) * size, :].astype(out.dtype)


def coarse_kernel(cw_ref, cells_ref, bias_ref, *refs):
    n_groups = len(step_table)
    sources = refs[: 1 + n_groups]
    outs = refs[1 + n_groups : 2 + 2 * n_groups]
    acc, coarse = refs[2 + 2 * n_groups :]
    cell_windows = acc.shape[0] // WIN
    acc[...] = jnp.zeros_like(acc)

    def pick_of(w):
        window = jnp.minimum(cw_ref[w], cell_windows - 1)
        cells = cells_ref[pl.ds(w, 1), :]
        inside = jnp.where(cells < C_DEV, cells - window * WIN, -1)
        rows = pl.ds(pl.multiple_of(window * WIN, WIN), WIN)
        return one_hot_rows(inside), rows

    base = 0
    for src in sources:
        count = src.shape[0] // WIN

        def gather_body(u, carry, src=src, base=base):
            results = []
            for t in range(WIN_UNROLL):
                j = u * WIN_UNROLL + t
                pick, rows = pick_of(base + j)
                entries = src[pl.ds(pl.multiple_of(j * WIN, WIN), WIN), :]
                results.append((rows, jnp.dot(pick, entries, preferred_element_type=jnp.float32)))
            for rows, value in results:
                acc[rows, :] += value
            return carry

        lax.fori_loop(0, count // WIN_UNROLL, gather_body, 0)
        base += count

    coarse[...] = jnp.maximum(acc[...] + bias_ref[...], 0.0).astype(jnp.bfloat16)

    base = 0
    for out in outs:
        count = out.shape[1] // WIN

        def scatter_body(u, carry, out=out, base=base):
            for t in range(WIN_UNROLL):
                j = u * WIN_UNROLL + t
                pick, rows = pick_of(base + j)
                chosen = lax.dot_general(coarse[rows, :], pick, TN, preferred_element_type=jnp.float32)
                out[:, pl.ds(pl.multiple_of(j * WIN, WIN), WIN)] = chosen.astype(jnp.bfloat16)
            return carry

        lax.fori_loop(0, count // WIN_UNROLL, scatter_body, 0)
        base += count


def up_kernel(win_ref, off_ref, xt_ref, e_ref, wt_ref, *refs):
    n_groups = len(step_table)
    sources = refs[: 1 + n_groups]
    out_ref = refs[1 + n_groups]
    stack, sems = refs[2 + n_groups :]
    step = pl.program_id(0)
    per_step = e_ref.shape[0]

    @pl.when(step == 0)
    def _():
        copies = []
        start = 0
        for index, src in enumerate(sources):
            size = src.shape[1]
            copy = pltpu.make_async_copy(src, stack.at[:, pl.ds(start, size)], sems.at[index])
            copy.start()
            copies.append(copy)
            start += size
        for copy in copies:
            copy.wait()

    def body(u, carry):
        for t in range(UNROLL):
            j = u * UNROLL + t
            brick = step * per_step + j
            window = win_ref[brick]
            offset = off_ref[brick]
            inside = jnp.bitwise_and(e_ref[pl.ds(j, 1), :], WIN - 1)
            pick = one_hot_rows(inside)
            parents = stack[:, pl.ds(pl.multiple_of(window * WIN, WIN), WIN)]
            rows_t = jnp.dot(parents, pick, preferred_element_type=jnp.float32).astype(jnp.bfloat16)
            lifted = jnp.dot(wt_ref[offset], rows_t, preferred_element_type=jnp.float32)
            cols = pl.ds(pl.multiple_of(j * BLK, BLK), BLK)
            out_ref[:, cols] = (xt_ref[:, cols].astype(jnp.float32) + lifted).astype(out_ref.dtype)
        return carry

    lax.fori_loop(0, per_step // UNROLL, body, 0)


def group_route(g, sign):
    n_outer = lax.axis_size("outer")
    n_inner = lax.axis_size("inner")
    a, b = step_table[g]
    route = []
    for s in range(n_outer * n_inner):
        row, col = divmod(s, n_inner)
        owner = ((row + a) % n_outer) * n_inner + (col + b) % n_inner
        route.append((s, owner) if sign > 0 else (owner, s))
    return route


def local(features, block_offset, parent_entry, owner_cell, w_down, b_down, w_up):
    n_groups = len(step_table)
    fine_rows, in_width = features.shape
    out_width = w_down.shape[2]
    entries = owner_cell.shape[1]
    cap = (entries - SELF_CAP) // n_groups
    blocks = fine_rows // BLK
    steps = blocks // BRICKS_PER_STEP

    xt = features.T
    entry_rows = parent_entry.reshape(blocks, BLK)
    brick_window = entry_rows[:, 0] // WIN
    cells = owner_cell.reshape(entries // WIN, WIN)
    cell_window = jnp.min(cells, axis=1) // WIN
    w_up_t = jnp.swapaxes(w_up, 1, 2)

    part_shapes = [jax.ShapeDtypeStruct((SELF_CAP, out_width), jnp.bfloat16)] + [
        jax.ShapeDtypeStruct((cap, out_width), jnp.bfloat16)
    ] * n_groups
    answer_shapes = [jax.ShapeDtypeStruct((s.shape[1], s.shape[0]), s.dtype) for s in part_shapes]
    whole = lambda shape: pl.BlockSpec(shape, lambda *idx: (0,) * len(shape))

    is_far = (brick_window >= SELF_CAP // WIN).astype(jnp.int32).reshape(steps, BRICKS_PER_STEP)
    far_count = jnp.sum(is_far, axis=1)
    far_rank = jnp.cumsum(is_far, axis=1) - is_far
    own_rank = jnp.cumsum(1 - is_far, axis=1) - (1 - is_far)
    position = jnp.where(is_far == 1, far_rank, far_count[:, None] + own_rank)
    local_ids = jnp.arange(BRICKS_PER_STEP, dtype=jnp.int32)
    order = jnp.sum(
        jnp.where(position[:, None, :] == local_ids[None, :, None], local_ids[None, None, :], 0), axis=2
    )
    order = order.reshape(blocks).astype(jnp.int32)
    counts = far_count.astype(jnp.int32)

    def down_call(first_window, shapes):
        rows = sum(s.shape[0] for s in shapes)
        return pl.pallas_call(
            functools.partial(down_kernel, first_window),
            out_shape=shapes,
            grid_spec=pltpu.PrefetchScalarGridSpec(
                num_scalar_prefetch=4,
                grid=(steps,),
                in_specs=[
                    pl.BlockSpec((in_width, BRICKS_PER_STEP * BLK), lambda i, *_: (0, i)),
                    pl.BlockSpec((BRICKS_PER_STEP, BLK), lambda i, *_: (i, 0)),
                    whole(w_down.shape),
                ],
                out_specs=[whole(s.shape) for s in shapes],
                scratch_shapes=[pltpu.VMEM((rows + WIN, out_width), jnp.float32)],
            ),
            compiler_params=pltpu.CompilerParams(dimension_semantics=("arbitrary",)),
            cost_estimate=pl.CostEstimate(
                flops=2 * fine_rows * in_width * out_width,
                transcendentals=0,
                bytes_accessed=fine_rows * (in_width * 2 + 4) + rows * out_width * 2,
            ),
        )(counts, order, brick_window, block_offset, xt, entry_rows, w_down)

    parts = [None] + list(down_call(SELF_CAP // WIN, part_shapes[1:]))
    parts[0] = down_call(0, part_shapes[:1])[0]

    arrived = [
        lax.ppermute(parts[1 + g], ("outer", "inner"), group_route(g, 1)) for g in range(n_groups)
    ]

    coarse = pl.pallas_call(
        coarse_kernel,
        out_shape=answer_shapes,
        grid_spec=pltpu.PrefetchScalarGridSpec(
            num_scalar_prefetch=1,
            grid=(1,),
            in_specs=[whole(cells.shape), whole((1, out_width))]
            + [whole(s.shape) for s in part_shapes],
            out_specs=[whole(s.shape) for s in answer_shapes],
            scratch_shapes=[
                pltpu.VMEM((C_DEV, out_width), jnp.float32),
                pltpu.VMEM((C_DEV, out_width), jnp.bfloat16),
            ],
        ),
        cost_estimate=pl.CostEstimate(
            flops=4 * entries * WIN * out_width,
            transcendentals=0,
            bytes_accessed=4 * entries * out_width,
        ),
    )
    answers = coarse(cell_window, cells, b_down.reshape(1, out_width), parts[0], *arrived)

    returned = [
        lax.ppermute(answers[1 + g], ("outer", "inner"), group_route(g, -1)) for g in range(n_groups)
    ]

    up = pl.pallas_call(
        up_kernel,
        out_shape=jax.ShapeDtypeStruct((in_width, fine_rows), features.dtype),
        grid_spec=pltpu.PrefetchScalarGridSpec(
            num_scalar_prefetch=2,
            grid=(steps,),
            in_specs=[
                pl.BlockSpec((in_width, BRICKS_PER_STEP * BLK), lambda i, *_: (0, i)),
                pl.BlockSpec((BRICKS_PER_STEP, BLK), lambda i, *_: (i, 0)),
                whole(w_up_t.shape),
            ]
            + [pl.BlockSpec(memory_space=pl.ANY)] * (1 + n_groups),
            out_specs=pl.BlockSpec((in_width, BRICKS_PER_STEP * BLK), lambda i, *_: (0, i)),
            scratch_shapes=[
                pltpu.VMEM((out_width, entries), jnp.bfloat16),
                pltpu.SemaphoreType.DMA((1 + n_groups,)),
            ],
        ),
        compiler_params=pltpu.CompilerParams(dimension_semantics=("arbitrary",)),
        cost_estimate=pl.CostEstimate(
            flops=6 * fine_rows * in_width * out_width,
            transcendentals=0,
            bytes_accessed=fine_rows * (in_width * 4 + 4) + entries * out_width * 2,
        ),
    )
    out_t = up(brick_window, block_offset, xt, entry_rows, w_up_t, answers[0], *returned)
    return out_t.T


def solution(mesh):
    in_specs = (
        P(("outer", "inner"), None),
        P(("outer", "inner")),
        P(("outer", "inner")),
        P(("outer", "inner"), None),
        P(),
        P(),
        P(),
    )
    out_specs = P(("outer", "inner"), None)
    return jax.shard_map(local, mesh=mesh, in_specs=in_specs, out_specs=out_specs, check_vma=False)
```

```python
import functools

import jax
import jax.numpy as jnp
from jax import lax
from jax.experimental import pallas as pl
from jax.experimental.pallas import tpu as pltpu
from jax.sharding import PartitionSpec as P

BLK = 128
C_DEV = 4096
SELF_CAP = 4096
WIN = 128
BRICKS_PER_STEP = 64
UNROLL = 16
WIN_UNROLL = 8

step_table = ((-1, -1), (-1, 0), (-1, 1), (0, -1), (0, 1), (1, -1), (1, 0), (1, 1))

NT = (((1,), (1,)), ((), ()))
TN = (((0,), (0,)), ((), ()))


def split_parts(data):
    high = data.astype(jnp.bfloat16)
    low = (data - high.astype(jnp.float32)).astype(jnp.bfloat16)
    return high, low


def one_hot_rows(index_row):
    span = lax.broadcasted_iota(jnp.int32, (WIN, index_row.shape[1]), 0)
    return (span == index_row).astype(jnp.bfloat16)


def down_kernel(first_window, count_ref, order_ref, win_ref, off_ref, xt_ref, e_ref, w_ref, *refs):
    outs = refs[:-1]
    acc = refs[-1]
    step = pl.program_id(0)
    per_step = e_ref.shape[0]
    trash = acc.shape[0] // WIN - 1

    @pl.when(step == 0)
    def _():
        acc[...] = jnp.zeros_like(acc)

    neighbours = count_ref[step]
    if first_window == 0:
        start, stop = neighbours, per_step
    else:
        start, stop = 0, neighbours

    def body(u, carry):
        results = []
        for t in range(UNROLL):
            position = start + u * UNROLL + t
            j = order_ref[step * per_step + jnp.minimum(position, per_step - 1)]
            brick = step * per_step + j
            window = jnp.where(position < stop, win_ref[brick] - first_window, trash)
            offset = off_ref[brick]
            inside = jnp.bitwise_and(e_ref[pl.ds(j, 1), :], WIN - 1)
            pick = one_hot_rows(inside)
            cols = pl.ds(pl.multiple_of(j * BLK, BLK), BLK)
            summed = lax.dot_general(pick, xt_ref[:, cols], NT, preferred_element_type=jnp.float32)
            part = jnp.dot(summed.astype(jnp.bfloat16), w_ref[offset], preferred_element_type=jnp.float32)
            results.append((window, part))
        for window, part in results:
            rows = pl.ds(pl.multiple_of(window * WIN, WIN), WIN)
            acc[rows, :] += part
        return carry

    lax.fori_loop(0, (stop - start + UNROLL - 1) // UNROLL, body, 0)

    @pl.when(step == pl.num_programs(0) - 1)
    def _():
        size = outs[0].shape[0]
        for g, out in enumerate(outs):
            out[...] = acc[g * size : (g + 1) * size, :].astype(out.dtype)


def coarse_kernel(cw_ref, cells_ref, bias_ref, *refs):
    n_groups = len(step_table)
    sources = refs[: 1 + n_groups]
    outs = refs[1 + n_groups : 2 + 2 * n_groups]
    acc, coarse = refs[2 + 2 * n_groups :]
    cell_windows = acc.shape[0] // WIN
    acc[...] = jnp.zeros_like(acc)

    def pick_of(w):
        window = jnp.minimum(cw_ref[w], cell_windows - 1)
        cells = cells_ref[pl.ds(w, 1), :]
        inside = jnp.where(cells < C_DEV, cells - window * WIN, -1)
        rows = pl.ds(pl.multiple_of(window * WIN, WIN), WIN)
        return one_hot_rows(inside), rows

    base = 0
    for src in sources:
        count = src.shape[0] // WIN
        unroll = min(WIN_UNROLL, count)

        def gather_body(u, carry, src=src, base=base, unroll=unroll):
            results = []
            for t in range(unroll):
                j = u * unroll + t
                pick, rows = pick_of(base + j)
                entries = src[pl.ds(pl.multiple_of(j * WIN, WIN), WIN), :]
                results.append((rows, jnp.dot(pick, entries, preferred_element_type=jnp.float32)))
            for rows, value in results:
                acc[rows, :] += value
            return carry

        lax.fori_loop(0, count // unroll, gather_body, 0)
        base += count

    coarse[...] = jnp.maximum(acc[...] + bias_ref[...], 0.0).astype(jnp.bfloat16)

    base = 0
    for out in outs:
        count = out.shape[1] // WIN
        unroll = min(WIN_UNROLL, count)

        def scatter_body(u, carry, out=out, base=base, unroll=unroll):
            for t in range(unroll):
                j = u * unroll + t
                pick, rows = pick_of(base + j)
                chosen = lax.dot_general(coarse[rows, :], pick, TN, preferred_element_type=jnp.float32)
                out[:, pl.ds(pl.multiple_of(j * WIN, WIN), WIN)] = chosen.astype(jnp.bfloat16)
            return carry

        lax.fori_loop(0, count // unroll, scatter_body, 0)
        base += count


def up_kernel(win_ref, off_ref, xt_ref, e_ref, wt_ref, *refs):
    n_groups = len(step_table)
    sources = refs[: 1 + n_groups]
    out_ref = refs[1 + n_groups]
    stack, sems = refs[2 + n_groups :]
    step = pl.program_id(0)
    per_step = e_ref.shape[0]

    @pl.when(step == 0)
    def _():
        copies = []
        start = 0
        for index, src in enumerate(sources):
            size = src.shape[1]
            copy = pltpu.make_async_copy(src, stack.at[:, pl.ds(start, size)], sems.at[index])
            copy.start()
            copies.append(copy)
            start += size
        for copy in copies:
            copy.wait()

    def body(u, carry):
        for t in range(UNROLL):
            j = u * UNROLL + t
            brick = step * per_step + j
            window = win_ref[brick]
            offset = off_ref[brick]
            inside = jnp.bitwise_and(e_ref[pl.ds(j, 1), :], WIN - 1)
            pick = one_hot_rows(inside)
            parents = stack[:, pl.ds(pl.multiple_of(window * WIN, WIN), WIN)]
            rows_t = jnp.dot(parents, pick, preferred_element_type=jnp.float32).astype(jnp.bfloat16)
            lifted = jnp.dot(wt_ref[offset], rows_t, preferred_element_type=jnp.float32)
            cols = pl.ds(pl.multiple_of(j * BLK, BLK), BLK)
            out_ref[:, cols] = (xt_ref[:, cols].astype(jnp.float32) + lifted).astype(out_ref.dtype)
        return carry

    lax.fori_loop(0, per_step // UNROLL, body, 0)


def group_route(g, sign):
    n_outer = lax.axis_size("outer")
    n_inner = lax.axis_size("inner")
    a, b = step_table[g]
    route = []
    for s in range(n_outer * n_inner):
        row, col = divmod(s, n_inner)
        owner = ((row + a) % n_outer) * n_inner + (col + b) % n_inner
        route.append((s, owner) if sign > 0 else (owner, s))
    return route


def local(features, block_offset, parent_entry, owner_cell, w_down, b_down, w_up):
    n_groups = len(step_table)
    fine_rows, in_width = features.shape
    out_width = w_down.shape[2]
    entries = owner_cell.shape[1]
    cap = (entries - SELF_CAP) // n_groups
    blocks = fine_rows // BLK
    steps = blocks // BRICKS_PER_STEP

    xt = features.T
    entry_rows = parent_entry.reshape(blocks, BLK)
    brick_window = entry_rows[:, 0] // WIN
    cells = owner_cell.reshape(entries // WIN, WIN)
    cell_window = jnp.min(cells, axis=1) // WIN
    w_up_t = jnp.swapaxes(w_up, 1, 2)

    part_shapes = [jax.ShapeDtypeStruct((SELF_CAP, out_width), jnp.bfloat16)] + [
        jax.ShapeDtypeStruct((cap, out_width), jnp.bfloat16)
    ] * n_groups
    answer_shapes = [jax.ShapeDtypeStruct((s.shape[1], s.shape[0]), s.dtype) for s in part_shapes]
    whole = lambda shape: pl.BlockSpec(shape, lambda *idx: (0,) * len(shape))

    is_far = (brick_window >= SELF_CAP // WIN).astype(jnp.int32).reshape(steps, BRICKS_PER_STEP)
    far_count = jnp.sum(is_far, axis=1)
    far_rank = jnp.cumsum(is_far, axis=1) - is_far
    own_rank = jnp.cumsum(1 - is_far, axis=1) - (1 - is_far)
    position = jnp.where(is_far == 1, far_rank, far_count[:, None] + own_rank)
    local_ids = jnp.arange(BRICKS_PER_STEP, dtype=jnp.int32)
    order = jnp.sum(
        jnp.where(position[:, None, :] == local_ids[None, :, None], local_ids[None, None, :], 0), axis=2
    )
    order = order.reshape(blocks).astype(jnp.int32)
    counts = far_count.astype(jnp.int32)

    def down_call(first_window, shapes):
        rows = sum(s.shape[0] for s in shapes)
        return pl.pallas_call(
            functools.partial(down_kernel, first_window),
            out_shape=shapes,
            grid_spec=pltpu.PrefetchScalarGridSpec(
                num_scalar_prefetch=4,
                grid=(steps,),
                in_specs=[
                    pl.BlockSpec((in_width, BRICKS_PER_STEP * BLK), lambda i, *_: (0, i)),
                    pl.BlockSpec((BRICKS_PER_STEP, BLK), lambda i, *_: (i, 0)),
                    whole(w_down.shape),
                ],
                out_specs=[whole(s.shape) for s in shapes],
                scratch_shapes=[pltpu.VMEM((rows + WIN, out_width), jnp.float32)],
            ),
            compiler_params=pltpu.CompilerParams(dimension_semantics=("arbitrary",)),
            cost_estimate=pl.CostEstimate(
                flops=2 * fine_rows * in_width * out_width,
                transcendentals=0,
                bytes_accessed=fine_rows * (in_width * 2 + 4) + rows * out_width * 2,
            ),
        )(counts, order, brick_window, block_offset, xt, entry_rows, w_down)

    parts = [None] + list(down_call(SELF_CAP // WIN, part_shapes[1:]))
    parts[0] = down_call(0, part_shapes[:1])[0]

    arrived = [
        lax.ppermute(parts[1 + g], ("outer", "inner"), group_route(g, 1)) for g in range(n_groups)
    ]

    coarse = pl.pallas_call(
        coarse_kernel,
        out_shape=answer_shapes,
        grid_spec=pltpu.PrefetchScalarGridSpec(
            num_scalar_prefetch=1,
            grid=(1,),
            in_specs=[whole(cells.shape), whole((1, out_width))]
            + [whole(s.shape) for s in part_shapes],
            out_specs=[whole(s.shape) for s in answer_shapes],
            scratch_shapes=[
                pltpu.VMEM((C_DEV, out_width), jnp.float32),
                pltpu.VMEM((C_DEV, out_width), jnp.bfloat16),
            ],
        ),
        cost_estimate=pl.CostEstimate(
            flops=4 * entries * WIN * out_width,
            transcendentals=0,
            bytes_accessed=4 * entries * out_width,
        ),
    )
    answers = coarse(cell_window, cells, b_down.reshape(1, out_width), parts[0], *arrived)

    returned = [
        lax.ppermute(answers[1 + g], ("outer", "inner"), group_route(g, -1)) for g in range(n_groups)
    ]

    up = pl.pallas_call(
        up_kernel,
        out_shape=jax.ShapeDtypeStruct((in_width, fine_rows), features.dtype),
        grid_spec=pltpu.PrefetchScalarGridSpec(
            num_scalar_prefetch=2,
            grid=(steps,),
            in_specs=[
                pl.BlockSpec((in_width, BRICKS_PER_STEP * BLK), lambda i, *_: (0, i)),
                pl.BlockSpec((BRICKS_PER_STEP, BLK), lambda i, *_: (i, 0)),
                whole(w_up_t.shape),
            ]
            + [pl.BlockSpec(memory_space=pl.ANY)] * (1 + n_groups),
            out_specs=pl.BlockSpec((in_width, BRICKS_PER_STEP * BLK), lambda i, *_: (0, i)),
            scratch_shapes=[
                pltpu.VMEM((out_width, entries), jnp.bfloat16),
                pltpu.SemaphoreType.DMA((1 + n_groups,)),
            ],
        ),
        compiler_params=pltpu.CompilerParams(dimension_semantics=("arbitrary",)),
        cost_estimate=pl.CostEstimate(
            flops=6 * fine_rows * in_width * out_width,
            transcendentals=0,
            bytes_accessed=fine_rows * (in_width * 4 + 4) + entries * out_width * 2,
        ),
    )
    out_t = up(brick_window, block_offset, xt, entry_rows, w_up_t, answers[0], *returned)
    return out_t.T


def solution(mesh):
    in_specs = (
        P(("outer", "inner"), None),
        P(("outer", "inner")),
        P(("outer", "inner")),
        P(("outer", "inner"), None),
        P(),
        P(),
        P(),
    )
    out_specs = P(("outer", "inner"), None)
    return jax.shard_map(local, mesh=mesh, in_specs=in_specs, out_specs=out_specs, check_vma=False)
```

```python
import functools

import jax
import jax.numpy as jnp
from jax import lax
from jax.experimental import pallas as pl
from jax.experimental.pallas import tpu as pltpu
from jax.sharding import PartitionSpec as P

BLK = 128
C_DEV = 4096
SELF_CAP = 4096
WIN = 128
BRICKS_PER_STEP = 64
UNROLL = 16
TAIL = 4
UP_UNROLL = 32
WIN_UNROLL = 16

step_table = ((-1, -1), (-1, 0), (-1, 1), (0, -1), (0, 1), (1, -1), (1, 0), (1, 1))

NT = (((1,), (1,)), ((), ()))
TN = (((0,), (0,)), ((), ()))


def split_parts(data):
    high = data.astype(jnp.bfloat16)
    low = (data - high.astype(jnp.float32)).astype(jnp.bfloat16)
    return high, low


def one_hot_rows(index_row):
    span = lax.broadcasted_iota(jnp.int32, (WIN, index_row.shape[1]), 0)
    return (span == index_row).astype(jnp.bfloat16)


def down_kernel(first_window, count_ref, order_ref, win_ref, off_ref, xt_ref, e_ref, w_ref, *refs):
    outs = refs[:-1]
    acc = refs[-1]
    step = pl.program_id(0)
    per_step = e_ref.shape[0]
    trash = acc.shape[0] // WIN - 1

    @pl.when(step == 0)
    def _():
        acc[...] = jnp.zeros_like(acc)

    neighbours = count_ref[step]
    if first_window == 0:
        start, stop = neighbours, per_step
    else:
        start, stop = 0, neighbours

    def run(first, width, trips):
        def body(u, carry):
            results = []
            for t in range(width):
                position = first + u * width + t
                j = order_ref[step * per_step + jnp.minimum(position, per_step - 1)]
                brick = step * per_step + j
                window = jnp.where(position < stop, win_ref[brick] - first_window, trash)
                offset = off_ref[brick]
                inside = jnp.bitwise_and(e_ref[pl.ds(j, 1), :], WIN - 1)
                pick = one_hot_rows(inside)
                cols = pl.ds(pl.multiple_of(j * BLK, BLK), BLK)
                summed = lax.dot_general(pick, xt_ref[:, cols], NT, preferred_element_type=jnp.float32)
                part = jnp.dot(summed.astype(jnp.bfloat16), w_ref[offset], preferred_element_type=jnp.float32)
                results.append((window, part))
            for window, part in results:
                rows = pl.ds(pl.multiple_of(window * WIN, WIN), WIN)
                acc[rows, :] += part
            return carry

        lax.fori_loop(0, trips, body, 0)

    full = (stop - start) // UNROLL
    run(start, UNROLL, full)
    tail_start = start + full * UNROLL
    run(tail_start, TAIL, (stop - tail_start + TAIL - 1) // TAIL)

    @pl.when(step == pl.num_programs(0) - 1)
    def _():
        size = outs[0].shape[0]
        for g, out in enumerate(outs):
            out[...] = acc[g * size : (g + 1) * size, :].astype(out.dtype)


def coarse_kernel(cw_ref, cells_ref, bias_ref, *refs):
    n_groups = len(step_table)
    sources = refs[: 1 + n_groups]
    outs = refs[1 + n_groups : 2 + 2 * n_groups]
    acc, coarse = refs[2 + 2 * n_groups :]
    cell_windows = acc.shape[0] // WIN
    acc[...] = jnp.zeros_like(acc)

    def pick_of(w):
        window = jnp.minimum(cw_ref[w], cell_windows - 1)
        cells = cells_ref[pl.ds(w, 1), :]
        inside = jnp.where(cells < C_DEV, cells - window * WIN, -1)
        rows = pl.ds(pl.multiple_of(window * WIN, WIN), WIN)
        return one_hot_rows(inside), rows

    base = 0
    for src in sources:
        count = src.shape[0] // WIN
        unroll = min(WIN_UNROLL, count)

        def gather_body(u, carry, src=src, base=base, unroll=unroll):
            results = []
            for t in range(unroll):
                j = u * unroll + t
                pick, rows = pick_of(base + j)
                entries = src[pl.ds(pl.multiple_of(j * WIN, WIN), WIN), :]
                results.append((rows, jnp.dot(pick, entries, preferred_element_type=jnp.float32)))
            for rows, value in results:
                acc[rows, :] += value
            return carry

        lax.fori_loop(0, count // unroll, gather_body, 0)
        base += count

    coarse[...] = jnp.maximum(acc[...] + bias_ref[...], 0.0).astype(jnp.bfloat16)

    base = 0
    for out in outs:
        count = out.shape[1] // WIN
        unroll = min(WIN_UNROLL, count)

        def scatter_body(u, carry, out=out, base=base, unroll=unroll):
            for t in range(unroll):
                j = u * unroll + t
                pick, rows = pick_of(base + j)
                chosen = lax.dot_general(coarse[rows, :], pick, TN, preferred_element_type=jnp.float32)
                out[:, pl.ds(pl.multiple_of(j * WIN, WIN), WIN)] = chosen.astype(jnp.bfloat16)
            return carry

        lax.fori_loop(0, count // unroll, scatter_body, 0)
        base += count


def up_kernel(win_ref, off_ref, xt_ref, e_ref, wt_ref, *refs):
    n_groups = len(step_table)
    sources = refs[: 1 + n_groups]
    out_ref = refs[1 + n_groups]
    stack, sems = refs[2 + n_groups :]
    step = pl.program_id(0)
    per_step = e_ref.shape[0]

    @pl.when(step == 0)
    def _():
        copies = []
        start = 0
        for index, src in enumerate(sources):
            size = src.shape[1]
            copy = pltpu.make_async_copy(src, stack.at[:, pl.ds(start, size)], sems.at[index])
            copy.start()
            copies.append(copy)
            start += size
        for copy in copies:
            copy.wait()

    def body(u, carry):
        for t in range(UP_UNROLL):
            j = u * UP_UNROLL + t
            brick = step * per_step + j
            window = win_ref[brick]
            offset = off_ref[brick]
            inside = jnp.bitwise_and(e_ref[pl.ds(j, 1), :], WIN - 1)
            pick = one_hot_rows(inside)
            parents = stack[:, pl.ds(pl.multiple_of(window * WIN, WIN), WIN)]
            rows_t = jnp.dot(parents, pick, preferred_element_type=jnp.float32).astype(jnp.bfloat16)
            lifted = jnp.dot(wt_ref[offset], rows_t, preferred_element_type=jnp.float32)
            cols = pl.ds(pl.multiple_of(j * BLK, BLK), BLK)
            out_ref[:, cols] = (xt_ref[:, cols].astype(jnp.float32) + lifted).astype(out_ref.dtype)
        return carry

    lax.fori_loop(0, per_step // UP_UNROLL, body, 0)


def group_route(g, sign):
    n_outer = lax.axis_size("outer")
    n_inner = lax.axis_size("inner")
    a, b = step_table[g]
    route = []
    for s in range(n_outer * n_inner):
        row, col = divmod(s, n_inner)
        owner = ((row + a) % n_outer) * n_inner + (col + b) % n_inner
        route.append((s, owner) if sign > 0 else (owner, s))
    return route


def local(features, block_offset, parent_entry, owner_cell, w_down, b_down, w_up):
    n_groups = len(step_table)
    fine_rows, in_width = features.shape
    out_width = w_down.shape[2]
    entries = owner_cell.shape[1]
    cap = (entries - SELF_CAP) // n_groups
    blocks = fine_rows // BLK
    steps = blocks // BRICKS_PER_STEP

    xt = features.T
    entry_rows = parent_entry.reshape(blocks, BLK)
    brick_window = entry_rows[:, 0] // WIN
    cells = owner_cell.reshape(entries // WIN, WIN)
    cell_window = jnp.min(cells, axis=1) // WIN
    w_up_t = jnp.swapaxes(w_up, 1, 2)

    part_shapes = [jax.ShapeDtypeStruct((SELF_CAP, out_width), jnp.bfloat16)] + [
        jax.ShapeDtypeStruct((cap, out_width), jnp.bfloat16)
    ] * n_groups
    answer_shapes = [jax.ShapeDtypeStruct((s.shape[1], s.shape[0]), s.dtype) for s in part_shapes]
    whole = lambda shape: pl.BlockSpec(shape, lambda *idx: (0,) * len(shape))

    is_far = (brick_window >= SELF_CAP // WIN).astype(jnp.int32).reshape(steps, BRICKS_PER_STEP)
    far_count = jnp.sum(is_far, axis=1)
    far_rank = jnp.cumsum(is_far, axis=1) - is_far
    own_rank = jnp.cumsum(1 - is_far, axis=1) - (1 - is_far)
    position = jnp.where(is_far == 1, far_rank, far_count[:, None] + own_rank)
    local_ids = jnp.arange(BRICKS_PER_STEP, dtype=jnp.int32)
    order = jnp.sum(
        jnp.where(position[:, None, :] == local_ids[None, :, None], local_ids[None, None, :], 0), axis=2
    )
    order = order.reshape(blocks).astype(jnp.int32)
    counts = far_count.astype(jnp.int32)

    def down_call(first_window, shapes):
        rows = sum(s.shape[0] for s in shapes)
        return pl.pallas_call(
            functools.partial(down_kernel, first_window),
            out_shape=shapes,
            grid_spec=pltpu.PrefetchScalarGridSpec(
                num_scalar_prefetch=4,
                grid=(steps,),
                in_specs=[
                    pl.BlockSpec((in_width, BRICKS_PER_STEP * BLK), lambda i, *_: (0, i)),
                    pl.BlockSpec((BRICKS_PER_STEP, BLK), lambda i, *_: (i, 0)),
                    whole(w_down.shape),
                ],
                out_specs=[whole(s.shape) for s in shapes],
                scratch_shapes=[pltpu.VMEM((rows + WIN, out_width), jnp.float32)],
            ),
            compiler_params=pltpu.CompilerParams(dimension_semantics=("arbitrary",)),
            cost_estimate=pl.CostEstimate(
                flops=2 * fine_rows * in_width * out_width,
                transcendentals=0,
                bytes_accessed=fine_rows * (in_width * 2 + 4) + rows * out_width * 2,
            ),
        )(counts, order, brick_window, block_offset, xt, entry_rows, w_down)

    parts = [None] + list(down_call(SELF_CAP // WIN, part_shapes[1:]))
    parts[0] = down_call(0, part_shapes[:1])[0]

    arrived = [
        lax.ppermute(parts[1 + g], ("outer", "inner"), group_route(g, 1)) for g in range(n_groups)
    ]

    coarse = pl.pallas_call(
        coarse_kernel,
        out_shape=answer_shapes,
        grid_spec=pltpu.PrefetchScalarGridSpec(
            num_scalar_prefetch=1,
            grid=(1,),
            in_specs=[whole(cells.shape), whole((1, out_width))]
            + [whole(s.shape) for s in part_shapes],
            out_specs=[whole(s.shape) for s in answer_shapes],
            scratch_shapes=[
                pltpu.VMEM((C_DEV, out_width), jnp.float32),
                pltpu.VMEM((C_DEV, out_width), jnp.bfloat16),
            ],
        ),
        cost_estimate=pl.CostEstimate(
            flops=4 * entries * WIN * out_width,
            transcendentals=0,
            bytes_accessed=4 * entries * out_width,
        ),
    )
    answers = coarse(cell_window, cells, b_down.reshape(1, out_width), parts[0], *arrived)

    returned = [
        lax.ppermute(answers[1 + g], ("outer", "inner"), group_route(g, -1)) for g in range(n_groups)
    ]

    up = pl.pallas_call(
        up_kernel,
        out_shape=jax.ShapeDtypeStruct((in_width, fine_rows), features.dtype),
        grid_spec=pltpu.PrefetchScalarGridSpec(
            num_scalar_prefetch=2,
            grid=(steps,),
            in_specs=[
                pl.BlockSpec((in_width, BRICKS_PER_STEP * BLK), lambda i, *_: (0, i)),
                pl.BlockSpec((BRICKS_PER_STEP, BLK), lambda i, *_: (i, 0)),
                whole(w_up_t.shape),
            ]
            + [pl.BlockSpec(memory_space=pl.ANY)] * (1 + n_groups),
            out_specs=pl.BlockSpec((in_width, BRICKS_PER_STEP * BLK), lambda i, *_: (0, i)),
            scratch_shapes=[
                pltpu.VMEM((out_width, entries), jnp.bfloat16),
                pltpu.SemaphoreType.DMA((1 + n_groups,)),
            ],
        ),
        compiler_params=pltpu.CompilerParams(dimension_semantics=("arbitrary",)),
        cost_estimate=pl.CostEstimate(
            flops=6 * fine_rows * in_width * out_width,
            transcendentals=0,
            bytes_accessed=fine_rows * (in_width * 4 + 4) + entries * out_width * 2,
        ),
    )
    out_t = up(brick_window, block_offset, xt, entry_rows, w_up_t, answers[0], *returned)
    return out_t.T


def solution(mesh):
    in_specs = (
        P(("outer", "inner"), None),
        P(("outer", "inner")),
        P(("outer", "inner")),
        P(("outer", "inner"), None),
        P(),
        P(),
        P(),
    )
    out_specs = P(("outer", "inner"), None)
    return jax.shard_map(local, mesh=mesh, in_specs=in_specs, out_specs=out_specs, check_vma=False)
```

```python
import functools

import jax
import jax.numpy as jnp
from jax import lax
from jax.experimental import pallas as pl
from jax.experimental.pallas import tpu as pltpu
from jax.sharding import PartitionSpec as P

BLK = 128
C_DEV = 4096
SELF_CAP = 4096
WIN = 128
BRICKS_PER_STEP = 64
UNROLL = 16
UP_UNROLL = 32
WIN_UNROLL = 16

step_table = ((-1, -1), (-1, 0), (-1, 1), (0, -1), (0, 1), (1, -1), (1, 0), (1, 1))

NT = (((1,), (1,)), ((), ()))
TN = (((0,), (0,)), ((), ()))


def split_parts(data):
    high = data.astype(jnp.bfloat16)
    low = (data - high.astype(jnp.float32)).astype(jnp.bfloat16)
    return high, low


def one_hot_rows(index_row):
    span = lax.broadcasted_iota(jnp.int32, (WIN, index_row.shape[1]), 0)
    return (span == index_row).astype(jnp.bfloat16)


def down_kernel(first_window, count_ref, order_ref, win_ref, off_ref, xt_ref, e_ref, w_ref, *refs):
    outs = refs[:-1]
    acc = refs[-1]
    step = pl.program_id(0)
    per_step = e_ref.shape[0]
    trash = acc.shape[0] // WIN - 1

    @pl.when(step == 0)
    def _():
        acc[...] = jnp.zeros_like(acc)

    neighbours = count_ref[step]
    if first_window == 0:
        start, stop = neighbours, per_step
    else:
        start, stop = 0, neighbours

    def run(first, width, trips):
        def body(u, carry):
            results = []
            for t in range(width):
                position = first + u * width + t
                j = order_ref[step * per_step + jnp.minimum(position, per_step - 1)]
                brick = step * per_step + j
                window = jnp.where(position < stop, win_ref[brick] - first_window, trash)
                offset = off_ref[brick]
                inside = jnp.bitwise_and(e_ref[pl.ds(j, 1), :], WIN - 1)
                pick = one_hot_rows(inside)
                cols = pl.ds(pl.multiple_of(j * BLK, BLK), BLK)
                summed = lax.dot_general(pick, xt_ref[:, cols], NT, preferred_element_type=jnp.float32)
                part = jnp.dot(summed.astype(jnp.bfloat16), w_ref[offset], preferred_element_type=jnp.float32)
                results.append((window, part))
            for window, part in results:
                rows = pl.ds(pl.multiple_of(window * WIN, WIN), WIN)
                acc[rows, :] += part
            return carry

        lax.fori_loop(0, trips, body, 0)

    run(start, UNROLL, (stop - start + UNROLL - 1) // UNROLL)

    @pl.when(step == pl.num_programs(0) - 1)
    def _():
        size = outs[0].shape[0]
        for g, out in enumerate(outs):
            out[...] = acc[g * size : (g + 1) * size, :].astype(out.dtype)


def coarse_kernel(cw_ref, cells_ref, bias_ref, *refs):
    n_groups = len(step_table)
    sources = refs[: 1 + n_groups]
    outs = refs[1 + n_groups : 2 + 2 * n_groups]
    acc, coarse = refs[2 + 2 * n_groups :]
    cell_windows = acc.shape[0] // WIN
    acc[...] = jnp.zeros_like(acc)

    def pick_of(w):
        window = jnp.minimum(cw_ref[w], cell_windows - 1)
        cells = cells_ref[pl.ds(w, 1), :]
        inside = jnp.where(cells < C_DEV, cells - window * WIN, -1)
        rows = pl.ds(pl.multiple_of(window * WIN, WIN), WIN)
        return one_hot_rows(inside), rows

    base = 0
    for src in sources:
        count = src.shape[0] // WIN
        unroll = min(WIN_UNROLL, count)

        def gather_body(u, carry, src=src, base=base, unroll=unroll):
            results = []
            for t in range(unroll):
                j = u * unroll + t
                pick, rows = pick_of(base + j)
                entries = src[pl.ds(pl.multiple_of(j * WIN, WIN), WIN), :]
                results.append((rows, jnp.dot(pick, entries, preferred_element_type=jnp.float32)))
            for rows, value in results:
                acc[rows, :] += value
            return carry

        lax.fori_loop(0, count // unroll, gather_body, 0)
        base += count

    coarse[...] = jnp.maximum(acc[...] + bias_ref[...], 0.0).astype(jnp.bfloat16)

    base = 0
    for out in outs:
        count = out.shape[1] // WIN
        unroll = min(WIN_UNROLL, count)

        def scatter_body(u, carry, out=out, base=base, unroll=unroll):
            for t in range(unroll):
                j = u * unroll + t
                pick, rows = pick_of(base + j)
                chosen = lax.dot_general(coarse[rows, :], pick, TN, preferred_element_type=jnp.float32)
                out[:, pl.ds(pl.multiple_of(j * WIN, WIN), WIN)] = chosen.astype(jnp.bfloat16)
            return carry

        lax.fori_loop(0, count // unroll, scatter_body, 0)
        base += count


def up_kernel(win_ref, off_ref, xt_ref, e_ref, wt_ref, *refs):
    n_groups = len(step_table)
    sources = refs[: 1 + n_groups]
    out_ref = refs[1 + n_groups]
    stack, sems = refs[2 + n_groups :]
    step = pl.program_id(0)
    per_step = e_ref.shape[0]

    @pl.when(step == 0)
    def _():
        copies = []
        start = 0
        for index, src in enumerate(sources):
            size = src.shape[1]
            copy = pltpu.make_async_copy(src, stack.at[:, pl.ds(start, size)], sems.at[index])
            copy.start()
            copies.append(copy)
            start += size
        for copy in copies:
            copy.wait()

    def body(u, carry):
        for t in range(UP_UNROLL):
            j = u * UP_UNROLL + t
            brick = step * per_step + j
            window = win_ref[brick]
            offset = off_ref[brick]
            inside = jnp.bitwise_and(e_ref[pl.ds(j, 1), :], WIN - 1)
            pick = one_hot_rows(inside)
            parents = stack[:, pl.ds(pl.multiple_of(window * WIN, WIN), WIN)]
            rows_t = jnp.dot(parents, pick, preferred_element_type=jnp.float32).astype(jnp.bfloat16)
            lifted = jnp.dot(wt_ref[offset], rows_t, preferred_element_type=jnp.float32)
            cols = pl.ds(pl.multiple_of(j * BLK, BLK), BLK)
            out_ref[:, cols] = (xt_ref[:, cols].astype(jnp.float32) + lifted).astype(out_ref.dtype)
        return carry

    lax.fori_loop(0, per_step // UP_UNROLL, body, 0)


def group_route(g, sign):
    n_outer = lax.axis_size("outer")
    n_inner = lax.axis_size("inner")
    a, b = step_table[g]
    route = []
    for s in range(n_outer * n_inner):
        row, col = divmod(s, n_inner)
        owner = ((row + a) % n_outer) * n_inner + (col + b) % n_inner
        route.append((s, owner) if sign > 0 else (owner, s))
    return route


def local(features, block_offset, parent_entry, owner_cell, w_down, b_down, w_up):
    n_groups = len(step_table)
    fine_rows, in_width = features.shape
    out_width = w_down.shape[2]
    entries = owner_cell.shape[1]
    cap = (entries - SELF_CAP) // n_groups
    blocks = fine_rows // BLK
    steps = blocks // BRICKS_PER_STEP

    xt = features.T
    entry_rows = parent_entry.reshape(blocks, BLK)
    brick_window = entry_rows[:, 0] // WIN
    cells = owner_cell.reshape(entries // WIN, WIN)
    cell_window = jnp.min(cells, axis=1) // WIN
    w_up_t = jnp.swapaxes(w_up, 1, 2)

    part_shapes = [jax.ShapeDtypeStruct((SELF_CAP, out_width), jnp.bfloat16)] + [
        jax.ShapeDtypeStruct((cap, out_width), jnp.bfloat16)
    ] * n_groups
    answer_shapes = [jax.ShapeDtypeStruct((s.shape[1], s.shape[0]), s.dtype) for s in part_shapes]
    whole = lambda shape: pl.BlockSpec(shape, lambda *idx: (0,) * len(shape))

    is_far = (brick_window >= SELF_CAP // WIN).astype(jnp.int32).reshape(steps, BRICKS_PER_STEP)
    far_count = jnp.sum(is_far, axis=1)
    far_rank = jnp.cumsum(is_far, axis=1) - is_far
    own_rank = jnp.cumsum(1 - is_far, axis=1) - (1 - is_far)
    position = jnp.where(is_far == 1, far_rank, far_count[:, None] + own_rank)
    local_ids = jnp.arange(BRICKS_PER_STEP, dtype=jnp.int32)
    order = jnp.sum(
        jnp.where(position[:, None, :] == local_ids[None, :, None], local_ids[None, None, :], 0), axis=2
    )
    order = order.reshape(blocks).astype(jnp.int32)
    counts = far_count.astype(jnp.int32)

    def down_call(first_window, shapes):
        rows = sum(s.shape[0] for s in shapes)
        return pl.pallas_call(
            functools.partial(down_kernel, first_window),
            out_shape=shapes,
            grid_spec=pltpu.PrefetchScalarGridSpec(
                num_scalar_prefetch=4,
                grid=(steps,),
                in_specs=[
                    pl.BlockSpec((in_width, BRICKS_PER_STEP * BLK), lambda i, *_: (0, i)),
                    pl.BlockSpec((BRICKS_PER_STEP, BLK), lambda i, *_: (i, 0)),
                    whole(w_down.shape),
                ],
                out_specs=[whole(s.shape) for s in shapes],
                scratch_shapes=[pltpu.VMEM((rows + WIN, out_width), jnp.float32)],
            ),
            compiler_params=pltpu.CompilerParams(dimension_semantics=("arbitrary",)),
            cost_estimate=pl.CostEstimate(
                flops=2 * fine_rows * in_width * out_width,
                transcendentals=0,
                bytes_accessed=fine_rows * (in_width * 2 + 4) + rows * out_width * 2,
            ),
        )(counts, order, brick_window, block_offset, xt, entry_rows, w_down)

    parts = [None] + list(down_call(SELF_CAP // WIN, part_shapes[1:]))
    parts[0] = down_call(0, part_shapes[:1])[0]

    arrived = [
        lax.ppermute(parts[1 + g], ("outer", "inner"), group_route(g, 1)) for g in range(n_groups)
    ]

    coarse = pl.pallas_call(
        coarse_kernel,
        out_shape=answer_shapes,
        grid_spec=pltpu.PrefetchScalarGridSpec(
            num_scalar_prefetch=1,
            grid=(1,),
            in_specs=[whole(cells.shape), whole((1, out_width))]
            + [whole(s.shape) for s in part_shapes],
            out_specs=[whole(s.shape) for s in answer_shapes],
            scratch_shapes=[
                pltpu.VMEM((C_DEV, out_width), jnp.float32),
                pltpu.VMEM((C_DEV, out_width), jnp.bfloat16),
            ],
        ),
        cost_estimate=pl.CostEstimate(
            flops=4 * entries * WIN * out_width,
            transcendentals=0,
            bytes_accessed=4 * entries * out_width,
        ),
    )
    answers = coarse(cell_window, cells, b_down.reshape(1, out_width), parts[0], *arrived)

    returned = [
        lax.ppermute(answers[1 + g], ("outer", "inner"), group_route(g, -1)) for g in range(n_groups)
    ]

    up = pl.pallas_call(
        up_kernel,
        out_shape=jax.ShapeDtypeStruct((in_width, fine_rows), features.dtype),
        grid_spec=pltpu.PrefetchScalarGridSpec(
            num_scalar_prefetch=2,
            grid=(steps,),
            in_specs=[
                pl.BlockSpec((in_width, BRICKS_PER_STEP * BLK), lambda i, *_: (0, i)),
                pl.BlockSpec((BRICKS_PER_STEP, BLK), lambda i, *_: (i, 0)),
                whole(w_up_t.shape),
            ]
            + [pl.BlockSpec(memory_space=pl.ANY)] * (1 + n_groups),
            out_specs=pl.BlockSpec((in_width, BRICKS_PER_STEP * BLK), lambda i, *_: (0, i)),
            scratch_shapes=[
                pltpu.VMEM((out_width, entries), jnp.bfloat16),
                pltpu.SemaphoreType.DMA((1 + n_groups,)),
            ],
        ),
        compiler_params=pltpu.CompilerParams(dimension_semantics=("arbitrary",)),
        cost_estimate=pl.CostEstimate(
            flops=6 * fine_rows * in_width * out_width,
            transcendentals=0,
            bytes_accessed=fine_rows * (in_width * 4 + 4) + entries * out_width * 2,
        ),
    )
    out_t = up(brick_window, block_offset, xt, entry_rows, w_up_t, answers[0], *returned)
    return out_t.T


def solution(mesh):
    in_specs = (
        P(("outer", "inner"), None),
        P(("outer", "inner")),
        P(("outer", "inner")),
        P(("outer", "inner"), None),
        P(),
        P(),
        P(),
    )
    out_specs = P(("outer", "inner"), None)
    return jax.shard_map(local, mesh=mesh, in_specs=in_specs, out_specs=out_specs, check_vma=False)
```

```python
import functools

import jax
import jax.numpy as jnp
from jax import lax
from jax.experimental import pallas as pl
from jax.experimental.pallas import tpu as pltpu
from jax.sharding import PartitionSpec as P

BLK = 128
C_DEV = 4096
SELF_CAP = 4096
WIN = 128
BRICKS_PER_STEP = 64
UNROLL = 16
SPLIT_UNROLL = 16
WIN_UNROLL = 16

step_table = ((-1, -1), (-1, 0), (-1, 1), (0, -1), (0, 1), (1, -1), (1, 0), (1, 1))

NT = (((1,), (1,)), ((), ()))
TN = (((0,), (0,)), ((), ()))


def split_parts(data):
    high = data.astype(jnp.bfloat16)
    low = (data - high.astype(jnp.float32)).astype(jnp.bfloat16)
    return high, low


def one_hot_rows(index_row):
    span = lax.broadcasted_iota(jnp.int32, (WIN, index_row.shape[1]), 0)
    return (span == index_row).astype(jnp.bfloat16)


def down_kernel(first_window, count_ref, order_ref, win_ref, off_ref, xt_ref, e_ref, w_ref, *refs):
    outs = refs[:-1]
    acc = refs[-1]
    step = pl.program_id(0)
    per_step = e_ref.shape[0]
    trash = acc.shape[0] // WIN - 1

    @pl.when(step == 0)
    def _():
        acc[...] = jnp.zeros_like(acc)

    neighbours = count_ref[step]
    if first_window == 0:
        start, stop = neighbours, per_step
    else:
        start, stop = 0, neighbours

    def run(first, width, trips):
        def body(u, carry):
            results = []
            for t in range(width):
                position = first + u * width + t
                j = order_ref[step * per_step + jnp.minimum(position, per_step - 1)]
                brick = step * per_step + j
                window = jnp.where(position < stop, win_ref[brick] - first_window, trash)
                offset = off_ref[brick]
                inside = jnp.bitwise_and(e_ref[pl.ds(j, 1), :], WIN - 1)
                pick = one_hot_rows(inside)
                cols = pl.ds(pl.multiple_of(j * BLK, BLK), BLK)
                summed = lax.dot_general(pick, xt_ref[:, cols], NT, preferred_element_type=jnp.float32)
                part = jnp.dot(summed.astype(jnp.bfloat16), w_ref[offset], preferred_element_type=jnp.float32)
                results.append((window, part))
            for window, part in results:
                rows = pl.ds(pl.multiple_of(window * WIN, WIN), WIN)
                acc[rows, :] += part
            return carry

        lax.fori_loop(0, trips, body, 0)

    run(start, UNROLL, (stop - start + UNROLL - 1) // UNROLL)

    @pl.when(step == pl.num_programs(0) - 1)
    def _():
        size = outs[0].shape[0]
        for g, out in enumerate(outs):
            out[...] = acc[g * size : (g + 1) * size, :].astype(out.dtype)


def coarse_kernel(cw_ref, cells_ref, bias_ref, *refs):
    n_groups = len(step_table)
    sources = refs[: 1 + n_groups]
    outs = refs[1 + n_groups : 2 + 2 * n_groups]
    acc, coarse = refs[2 + 2 * n_groups :]
    cell_windows = acc.shape[0] // WIN
    acc[...] = jnp.zeros_like(acc)

    def pick_of(w):
        window = jnp.minimum(cw_ref[w], cell_windows - 1)
        cells = cells_ref[pl.ds(w, 1), :]
        inside = jnp.where(cells < C_DEV, cells - window * WIN, -1)
        rows = pl.ds(pl.multiple_of(window * WIN, WIN), WIN)
        return one_hot_rows(inside), rows

    base = 0
    for src in sources:
        count = src.shape[0] // WIN
        unroll = min(WIN_UNROLL, count)

        def gather_body(u, carry, src=src, base=base, unroll=unroll):
            results = []
            for t in range(unroll):
                j = u * unroll + t
                pick, rows = pick_of(base + j)
                entries = src[pl.ds(pl.multiple_of(j * WIN, WIN), WIN), :]
                results.append((rows, jnp.dot(pick, entries, preferred_element_type=jnp.float32)))
            for rows, value in results:
                acc[rows, :] += value
            return carry

        lax.fori_loop(0, count // unroll, gather_body, 0)
        base += count

    coarse[...] = jnp.maximum(acc[...] + bias_ref[...], 0.0).astype(jnp.bfloat16)

    base = 0
    for out in outs:
        count = out.shape[1] // WIN
        unroll = min(WIN_UNROLL, count)

        def scatter_body(u, carry, out=out, base=base, unroll=unroll):
            for t in range(unroll):
                j = u * unroll + t
                pick, rows = pick_of(base + j)
                chosen = lax.dot_general(coarse[rows, :], pick, TN, preferred_element_type=jnp.float32)
                out[:, pl.ds(pl.multiple_of(j * WIN, WIN), WIN)] = chosen.astype(jnp.bfloat16)
            return carry

        lax.fori_loop(0, count // unroll, scatter_body, 0)
        base += count


def up_kernel(own_mode, count_ref, order_ref, win_ref, off_ref, xt_ref, e_ref, wt_ref, *refs):
    step = pl.program_id(0)
    per_step = e_ref.shape[0]
    neighbours = count_ref[step]
    if own_mode:
        parents_ref, out_ref = refs
        first_window = 0
        start, stop = neighbours, per_step
    else:
        n_groups = len(step_table)
        sources = refs[:n_groups]
        prev_ref, out_ref, parents_ref, sems = refs[n_groups:]
        first_window = SELF_CAP // WIN
        start, stop = 0, neighbours

        @pl.when(step == 0)
        def _():
            copies = []
            offset = 0
            for index, src in enumerate(sources):
                size = src.shape[1]
                copy = pltpu.make_async_copy(src, parents_ref.at[:, pl.ds(offset, size)], sems.at[index])
                copy.start()
                copies.append(copy)
                offset += size
            for copy in copies:
                copy.wait()

        out_ref[...] = prev_ref[...]

    def body(u, carry):
        for t in range(SPLIT_UNROLL):
            position = jnp.minimum(start + u * SPLIT_UNROLL + t, stop - 1)
            j = order_ref[step * per_step + position]
            brick = step * per_step + j
            window = win_ref[brick] - first_window
            offset = off_ref[brick]
            inside = jnp.bitwise_and(e_ref[pl.ds(j, 1), :], WIN - 1)
            pick = one_hot_rows(inside)
            parents = parents_ref[:, pl.ds(pl.multiple_of(window * WIN, WIN), WIN)]
            rows_t = jnp.dot(parents, pick, preferred_element_type=jnp.float32).astype(jnp.bfloat16)
            lifted = jnp.dot(wt_ref[offset], rows_t, preferred_element_type=jnp.float32)
            cols = pl.ds(pl.multiple_of(j * BLK, BLK), BLK)
            out_ref[:, cols] = (xt_ref[:, cols].astype(jnp.float32) + lifted).astype(out_ref.dtype)
        return carry

    lax.fori_loop(0, (stop - start + SPLIT_UNROLL - 1) // SPLIT_UNROLL, body, 0)


def group_route(g, sign):
    n_outer = lax.axis_size("outer")
    n_inner = lax.axis_size("inner")
    a, b = step_table[g]
    route = []
    for s in range(n_outer * n_inner):
        row, col = divmod(s, n_inner)
        owner = ((row + a) % n_outer) * n_inner + (col + b) % n_inner
        route.append((s, owner) if sign > 0 else (owner, s))
    return route


def local(features, block_offset, parent_entry, owner_cell, w_down, b_down, w_up):
    n_groups = len(step_table)
    fine_rows, in_width = features.shape
    out_width = w_down.shape[2]
    entries = owner_cell.shape[1]
    cap = (entries - SELF_CAP) // n_groups
    blocks = fine_rows // BLK
    steps = blocks // BRICKS_PER_STEP

    xt = features.T
    entry_rows = parent_entry.reshape(blocks, BLK)
    brick_window = entry_rows[:, 0] // WIN
    cells = owner_cell.reshape(entries // WIN, WIN)
    cell_window = jnp.min(cells, axis=1) // WIN
    w_up_t = jnp.swapaxes(w_up, 1, 2)

    part_shapes = [jax.ShapeDtypeStruct((SELF_CAP, out_width), jnp.bfloat16)] + [
        jax.ShapeDtypeStruct((cap, out_width), jnp.bfloat16)
    ] * n_groups
    answer_shapes = [jax.ShapeDtypeStruct((s.shape[1], s.shape[0]), s.dtype) for s in part_shapes]
    whole = lambda shape: pl.BlockSpec(shape, lambda *idx: (0,) * len(shape))

    is_far = (brick_window >= SELF_CAP // WIN).astype(jnp.int32).reshape(steps, BRICKS_PER_STEP)
    far_count = jnp.sum(is_far, axis=1)
    far_rank = jnp.cumsum(is_far, axis=1) - is_far
    own_rank = jnp.cumsum(1 - is_far, axis=1) - (1 - is_far)
    position = jnp.where(is_far == 1, far_rank, far_count[:, None] + own_rank)
    local_ids = jnp.arange(BRICKS_PER_STEP, dtype=jnp.int32)
    order = jnp.sum(
        jnp.where(position[:, None, :] == local_ids[None, :, None], local_ids[None, None, :], 0), axis=2
    )
    order = order.reshape(blocks).astype(jnp.int32)
    counts = far_count.astype(jnp.int32)

    def down_call(first_window, shapes):
        rows = sum(s.shape[0] for s in shapes)
        return pl.pallas_call(
            functools.partial(down_kernel, first_window),
            out_shape=shapes,
            grid_spec=pltpu.PrefetchScalarGridSpec(
                num_scalar_prefetch=4,
                grid=(steps,),
                in_specs=[
                    pl.BlockSpec((in_width, BRICKS_PER_STEP * BLK), lambda i, *_: (0, i)),
                    pl.BlockSpec((BRICKS_PER_STEP, BLK), lambda i, *_: (i, 0)),
                    whole(w_down.shape),
                ],
                out_specs=[whole(s.shape) for s in shapes],
                scratch_shapes=[pltpu.VMEM((rows + WIN, out_width), jnp.float32)],
            ),
            compiler_params=pltpu.CompilerParams(dimension_semantics=("arbitrary",)),
            cost_estimate=pl.CostEstimate(
                flops=2 * fine_rows * in_width * out_width,
                transcendentals=0,
                bytes_accessed=fine_rows * (in_width * 2 + 4) + rows * out_width * 2,
            ),
        )(counts, order, brick_window, block_offset, xt, entry_rows, w_down)

    parts = [None] + list(down_call(SELF_CAP // WIN, part_shapes[1:]))
    parts[0] = down_call(0, part_shapes[:1])[0]

    arrived = [
        lax.ppermute(parts[1 + g], ("outer", "inner"), group_route(g, 1)) for g in range(n_groups)
    ]

    coarse = pl.pallas_call(
        coarse_kernel,
        out_shape=answer_shapes,
        grid_spec=pltpu.PrefetchScalarGridSpec(
            num_scalar_prefetch=1,
            grid=(1,),
            in_specs=[whole(cells.shape), whole((1, out_width))]
            + [whole(s.shape) for s in part_shapes],
            out_specs=[whole(s.shape) for s in answer_shapes],
            scratch_shapes=[
                pltpu.VMEM((C_DEV, out_width), jnp.float32),
                pltpu.VMEM((C_DEV, out_width), jnp.bfloat16),
            ],
        ),
        cost_estimate=pl.CostEstimate(
            flops=4 * entries * WIN * out_width,
            transcendentals=0,
            bytes_accessed=4 * entries * out_width,
        ),
    )
    answers = coarse(cell_window, cells, b_down.reshape(1, out_width), parts[0], *arrived)

    returned = [
        lax.ppermute(answers[1 + g], ("outer", "inner"), group_route(g, -1)) for g in range(n_groups)
    ]

    chunk = pl.BlockSpec((in_width, BRICKS_PER_STEP * BLK), lambda i, *_: (0, i))
    rows_spec = pl.BlockSpec((BRICKS_PER_STEP, BLK), lambda i, *_: (i, 0))
    out_shape = jax.ShapeDtypeStruct((in_width, fine_rows), features.dtype)
    up_cost = pl.CostEstimate(
        flops=2 * fine_rows * in_width * out_width,
        transcendentals=0,
        bytes_accessed=fine_rows * (in_width * 2 + 2),
    )
    own_up = pl.pallas_call(
        functools.partial(up_kernel, True),
        out_shape=out_shape,
        grid_spec=pltpu.PrefetchScalarGridSpec(
            num_scalar_prefetch=4,
            grid=(steps,),
            in_specs=[chunk, rows_spec, whole(w_up_t.shape), whole(answer_shapes[0].shape)],
            out_specs=chunk,
        ),
        compiler_params=pltpu.CompilerParams(dimension_semantics=("arbitrary",)),
        cost_estimate=up_cost,
    )
    partial_out = own_up(counts, order, brick_window, block_offset, xt, entry_rows, w_up_t, answers[0])

    far_up = pl.pallas_call(
        functools.partial(up_kernel, False),
        out_shape=out_shape,
        grid_spec=pltpu.PrefetchScalarGridSpec(
            num_scalar_prefetch=4,
            grid=(steps,),
            in_specs=[chunk, rows_spec, whole(w_up_t.shape)]
            + [pl.BlockSpec(memory_space=pl.ANY)] * n_groups
            + [chunk],
            out_specs=chunk,
            scratch_shapes=[
                pltpu.VMEM((out_width, entries - SELF_CAP), jnp.bfloat16),
                pltpu.SemaphoreType.DMA((n_groups,)),
            ],
        ),
        input_output_aliases={4 + 3 + n_groups: 0},
        compiler_params=pltpu.CompilerParams(dimension_semantics=("arbitrary",)),
        cost_estimate=up_cost,
    )
    out_t = far_up(counts, order, brick_window, block_offset, xt, entry_rows, w_up_t, *returned, partial_out)
    return out_t.T


def solution(mesh):
    in_specs = (
        P(("outer", "inner"), None),
        P(("outer", "inner")),
        P(("outer", "inner")),
        P(("outer", "inner"), None),
        P(),
        P(),
        P(),
    )
    out_specs = P(("outer", "inner"), None)
    return jax.shard_map(local, mesh=mesh, in_specs=in_specs, out_specs=out_specs, check_vma=False)
```

```python
import functools

import jax
import jax.numpy as jnp
from jax import lax
from jax.experimental import pallas as pl
from jax.experimental.pallas import tpu as pltpu
from jax.sharding import PartitionSpec as P

BLK = 128
C_DEV = 4096
SELF_CAP = 4096
WIN = 128
BRICKS_PER_STEP = 64
UNROLL = 16
UP_UNROLL = 32
WIN_UNROLL = 16

step_table = ((-1, -1), (-1, 0), (-1, 1), (0, -1), (0, 1), (1, -1), (1, 0), (1, 1))

NT = (((1,), (1,)), ((), ()))
TN = (((0,), (0,)), ((), ()))


def split_parts(data):
    high = data.astype(jnp.bfloat16)
    low = (data - high.astype(jnp.float32)).astype(jnp.bfloat16)
    return high, low


def one_hot_rows(index_row):
    span = lax.broadcasted_iota(jnp.int32, (WIN, index_row.shape[1]), 0)
    return (span == index_row).astype(jnp.bfloat16)


def down_kernel(first_window, count_ref, order_ref, win_ref, off_ref, xt_ref, e_ref, w_ref, *refs):
    outs = refs[:-1]
    acc = refs[-1]
    step = pl.program_id(0)
    per_step = e_ref.shape[0]
    trash = acc.shape[0] // WIN - 1

    @pl.when(step == 0)
    def _():
        acc[...] = jnp.zeros_like(acc)

    neighbours = count_ref[step]
    if first_window == 0:
        start, stop = neighbours, per_step
    else:
        start, stop = 0, neighbours

    def run(first, width, trips):
        def body(u, carry):
            results = []
            for t in range(width):
                position = first + u * width + t
                packed = order_ref[step * per_step + jnp.minimum(position, per_step - 1)]
                j = jnp.bitwise_and(packed, 255)
                window = jnp.bitwise_and(jnp.right_shift(packed, 8), 255)
                window = jnp.where(position < stop, window - first_window, trash)
                offset = jnp.right_shift(packed, 16)
                inside = jnp.bitwise_and(e_ref[pl.ds(j, 1), :], WIN - 1)
                pick = one_hot_rows(inside)
                cols = pl.ds(pl.multiple_of(j * BLK, BLK), BLK)
                summed = lax.dot_general(pick, xt_ref[:, cols], NT, preferred_element_type=jnp.float32)
                part = jnp.dot(summed.astype(jnp.bfloat16), w_ref[offset], preferred_element_type=jnp.float32)
                results.append((window, part))
            for window, part in results:
                rows = pl.ds(pl.multiple_of(window * WIN, WIN), WIN)
                acc[rows, :] += part
            return carry

        lax.fori_loop(0, trips, body, 0)

    run(start, UNROLL, (stop - start + UNROLL - 1) // UNROLL)

    @pl.when(step == pl.num_programs(0) - 1)
    def _():
        size = outs[0].shape[0]
        for g, out in enumerate(outs):
            out[...] = acc[g * size : (g + 1) * size, :].astype(out.dtype)


def coarse_kernel(cw_ref, cells_ref, bias_ref, *refs):
    n_groups = len(step_table)
    sources = refs[: 1 + n_groups]
    outs = refs[1 + n_groups : 2 + 2 * n_groups]
    acc, coarse = refs[2 + 2 * n_groups :]
    cell_windows = acc.shape[0] // WIN
    acc[...] = jnp.zeros_like(acc)

    def pick_of(w):
        window = jnp.minimum(cw_ref[w], cell_windows - 1)
        cells = cells_ref[pl.ds(w, 1), :]
        inside = jnp.where(cells < C_DEV, cells - window * WIN, -1)
        rows = pl.ds(pl.multiple_of(window * WIN, WIN), WIN)
        return one_hot_rows(inside), rows

    base = 0
    for src in sources:
        count = src.shape[0] // WIN
        unroll = min(WIN_UNROLL, count)

        def gather_body(u, carry, src=src, base=base, unroll=unroll):
            results = []
            for t in range(unroll):
                j = u * unroll + t
                pick, rows = pick_of(base + j)
                entries = src[pl.ds(pl.multiple_of(j * WIN, WIN), WIN), :]
                results.append((rows, jnp.dot(pick, entries, preferred_element_type=jnp.float32)))
            for rows, value in results:
                acc[rows, :] += value
            return carry

        lax.fori_loop(0, count // unroll, gather_body, 0)
        base += count

    coarse[...] = jnp.maximum(acc[...] + bias_ref[...], 0.0).astype(jnp.bfloat16)

    base = 0
    for out in outs:
        count = out.shape[1] // WIN
        unroll = min(WIN_UNROLL, count)

        def scatter_body(u, carry, out=out, base=base, unroll=unroll):
            for t in range(unroll):
                j = u * unroll + t
                pick, rows = pick_of(base + j)
                chosen = lax.dot_general(coarse[rows, :], pick, TN, preferred_element_type=jnp.float32)
                out[:, pl.ds(pl.multiple_of(j * WIN, WIN), WIN)] = chosen.astype(jnp.bfloat16)
            return carry

        lax.fori_loop(0, count // unroll, scatter_body, 0)
        base += count


def up_kernel(win_ref, off_ref, xt_ref, e_ref, wt_ref, *refs):
    n_groups = len(step_table)
    sources = refs[: 1 + n_groups]
    out_ref = refs[1 + n_groups]
    stack, sems = refs[2 + n_groups :]
    step = pl.program_id(0)
    per_step = e_ref.shape[0]

    @pl.when(step == 0)
    def _():
        copies = []
        start = 0
        for index, src in enumerate(sources):
            size = src.shape[1]
            copy = pltpu.make_async_copy(src, stack.at[:, pl.ds(start, size)], sems.at[index])
            copy.start()
            copies.append(copy)
            start += size
        for copy in copies:
            copy.wait()

    def body(u, carry):
        for t in range(UP_UNROLL):
            j = u * UP_UNROLL + t
            brick = step * per_step + j
            window = win_ref[brick]
            offset = off_ref[brick]
            inside = jnp.bitwise_and(e_ref[pl.ds(j, 1), :], WIN - 1)
            pick = one_hot_rows(inside)
            parents = stack[:, pl.ds(pl.multiple_of(window * WIN, WIN), WIN)]
            rows_t = jnp.dot(parents, pick, preferred_element_type=jnp.float32).astype(jnp.bfloat16)
            lifted = jnp.dot(wt_ref[offset], rows_t, preferred_element_type=jnp.float32)
            cols = pl.ds(pl.multiple_of(j * BLK, BLK), BLK)
            out_ref[:, cols] = (xt_ref[:, cols].astype(jnp.float32) + lifted).astype(out_ref.dtype)
        return carry

    lax.fori_loop(0, per_step // UP_UNROLL, body, 0)


def group_route(g, sign):
    n_outer = lax.axis_size("outer")
    n_inner = lax.axis_size("inner")
    a, b = step_table[g]
    route = []
    for s in range(n_outer * n_inner):
        row, col = divmod(s, n_inner)
        owner = ((row + a) % n_outer) * n_inner + (col + b) % n_inner
        route.append((s, owner) if sign > 0 else (owner, s))
    return route


def local(features, block_offset, parent_entry, owner_cell, w_down, b_down, w_up):
    n_groups = len(step_table)
    fine_rows, in_width = features.shape
    out_width = w_down.shape[2]
    entries = owner_cell.shape[1]
    cap = (entries - SELF_CAP) // n_groups
    blocks = fine_rows // BLK
    steps = blocks // BRICKS_PER_STEP

    xt = features.T
    entry_rows = parent_entry.reshape(blocks, BLK)
    brick_window = entry_rows[:, 0] // WIN
    cells = owner_cell.reshape(entries // WIN, WIN)
    cell_window = jnp.min(cells, axis=1) // WIN
    w_up_t = jnp.swapaxes(w_up, 1, 2)

    part_shapes = [jax.ShapeDtypeStruct((SELF_CAP, out_width), jnp.bfloat16)] + [
        jax.ShapeDtypeStruct((cap, out_width), jnp.bfloat16)
    ] * n_groups
    answer_shapes = [jax.ShapeDtypeStruct((s.shape[1], s.shape[0]), s.dtype) for s in part_shapes]
    whole = lambda shape: pl.BlockSpec(shape, lambda *idx: (0,) * len(shape))

    is_far = (brick_window >= SELF_CAP // WIN).astype(jnp.int32).reshape(steps, BRICKS_PER_STEP)
    far_count = jnp.sum(is_far, axis=1)
    far_rank = jnp.cumsum(is_far, axis=1) - is_far
    own_rank = jnp.cumsum(1 - is_far, axis=1) - (1 - is_far)
    position = jnp.where(is_far == 1, far_rank, far_count[:, None] + own_rank)
    local_ids = jnp.arange(BRICKS_PER_STEP, dtype=jnp.int32)
    packed = (
        local_ids[None, :]
        + brick_window.reshape(steps, BRICKS_PER_STEP) * 256
        + block_offset.reshape(steps, BRICKS_PER_STEP) * 65536
    )
    order = jnp.sum(jnp.where(position[:, None, :] == local_ids[None, :, None], packed[:, None, :], 0), axis=2)
    order = order.reshape(blocks).astype(jnp.int32)
    counts = far_count.astype(jnp.int32)

    def down_call(first_window, shapes):
        rows = sum(s.shape[0] for s in shapes)
        return pl.pallas_call(
            functools.partial(down_kernel, first_window),
            out_shape=shapes,
            grid_spec=pltpu.PrefetchScalarGridSpec(
                num_scalar_prefetch=4,
                grid=(steps,),
                in_specs=[
                    pl.BlockSpec((in_width, BRICKS_PER_STEP * BLK), lambda i, *_: (0, i)),
                    pl.BlockSpec((BRICKS_PER_STEP, BLK), lambda i, *_: (i, 0)),
                    whole(w_down.shape),
                ],
                out_specs=[whole(s.shape) for s in shapes],
                scratch_shapes=[pltpu.VMEM((rows + WIN, out_width), jnp.float32)],
            ),
            compiler_params=pltpu.CompilerParams(dimension_semantics=("arbitrary",)),
            cost_estimate=pl.CostEstimate(
                flops=2 * fine_rows * in_width * out_width,
                transcendentals=0,
                bytes_accessed=fine_rows * (in_width * 2 + 4) + rows * out_width * 2,
            ),
        )(counts, order, brick_window, block_offset, xt, entry_rows, w_down)

    parts = [None] + list(down_call(SELF_CAP // WIN, part_shapes[1:]))
    parts[0] = down_call(0, part_shapes[:1])[0]

    arrived = [
        lax.ppermute(parts[1 + g], ("outer", "inner"), group_route(g, 1)) for g in range(n_groups)
    ]

    coarse = pl.pallas_call(
        coarse_kernel,
        out_shape=answer_shapes,
        grid_spec=pltpu.PrefetchScalarGridSpec(
            num_scalar_prefetch=1,
            grid=(1,),
            in_specs=[whole(cells.shape), whole((1, out_width))]
            + [whole(s.shape) for s in part_shapes],
            out_specs=[whole(s.shape) for s in answer_shapes],
            scratch_shapes=[
                pltpu.VMEM((C_DEV, out_width), jnp.float32),
                pltpu.VMEM((C_DEV, out_width), jnp.bfloat16),
            ],
        ),
        cost_estimate=pl.CostEstimate(
            flops=4 * entries * WIN * out_width,
            transcendentals=0,
            bytes_accessed=4 * entries * out_width,
        ),
    )
    answers = coarse(cell_window, cells, b_down.reshape(1, out_width), parts[0], *arrived)

    returned = [
        lax.ppermute(answers[1 + g], ("outer", "inner"), group_route(g, -1)) for g in range(n_groups)
    ]

    up = pl.pallas_call(
        up_kernel,
        out_shape=jax.ShapeDtypeStruct((in_width, fine_rows), features.dtype),
        grid_spec=pltpu.PrefetchScalarGridSpec(
            num_scalar_prefetch=2,
            grid=(steps,),
            in_specs=[
                pl.BlockSpec((in_width, BRICKS_PER_STEP * BLK), lambda i, *_: (0, i)),
                pl.BlockSpec((BRICKS_PER_STEP, BLK), lambda i, *_: (i, 0)),
                whole(w_up_t.shape),
            ]
            + [pl.BlockSpec(memory_space=pl.ANY)] * (1 + n_groups),
            out_specs=pl.BlockSpec((in_width, BRICKS_PER_STEP * BLK), lambda i, *_: (0, i)),
            scratch_shapes=[
                pltpu.VMEM((out_width, entries), jnp.bfloat16),
                pltpu.SemaphoreType.DMA((1 + n_groups,)),
            ],
        ),
        compiler_params=pltpu.CompilerParams(dimension_semantics=("arbitrary",)),
        cost_estimate=pl.CostEstimate(
            flops=6 * fine_rows * in_width * out_width,
            transcendentals=0,
            bytes_accessed=fine_rows * (in_width * 4 + 4) + entries * out_width * 2,
        ),
    )
    out_t = up(brick_window, block_offset, xt, entry_rows, w_up_t, answers[0], *returned)
    return out_t.T


def solution(mesh):
    in_specs = (
        P(("outer", "inner"), None),
        P(("outer", "inner")),
        P(("outer", "inner")),
        P(("outer", "inner"), None),
        P(),
        P(),
        P(),
    )
    out_specs = P(("outer", "inner"), None)
    return jax.shard_map(local, mesh=mesh, in_specs=in_specs, out_specs=out_specs, check_vma=False)
```

```python
import functools

import jax
import jax.numpy as jnp
from jax import lax
from jax.experimental import pallas as pl
from jax.experimental.pallas import tpu as pltpu
from jax.sharding import PartitionSpec as P

BLK = 128
C_DEV = 4096
SELF_CAP = 4096
WIN = 128
BRICKS_PER_STEP = 128
UNROLL = 16
UP_UNROLL = 32
WIN_UNROLL = 16

step_table = ((-1, -1), (-1, 0), (-1, 1), (0, -1), (0, 1), (1, -1), (1, 0), (1, 1))

NT = (((1,), (1,)), ((), ()))
TN = (((0,), (0,)), ((), ()))


def split_parts(data):
    high = data.astype(jnp.bfloat16)
    low = (data - high.astype(jnp.float32)).astype(jnp.bfloat16)
    return high, low


def one_hot_rows(index_row):
    span = lax.broadcasted_iota(jnp.int32, (WIN, index_row.shape[1]), 0)
    return (span == index_row).astype(jnp.bfloat16)


def down_kernel(first_window, count_ref, order_ref, win_ref, off_ref, xt_ref, e_ref, w_ref, *refs):
    outs = refs[:-1]
    acc = refs[-1]
    step = pl.program_id(0)
    per_step = e_ref.shape[0]
    trash = acc.shape[0] // WIN - 1

    @pl.when(step == 0)
    def _():
        acc[...] = jnp.zeros_like(acc)

    neighbours = count_ref[step]
    if first_window == 0:
        start, stop = neighbours, per_step
    else:
        start, stop = 0, neighbours

    def run(first, width, trips):
        def body(u, carry):
            results = []
            for t in range(width):
                position = first + u * width + t
                j = order_ref[step * per_step + jnp.minimum(position, per_step - 1)]
                brick = step * per_step + j
                window = jnp.where(position < stop, win_ref[brick] - first_window, trash)
                offset = off_ref[brick]
                inside = jnp.bitwise_and(e_ref[pl.ds(j, 1), :], WIN - 1)
                pick = one_hot_rows(inside)
                cols = pl.ds(pl.multiple_of(j * BLK, BLK), BLK)
                summed = lax.dot_general(pick, xt_ref[:, cols], NT, preferred_element_type=jnp.float32)
                part = jnp.dot(summed.astype(jnp.bfloat16), w_ref[offset], preferred_element_type=jnp.float32)
                results.append((window, part))
            for window, part in results:
                rows = pl.ds(pl.multiple_of(window * WIN, WIN), WIN)
                acc[rows, :] += part
            return carry

        lax.fori_loop(0, trips, body, 0)

    run(start, UNROLL, (stop - start + UNROLL - 1) // UNROLL)

    @pl.when(step == pl.num_programs(0) - 1)
    def _():
        size = outs[0].shape[0]
        for g, out in enumerate(outs):
            out[...] = acc[g * size : (g + 1) * size, :].astype(out.dtype)


def coarse_kernel(cw_ref, cells_ref, bias_ref, *refs):
    n_groups = len(step_table)
    sources = refs[: 1 + n_groups]
    outs = refs[1 + n_groups : 2 + 2 * n_groups]
    acc, coarse = refs[2 + 2 * n_groups :]
    cell_windows = acc.shape[0] // WIN
    acc[...] = jnp.zeros_like(acc)

    def pick_of(w):
        window = jnp.minimum(cw_ref[w], cell_windows - 1)
        cells = cells_ref[pl.ds(w, 1), :]
        inside = jnp.where(cells < C_DEV, cells - window * WIN, -1)
        rows = pl.ds(pl.multiple_of(window * WIN, WIN), WIN)
        return one_hot_rows(inside), rows

    base = 0
    for src in sources:
        count = src.shape[0] // WIN
        unroll = min(WIN_UNROLL, count)

        def gather_body(u, carry, src=src, base=base, unroll=unroll):
            results = []
            for t in range(unroll):
                j = u * unroll + t
                pick, rows = pick_of(base + j)
                entries = src[pl.ds(pl.multiple_of(j * WIN, WIN), WIN), :]
                results.append((rows, jnp.dot(pick, entries, preferred_element_type=jnp.float32)))
            for rows, value in results:
                acc[rows, :] += value
            return carry

        lax.fori_loop(0, count // unroll, gather_body, 0)
        base += count

    coarse[...] = jnp.maximum(acc[...] + bias_ref[...], 0.0).astype(jnp.bfloat16)

    base = 0
    for out in outs:
        count = out.shape[1] // WIN
        unroll = min(WIN_UNROLL, count)

        def scatter_body(u, carry, out=out, base=base, unroll=unroll):
            for t in range(unroll):
                j = u * unroll + t
                pick, rows = pick_of(base + j)
                chosen = lax.dot_general(coarse[rows, :], pick, TN, preferred_element_type=jnp.float32)
                out[:, pl.ds(pl.multiple_of(j * WIN, WIN), WIN)] = chosen.astype(jnp.bfloat16)
            return carry

        lax.fori_loop(0, count // unroll, scatter_body, 0)
        base += count


def up_kernel(win_ref, off_ref, xt_ref, e_ref, wt_ref, *refs):
    n_groups = len(step_table)
    sources = refs[: 1 + n_groups]
    out_ref = refs[1 + n_groups]
    stack, sems = refs[2 + n_groups :]
    step = pl.program_id(0)
    per_step = e_ref.shape[0]

    @pl.when(step == 0)
    def _():
        copies = []
        start = 0
        for index, src in enumerate(sources):
            size = src.shape[1]
            copy = pltpu.make_async_copy(src, stack.at[:, pl.ds(start, size)], sems.at[index])
            copy.start()
            copies.append(copy)
            start += size
        for copy in copies:
            copy.wait()

    def body(u, carry):
        for t in range(UP_UNROLL):
            j = u * UP_UNROLL + t
            brick = step * per_step + j
            window = win_ref[brick]
            offset = off_ref[brick]
            inside = jnp.bitwise_and(e_ref[pl.ds(j, 1), :], WIN - 1)
            pick = one_hot_rows(inside)
            parents = stack[:, pl.ds(pl.multiple_of(window * WIN, WIN), WIN)]
            rows_t = jnp.dot(parents, pick, preferred_element_type=jnp.float32).astype(jnp.bfloat16)
            lifted = jnp.dot(wt_ref[offset], rows_t, preferred_element_type=jnp.float32)
            cols = pl.ds(pl.multiple_of(j * BLK, BLK), BLK)
            out_ref[:, cols] = (xt_ref[:, cols].astype(jnp.float32) + lifted).astype(out_ref.dtype)
        return carry

    lax.fori_loop(0, per_step // UP_UNROLL, body, 0)


def group_route(g, sign):
    n_outer = lax.axis_size("outer")
    n_inner = lax.axis_size("inner")
    a, b = step_table[g]
    route = []
    for s in range(n_outer * n_inner):
        row, col = divmod(s, n_inner)
        owner = ((row + a) % n_outer) * n_inner + (col + b) % n_inner
        route.append((s, owner) if sign > 0 else (owner, s))
    return route


def local(features, block_offset, parent_entry, owner_cell, w_down, b_down, w_up):
    n_groups = len(step_table)
    fine_rows, in_width = features.shape
    out_width = w_down.shape[2]
    entries = owner_cell.shape[1]
    cap = (entries - SELF_CAP) // n_groups
    blocks = fine_rows // BLK
    steps = blocks // BRICKS_PER_STEP

    xt = features.T
    entry_rows = parent_entry.reshape(blocks, BLK)
    brick_window = entry_rows[:, 0] // WIN
    cells = owner_cell.reshape(entries // WIN, WIN)
    cell_window = jnp.min(cells, axis=1) // WIN
    w_up_t = jnp.swapaxes(w_up, 1, 2)

    part_shapes = [jax.ShapeDtypeStruct((SELF_CAP, out_width), jnp.bfloat16)] + [
        jax.ShapeDtypeStruct((cap, out_width), jnp.bfloat16)
    ] * n_groups
    answer_shapes = [jax.ShapeDtypeStruct((s.shape[1], s.shape[0]), s.dtype) for s in part_shapes]
    whole = lambda shape: pl.BlockSpec(shape, lambda *idx: (0,) * len(shape))

    is_far = (brick_window >= SELF_CAP // WIN).astype(jnp.int32).reshape(steps, BRICKS_PER_STEP)
    far_count = jnp.sum(is_far, axis=1)
    far_rank = jnp.cumsum(is_far, axis=1) - is_far
    own_rank = jnp.cumsum(1 - is_far, axis=1) - (1 - is_far)
    position = jnp.where(is_far == 1, far_rank, far_count[:, None] + own_rank)
    local_ids = jnp.arange(BRICKS_PER_STEP, dtype=jnp.int32)
    order = jnp.sum(
        jnp.where(position[:, None, :] == local_ids[None, :, None], local_ids[None, None, :], 0), axis=2
    )
    order = order.reshape(blocks).astype(jnp.int32)
    counts = far_count.astype(jnp.int32)

    def down_call(first_window, shapes):
        rows = sum(s.shape[0] for s in shapes)
        return pl.pallas_call(
            functools.partial(down_kernel, first_window),
            out_shape=shapes,
            grid_spec=pltpu.PrefetchScalarGridSpec(
                num_scalar_prefetch=4,
                grid=(steps,),
                in_specs=[
                    pl.BlockSpec((in_width, BRICKS_PER_STEP * BLK), lambda i, *_: (0, i)),
                    pl.BlockSpec((BRICKS_PER_STEP, BLK), lambda i, *_: (i, 0)),
                    whole(w_down.shape),
                ],
                out_specs=[whole(s.shape) for s in shapes],
                scratch_shapes=[pltpu.VMEM((rows + WIN, out_width), jnp.float32)],
            ),
            compiler_params=pltpu.CompilerParams(dimension_semantics=("arbitrary",)),
            cost_estimate=pl.CostEstimate(
                flops=2 * fine_rows * in_width * out_width,
                transcendentals=0,
                bytes_accessed=fine_rows * (in_width * 2 + 4) + rows * out_width * 2,
            ),
        )(counts, order, brick_window, block_offset, xt, entry_rows, w_down)

    parts = [None] + list(down_call(SELF_CAP // WIN, part_shapes[1:]))
    parts[0] = down_call(0, part_shapes[:1])[0]

    arrived = [
        lax.ppermute(parts[1 + g], ("outer", "inner"), group_route(g, 1)) for g in range(n_groups)
    ]

    coarse = pl.pallas_call(
        coarse_kernel,
        out_shape=answer_shapes,
        grid_spec=pltpu.PrefetchScalarGridSpec(
            num_scalar_prefetch=1,
            grid=(1,),
            in_specs=[whole(cells.shape), whole((1, out_width))]
            + [whole(s.shape) for s in part_shapes],
            out_specs=[whole(s.shape) for s in answer_shapes],
            scratch_shapes=[
                pltpu.VMEM((C_DEV, out_width), jnp.float32),
                pltpu.VMEM((C_DEV, out_width), jnp.bfloat16),
            ],
        ),
        cost_estimate=pl.CostEstimate(
            flops=4 * entries * WIN * out_width,
            transcendentals=0,
            bytes_accessed=4 * entries * out_width,
        ),
    )
    answers = coarse(cell_window, cells, b_down.reshape(1, out_width), parts[0], *arrived)

    returned = [
        lax.ppermute(answers[1 + g], ("outer", "inner"), group_route(g, -1)) for g in range(n_groups)
    ]

    up = pl.pallas_call(
        up_kernel,
        out_shape=jax.ShapeDtypeStruct((in_width, fine_rows), features.dtype),
        grid_spec=pltpu.PrefetchScalarGridSpec(
            num_scalar_prefetch=2,
            grid=(steps,),
            in_specs=[
                pl.BlockSpec((in_width, BRICKS_PER_STEP * BLK), lambda i, *_: (0, i)),
                pl.BlockSpec((BRICKS_PER_STEP, BLK), lambda i, *_: (i, 0)),
                whole(w_up_t.shape),
            ]
            + [pl.BlockSpec(memory_space=pl.ANY)] * (1 + n_groups),
            out_specs=pl.BlockSpec((in_width, BRICKS_PER_STEP * BLK), lambda i, *_: (0, i)),
            scratch_shapes=[
                pltpu.VMEM((out_width, entries), jnp.bfloat16),
                pltpu.SemaphoreType.DMA((1 + n_groups,)),
            ],
        ),
        compiler_params=pltpu.CompilerParams(dimension_semantics=("arbitrary",)),
        cost_estimate=pl.CostEstimate(
            flops=6 * fine_rows * in_width * out_width,
            transcendentals=0,
            bytes_accessed=fine_rows * (in_width * 4 + 4) + entries * out_width * 2,
        ),
    )
    out_t = up(brick_window, block_offset, xt, entry_rows, w_up_t, answers[0], *returned)
    return out_t.T


def solution(mesh):
    in_specs = (
        P(("outer", "inner"), None),
        P(("outer", "inner")),
        P(("outer", "inner")),
        P(("outer", "inner"), None),
        P(),
        P(),
        P(),
    )
    out_specs = P(("outer", "inner"), None)
    return jax.shard_map(local, mesh=mesh, in_specs=in_specs, out_specs=out_specs, check_vma=False)
```

```python
import functools

import jax
import jax.numpy as jnp
from jax import lax
from jax.experimental import pallas as pl
from jax.experimental.pallas import tpu as pltpu
from jax.sharding import PartitionSpec as P

BLK = 128
C_DEV = 4096
SELF_CAP = 4096
WIN = 128
BRICKS_PER_STEP = 64
UNROLL = 16
UP_UNROLL = 64
WIN_UNROLL = 32

step_table = ((-1, -1), (-1, 0), (-1, 1), (0, -1), (0, 1), (1, -1), (1, 0), (1, 1))

NT = (((1,), (1,)), ((), ()))
TN = (((0,), (0,)), ((), ()))


def split_parts(data):
    high = data.astype(jnp.bfloat16)
    low = (data - high.astype(jnp.float32)).astype(jnp.bfloat16)
    return high, low


def one_hot_rows(index_row):
    span = lax.broadcasted_iota(jnp.int32, (WIN, index_row.shape[1]), 0)
    return (span == index_row).astype(jnp.bfloat16)


def down_kernel(first_window, count_ref, order_ref, win_ref, off_ref, xt_ref, e_ref, w_ref, *refs):
    outs = refs[:-1]
    acc = refs[-1]
    step = pl.program_id(0)
    per_step = e_ref.shape[0]
    trash = acc.shape[0] // WIN - 1

    @pl.when(step == 0)
    def _():
        acc[...] = jnp.zeros_like(acc)

    neighbours = count_ref[step]
    if first_window == 0:
        start, stop = neighbours, per_step
    else:
        start, stop = 0, neighbours

    def run(first, width, trips):
        def body(u, carry):
            results = []
            for t in range(width):
                position = first + u * width + t
                j = order_ref[step * per_step + jnp.minimum(position, per_step - 1)]
                brick = step * per_step + j
                window = jnp.where(position < stop, win_ref[brick] - first_window, trash)
                offset = off_ref[brick]
                inside = jnp.bitwise_and(e_ref[pl.ds(j, 1), :], WIN - 1)
                pick = one_hot_rows(inside)
                cols = pl.ds(pl.multiple_of(j * BLK, BLK), BLK)
                summed = lax.dot_general(pick, xt_ref[:, cols], NT, preferred_element_type=jnp.float32)
                part = jnp.dot(summed.astype(jnp.bfloat16), w_ref[offset], preferred_element_type=jnp.float32)
                results.append((window, part))
            for window, part in results:
                rows = pl.ds(pl.multiple_of(window * WIN, WIN), WIN)
                acc[rows, :] += part
            return carry

        lax.fori_loop(0, trips, body, 0)

    run(start, UNROLL, (stop - start + UNROLL - 1) // UNROLL)

    @pl.when(step == pl.num_programs(0) - 1)
    def _():
        size = outs[0].shape[0]
        for g, out in enumerate(outs):
            out[...] = acc[g * size : (g + 1) * size, :].astype(out.dtype)


def coarse_kernel(cw_ref, cells_ref, bias_ref, *refs):
    n_groups = len(step_table)
    sources = refs[: 1 + n_groups]
    outs = refs[1 + n_groups : 2 + 2 * n_groups]
    acc, coarse = refs[2 + 2 * n_groups :]
    cell_windows = acc.shape[0] // WIN
    acc[...] = jnp.zeros_like(acc)

    def pick_of(w):
        window = jnp.minimum(cw_ref[w], cell_windows - 1)
        cells = cells_ref[pl.ds(w, 1), :]
        inside = jnp.where(cells < C_DEV, cells - window * WIN, -1)
        rows = pl.ds(pl.multiple_of(window * WIN, WIN), WIN)
        return one_hot_rows(inside), rows

    base = 0
    for src in sources:
        count = src.shape[0] // WIN
        unroll = min(WIN_UNROLL, count)

        def gather_body(u, carry, src=src, base=base, unroll=unroll):
            results = []
            for t in range(unroll):
                j = u * unroll + t
                pick, rows = pick_of(base + j)
                entries = src[pl.ds(pl.multiple_of(j * WIN, WIN), WIN), :]
                results.append((rows, jnp.dot(pick, entries, preferred_element_type=jnp.float32)))
            for rows, value in results:
                acc[rows, :] += value
            return carry

        lax.fori_loop(0, count // unroll, gather_body, 0)
        base += count

    coarse[...] = jnp.maximum(acc[...] + bias_ref[...], 0.0).astype(jnp.bfloat16)

    base = 0
    for out in outs:
        count = out.shape[1] // WIN
        unroll = min(WIN_UNROLL, count)

        def scatter_body(u, carry, out=out, base=base, unroll=unroll):
            for t in range(unroll):
                j = u * unroll + t
                pick, rows = pick_of(base + j)
                chosen = lax.dot_general(coarse[rows, :], pick, TN, preferred_element_type=jnp.float32)
                out[:, pl.ds(pl.multiple_of(j * WIN, WIN), WIN)] = chosen.astype(jnp.bfloat16)
            return carry

        lax.fori_loop(0, count // unroll, scatter_body, 0)
        base += count


def up_kernel(win_ref, off_ref, xt_ref, e_ref, wt_ref, *refs):
    n_groups = len(step_table)
    sources = refs[: 1 + n_groups]
    out_ref = refs[1 + n_groups]
    stack, sems = refs[2 + n_groups :]
    step = pl.program_id(0)
    per_step = e_ref.shape[0]

    @pl.when(step == 0)
    def _():
        copies = []
        start = 0
        for index, src in enumerate(sources):
            size = src.shape[1]
            copy = pltpu.make_async_copy(src, stack.at[:, pl.ds(start, size)], sems.at[index])
            copy.start()
            copies.append(copy)
            start += size
        for copy in copies:
            copy.wait()

    def body(u, carry):
        for t in range(UP_UNROLL):
            j = u * UP_UNROLL + t
            brick = step * per_step + j
            window = win_ref[brick]
            offset = off_ref[brick]
            inside = jnp.bitwise_and(e_ref[pl.ds(j, 1), :], WIN - 1)
            pick = one_hot_rows(inside)
            parents = stack[:, pl.ds(pl.multiple_of(window * WIN, WIN), WIN)]
            rows_t = jnp.dot(parents, pick, preferred_element_type=jnp.float32).astype(jnp.bfloat16)
            lifted = jnp.dot(wt_ref[offset], rows_t, preferred_element_type=jnp.float32)
            cols = pl.ds(pl.multiple_of(j * BLK, BLK), BLK)
            out_ref[:, cols] = (xt_ref[:, cols].astype(jnp.float32) + lifted).astype(out_ref.dtype)
        return carry

    lax.fori_loop(0, per_step // UP_UNROLL, body, 0)


def group_route(g, sign):
    n_outer = lax.axis_size("outer")
    n_inner = lax.axis_size("inner")
    a, b = step_table[g]
    route = []
    for s in range(n_outer * n_inner):
        row, col = divmod(s, n_inner)
        owner = ((row + a) % n_outer) * n_inner + (col + b) % n_inner
        route.append((s, owner) if sign > 0 else (owner, s))
    return route


def local(features, block_offset, parent_entry, owner_cell, w_down, b_down, w_up):
    n_groups = len(step_table)
    fine_rows, in_width = features.shape
    out_width = w_down.shape[2]
    entries = owner_cell.shape[1]
    cap = (entries - SELF_CAP) // n_groups
    blocks = fine_rows // BLK
    steps = blocks // BRICKS_PER_STEP

    xt = features.T
    entry_rows = parent_entry.reshape(blocks, BLK)
    brick_window = entry_rows[:, 0] // WIN
    cells = owner_cell.reshape(entries // WIN, WIN)
    cell_window = jnp.min(cells, axis=1) // WIN
    w_up_t = jnp.swapaxes(w_up, 1, 2)

    part_shapes = [jax.ShapeDtypeStruct((SELF_CAP, out_width), jnp.bfloat16)] + [
        jax.ShapeDtypeStruct((cap, out_width), jnp.bfloat16)
    ] * n_groups
    answer_shapes = [jax.ShapeDtypeStruct((s.shape[1], s.shape[0]), s.dtype) for s in part_shapes]
    whole = lambda shape: pl.BlockSpec(shape, lambda *idx: (0,) * len(shape))

    is_far = (brick_window >= SELF_CAP // WIN).astype(jnp.int32).reshape(steps, BRICKS_PER_STEP)
    far_count = jnp.sum(is_far, axis=1)
    far_rank = jnp.cumsum(is_far, axis=1) - is_far
    own_rank = jnp.cumsum(1 - is_far, axis=1) - (1 - is_far)
    position = jnp.where(is_far == 1, far_rank, far_count[:, None] + own_rank)
    local_ids = jnp.arange(BRICKS_PER_STEP, dtype=jnp.int32)
    order = jnp.sum(
        jnp.where(position[:, None, :] == local_ids[None, :, None], local_ids[None, None, :], 0), axis=2
    )
    order = order.reshape(blocks).astype(jnp.int32)
    counts = far_count.astype(jnp.int32)

    def down_call(first_window, shapes):
        rows = sum(s.shape[0] for s in shapes)
        return pl.pallas_call(
            functools.partial(down_kernel, first_window),
            out_shape=shapes,
            grid_spec=pltpu.PrefetchScalarGridSpec(
                num_scalar_prefetch=4,
                grid=(steps,),
                in_specs=[
                    pl.BlockSpec((in_width, BRICKS_PER_STEP * BLK), lambda i, *_: (0, i)),
                    pl.BlockSpec((BRICKS_PER_STEP, BLK), lambda i, *_: (i, 0)),
                    whole(w_down.shape),
                ],
                out_specs=[whole(s.shape) for s in shapes],
                scratch_shapes=[pltpu.VMEM((rows + WIN, out_width), jnp.float32)],
            ),
            compiler_params=pltpu.CompilerParams(dimension_semantics=("arbitrary",)),
            cost_estimate=pl.CostEstimate(
                flops=2 * fine_rows * in_width * out_width,
                transcendentals=0,
                bytes_accessed=fine_rows * (in_width * 2 + 4) + rows * out_width * 2,
            ),
        )(counts, order, brick_window, block_offset, xt, entry_rows, w_down)

    parts = [None] + list(down_call(SELF_CAP // WIN, part_shapes[1:]))
    parts[0] = down_call(0, part_shapes[:1])[0]

    arrived = [
        lax.ppermute(parts[1 + g], ("outer", "inner"), group_route(g, 1)) for g in range(n_groups)
    ]

    coarse = pl.pallas_call(
        coarse_kernel,
        out_shape=answer_shapes,
        grid_spec=pltpu.PrefetchScalarGridSpec(
            num_scalar_prefetch=1,
            grid=(1,),
            in_specs=[whole(cells.shape), whole((1, out_width))]
            + [whole(s.shape) for s in part_shapes],
            out_specs=[whole(s.shape) for s in answer_shapes],
            scratch_shapes=[
                pltpu.VMEM((C_DEV, out_width), jnp.float32),
                pltpu.VMEM((C_DEV, out_width), jnp.bfloat16),
            ],
        ),
        cost_estimate=pl.CostEstimate(
            flops=4 * entries * WIN * out_width,
            transcendentals=0,
            bytes_accessed=4 * entries * out_width,
        ),
    )
    answers = coarse(cell_window, cells, b_down.reshape(1, out_width), parts[0], *arrived)

    returned = [
        lax.ppermute(answers[1 + g], ("outer", "inner"), group_route(g, -1)) for g in range(n_groups)
    ]

    up = pl.pallas_call(
        up_kernel,
        out_shape=jax.ShapeDtypeStruct((in_width, fine_rows), features.dtype),
        grid_spec=pltpu.PrefetchScalarGridSpec(
            num_scalar_prefetch=2,
            grid=(steps,),
            in_specs=[
                pl.BlockSpec((in_width, BRICKS_PER_STEP * BLK), lambda i, *_: (0, i)),
                pl.BlockSpec((BRICKS_PER_STEP, BLK), lambda i, *_: (i, 0)),
                whole(w_up_t.shape),
            ]
            + [pl.BlockSpec(memory_space=pl.ANY)] * (1 + n_groups),
            out_specs=pl.BlockSpec((in_width, BRICKS_PER_STEP * BLK), lambda i, *_: (0, i)),
            scratch_shapes=[
                pltpu.VMEM((out_width, entries), jnp.bfloat16),
                pltpu.SemaphoreType.DMA((1 + n_groups,)),
            ],
        ),
        compiler_params=pltpu.CompilerParams(dimension_semantics=("arbitrary",)),
        cost_estimate=pl.CostEstimate(
            flops=6 * fine_rows * in_width * out_width,
            transcendentals=0,
            bytes_accessed=fine_rows * (in_width * 4 + 4) + entries * out_width * 2,
        ),
    )
    out_t = up(brick_window, block_offset, xt, entry_rows, w_up_t, answers[0], *returned)
    return out_t.T


def solution(mesh):
    in_specs = (
        P(("outer", "inner"), None),
        P(("outer", "inner")),
        P(("outer", "inner")),
        P(("outer", "inner"), None),
        P(),
        P(),
        P(),
    )
    out_specs = P(("outer", "inner"), None)
    return jax.shard_map(local, mesh=mesh, in_specs=in_specs, out_specs=out_specs, check_vma=False)
```

```python
import functools

import jax
import jax.numpy as jnp
from jax import lax
from jax.experimental import pallas as pl
from jax.experimental.pallas import tpu as pltpu
from jax.sharding import PartitionSpec as P

BLK = 128
C_DEV = 4096
SELF_CAP = 4096
WIN = 128
BRICKS_PER_STEP = 64
UNROLL = 16
UP_UNROLL = 128
WIN_UNROLL = 32

step_table = ((-1, -1), (-1, 0), (-1, 1), (0, -1), (0, 1), (1, -1), (1, 0), (1, 1))

NT = (((1,), (1,)), ((), ()))
TN = (((0,), (0,)), ((), ()))


def split_parts(data):
    high = data.astype(jnp.bfloat16)
    low = (data - high.astype(jnp.float32)).astype(jnp.bfloat16)
    return high, low


def one_hot_rows(index_row):
    span = lax.broadcasted_iota(jnp.int32, (WIN, index_row.shape[1]), 0)
    return (span == index_row).astype(jnp.bfloat16)


def down_kernel(first_window, count_ref, order_ref, win_ref, off_ref, xt_ref, e_ref, w_ref, *refs):
    outs = refs[:-1]
    acc = refs[-1]
    step = pl.program_id(0)
    per_step = e_ref.shape[0]
    trash = acc.shape[0] // WIN - 1

    @pl.when(step == 0)
    def _():
        acc[...] = jnp.zeros_like(acc)

    neighbours = count_ref[step]
    if first_window == 0:
        start, stop = neighbours, per_step
    else:
        start, stop = 0, neighbours

    def run(first, width, trips):
        def body(u, carry):
            results = []
            for t in range(width):
                position = first + u * width + t
                j = order_ref[step * per_step + jnp.minimum(position, per_step - 1)]
                brick = step * per_step + j
                window = jnp.where(position < stop, win_ref[brick] - first_window, trash)
                offset = off_ref[brick]
                inside = jnp.bitwise_and(e_ref[pl.ds(j, 1), :], WIN - 1)
                pick = one_hot_rows(inside)
                cols = pl.ds(pl.multiple_of(j * BLK, BLK), BLK)
                summed = lax.dot_general(pick, xt_ref[:, cols], NT, preferred_element_type=jnp.float32)
                part = jnp.dot(summed.astype(jnp.bfloat16), w_ref[offset], preferred_element_type=jnp.float32)
                results.append((window, part))
            for window, part in results:
                rows = pl.ds(pl.multiple_of(window * WIN, WIN), WIN)
                acc[rows, :] += part
            return carry

        lax.fori_loop(0, trips, body, 0)

    run(start, UNROLL, (stop - start + UNROLL - 1) // UNROLL)

    @pl.when(step == pl.num_programs(0) - 1)
    def _():
        size = outs[0].shape[0]
        for g, out in enumerate(outs):
            out[...] = acc[g * size : (g + 1) * size, :].astype(out.dtype)


def coarse_kernel(cw_ref, cells_ref, bias_ref, *refs):
    n_groups = len(step_table)
    sources = refs[: 1 + n_groups]
    outs = refs[1 + n_groups : 2 + 2 * n_groups]
    acc, coarse = refs[2 + 2 * n_groups :]
    cell_windows = acc.shape[0] // WIN
    acc[...] = jnp.zeros_like(acc)

    def pick_of(w):
        window = jnp.minimum(cw_ref[w], cell_windows - 1)
        cells = cells_ref[pl.ds(w, 1), :]
        inside = jnp.where(cells < C_DEV, cells - window * WIN, -1)
        rows = pl.ds(pl.multiple_of(window * WIN, WIN), WIN)
        return one_hot_rows(inside), rows

    base = 0
    for src in sources:
        count = src.shape[0] // WIN
        unroll = min(WIN_UNROLL, count)

        def gather_body(u, carry, src=src, base=base, unroll=unroll):
            results = []
            for t in range(unroll):
                j = u * unroll + t
                pick, rows = pick_of(base + j)
                entries = src[pl.ds(pl.multiple_of(j * WIN, WIN), WIN), :]
                results.append((rows, jnp.dot(pick, entries, preferred_element_type=jnp.float32)))
            for rows, value in results:
                acc[rows, :] += value
            return carry

        lax.fori_loop(0, count // unroll, gather_body, 0)
        base += count

    coarse[...] = jnp.maximum(acc[...] + bias_ref[...], 0.0).astype(jnp.bfloat16)

    base = 0
    for out in outs:
        count = out.shape[1] // WIN
        unroll = min(WIN_UNROLL, count)

        def scatter_body(u, carry, out=out, base=base, unroll=unroll):
            for t in range(unroll):
                j = u * unroll + t
                pick, rows = pick_of(base + j)
                chosen = lax.dot_general(coarse[rows, :], pick, TN, preferred_element_type=jnp.float32)
                out[:, pl.ds(pl.multiple_of(j * WIN, WIN), WIN)] = chosen.astype(jnp.bfloat16)
            return carry

        lax.fori_loop(0, count // unroll, scatter_body, 0)
        base += count


def up_kernel(win_ref, off_ref, xt_ref, e_ref, wt_ref, *refs):
    n_groups = len(step_table)
    sources = refs[: 1 + n_groups]
    out_ref = refs[1 + n_groups]
    stack, sems = refs[2 + n_groups :]
    step = pl.program_id(0)
    per_step = e_ref.shape[0]

    @pl.when(step == 0)
    def _():
        copies = []
        start = 0
        for index, src in enumerate(sources):
            size = src.shape[1]
            copy = pltpu.make_async_copy(src, stack.at[:, pl.ds(start, size)], sems.at[index])
            copy.start()
            copies.append(copy)
            start += size
        for copy in copies:
            copy.wait()

    def body(u, carry):
        for t in range(UP_UNROLL):
            j = u * UP_UNROLL + t
            brick = step * per_step + j
            window = win_ref[brick]
            offset = off_ref[brick]
            inside = jnp.bitwise_and(e_ref[pl.ds(j, 1), :], WIN - 1)
            pick = one_hot_rows(inside)
            parents = stack[:, pl.ds(pl.multiple_of(window * WIN, WIN), WIN)]
            rows_t = jnp.dot(parents, pick, preferred_element_type=jnp.float32).astype(jnp.bfloat16)
            lifted = jnp.dot(wt_ref[offset], rows_t, preferred_element_type=jnp.float32)
            cols = pl.ds(pl.multiple_of(j * BLK, BLK), BLK)
            out_ref[:, cols] = (xt_ref[:, cols].astype(jnp.float32) + lifted).astype(out_ref.dtype)
        return carry

    lax.fori_loop(0, per_step // UP_UNROLL, body, 0)


def group_route(g, sign):
    n_outer = lax.axis_size("outer")
    n_inner = lax.axis_size("inner")
    a, b = step_table[g]
    route = []
    for s in range(n_outer * n_inner):
        row, col = divmod(s, n_inner)
        owner = ((row + a) % n_outer) * n_inner + (col + b) % n_inner
        route.append((s, owner) if sign > 0 else (owner, s))
    return route


def local(features, block_offset, parent_entry, owner_cell, w_down, b_down, w_up):
    n_groups = len(step_table)
    fine_rows, in_width = features.shape
    out_width = w_down.shape[2]
    entries = owner_cell.shape[1]
    cap = (entries - SELF_CAP) // n_groups
    blocks = fine_rows // BLK
    steps = blocks // BRICKS_PER_STEP

    xt = features.T
    entry_rows = parent_entry.reshape(blocks, BLK)
    brick_window = entry_rows[:, 0] // WIN
    cells = owner_cell.reshape(entries // WIN, WIN)
    cell_window = jnp.min(cells, axis=1) // WIN
    w_up_t = jnp.swapaxes(w_up, 1, 2)

    part_shapes = [jax.ShapeDtypeStruct((SELF_CAP, out_width), jnp.bfloat16)] + [
        jax.ShapeDtypeStruct((cap, out_width), jnp.bfloat16)
    ] * n_groups
    answer_shapes = [jax.ShapeDtypeStruct((s.shape[1], s.shape[0]), s.dtype) for s in part_shapes]
    whole = lambda shape: pl.BlockSpec(shape, lambda *idx: (0,) * len(shape))

    is_far = (brick_window >= SELF_CAP // WIN).astype(jnp.int32).reshape(steps, BRICKS_PER_STEP)
    far_count = jnp.sum(is_far, axis=1)
    far_rank = jnp.cumsum(is_far, axis=1) - is_far
    own_rank = jnp.cumsum(1 - is_far, axis=1) - (1 - is_far)
    position = jnp.where(is_far == 1, far_rank, far_count[:, None] + own_rank)
    local_ids = jnp.arange(BRICKS_PER_STEP, dtype=jnp.int32)
    order = jnp.sum(
        jnp.where(position[:, None, :] == local_ids[None, :, None], local_ids[None, None, :], 0), axis=2
    )
    order = order.reshape(blocks).astype(jnp.int32)
    counts = far_count.astype(jnp.int32)

    def down_call(first_window, shapes):
        rows = sum(s.shape[0] for s in shapes)
        return pl.pallas_call(
            functools.partial(down_kernel, first_window),
            out_shape=shapes,
            grid_spec=pltpu.PrefetchScalarGridSpec(
                num_scalar_prefetch=4,
                grid=(steps,),
                in_specs=[
                    pl.BlockSpec((in_width, BRICKS_PER_STEP * BLK), lambda i, *_: (0, i)),
                    pl.BlockSpec((BRICKS_PER_STEP, BLK), lambda i, *_: (i, 0)),
                    whole(w_down.shape),
                ],
                out_specs=[whole(s.shape) for s in shapes],
                scratch_shapes=[pltpu.VMEM((rows + WIN, out_width), jnp.float32)],
            ),
            compiler_params=pltpu.CompilerParams(dimension_semantics=("arbitrary",)),
            cost_estimate=pl.CostEstimate(
                flops=2 * fine_rows * in_width * out_width,
                transcendentals=0,
                bytes_accessed=fine_rows * (in_width * 2 + 4) + rows * out_width * 2,
            ),
        )(counts, order, brick_window, block_offset, xt, entry_rows, w_down)

    parts = [None] + list(down_call(SELF_CAP // WIN, part_shapes[1:]))
    parts[0] = down_call(0, part_shapes[:1])[0]

    arrived = [
        lax.ppermute(parts[1 + g], ("outer", "inner"), group_route(g, 1)) for g in range(n_groups)
    ]

    coarse = pl.pallas_call(
        coarse_kernel,
        out_shape=answer_shapes,
        grid_spec=pltpu.PrefetchScalarGridSpec(
            num_scalar_prefetch=1,
            grid=(1,),
            in_specs=[whole(cells.shape), whole((1, out_width))]
            + [whole(s.shape) for s in part_shapes],
            out_specs=[whole(s.shape) for s in answer_shapes],
            scratch_shapes=[
                pltpu.VMEM((C_DEV, out_width), jnp.float32),
                pltpu.VMEM((C_DEV, out_width), jnp.bfloat16),
            ],
        ),
        cost_estimate=pl.CostEstimate(
            flops=4 * entries * WIN * out_width,
            transcendentals=0,
            bytes_accessed=4 * entries * out_width,
        ),
    )
    answers = coarse(cell_window, cells, b_down.reshape(1, out_width), parts[0], *arrived)

    returned = [
        lax.ppermute(answers[1 + g], ("outer", "inner"), group_route(g, -1)) for g in range(n_groups)
    ]

    up = pl.pallas_call(
        up_kernel,
        out_shape=jax.ShapeDtypeStruct((in_width, fine_rows), features.dtype),
        grid_spec=pltpu.PrefetchScalarGridSpec(
            num_scalar_prefetch=2,
            grid=(blocks // UP_UNROLL,),
            in_specs=[
                pl.BlockSpec((in_width, UP_UNROLL * BLK), lambda i, *_: (0, i)),
                pl.BlockSpec((UP_UNROLL, BLK), lambda i, *_: (i, 0)),
                whole(w_up_t.shape),
            ]
            + [pl.BlockSpec(memory_space=pl.ANY)] * (1 + n_groups),
            out_specs=pl.BlockSpec((in_width, UP_UNROLL * BLK), lambda i, *_: (0, i)),
            scratch_shapes=[
                pltpu.VMEM((out_width, entries), jnp.bfloat16),
                pltpu.SemaphoreType.DMA((1 + n_groups,)),
            ],
        ),
        compiler_params=pltpu.CompilerParams(dimension_semantics=("arbitrary",)),
        cost_estimate=pl.CostEstimate(
            flops=6 * fine_rows * in_width * out_width,
            transcendentals=0,
            bytes_accessed=fine_rows * (in_width * 4 + 4) + entries * out_width * 2,
        ),
    )
    out_t = up(brick_window, block_offset, xt, entry_rows, w_up_t, answers[0], *returned)
    return out_t.T


def solution(mesh):
    in_specs = (
        P(("outer", "inner"), None),
        P(("outer", "inner")),
        P(("outer", "inner")),
        P(("outer", "inner"), None),
        P(),
        P(),
        P(),
    )
    out_specs = P(("outer", "inner"), None)
    return jax.shard_map(local, mesh=mesh, in_specs=in_specs, out_specs=out_specs, check_vma=False)
```

```python
import functools

import jax
import jax.numpy as jnp
from jax import lax
from jax.experimental import pallas as pl
from jax.experimental.pallas import tpu as pltpu
from jax.sharding import PartitionSpec as P

BLK = 128
C_DEV = 4096
SELF_CAP = 4096
WIN = 128
BRICKS_PER_STEP = 64
UNROLL = 16
UP_UNROLL = 64
WIN_UNROLL = 32

step_table = ((-1, -1), (-1, 0), (-1, 1), (0, -1), (0, 1), (1, -1), (1, 0), (1, 1))

NT = (((1,), (1,)), ((), ()))
TN = (((0,), (0,)), ((), ()))


def split_parts(data):
    high = data.astype(jnp.bfloat16)
    low = (data - high.astype(jnp.float32)).astype(jnp.bfloat16)
    return high, low


def one_hot_rows(index_row):
    span = lax.broadcasted_iota(jnp.int32, (WIN, index_row.shape[1]), 0)
    return (span == index_row).astype(jnp.bfloat16)


def down_kernel(first_window, count_ref, order_ref, win_ref, off_ref, cw_ref, xt_ref, e_ref, w_ref, cells_ref, *refs):
    outs = refs[:-1]
    acc = refs[-1]
    step = pl.program_id(0)
    per_step = e_ref.shape[0]
    trash = acc.shape[0] // WIN - 1

    @pl.when(step == 0)
    def _():
        acc[...] = jnp.zeros_like(acc)

    neighbours = count_ref[step]
    if first_window == 0:
        start, stop = neighbours, per_step
    else:
        start, stop = 0, neighbours

    def run(first, width, trips):
        def body(u, carry):
            results = []
            for t in range(width):
                position = first + u * width + t
                j = order_ref[step * per_step + jnp.minimum(position, per_step - 1)]
                brick = step * per_step + j
                window = jnp.where(position < stop, win_ref[brick] - first_window, trash)
                offset = off_ref[brick]
                inside = jnp.bitwise_and(e_ref[pl.ds(j, 1), :], WIN - 1)
                pick = one_hot_rows(inside)
                cols = pl.ds(pl.multiple_of(j * BLK, BLK), BLK)
                summed = lax.dot_general(pick, xt_ref[:, cols], NT, preferred_element_type=jnp.float32)
                part = jnp.dot(summed.astype(jnp.bfloat16), w_ref[offset], preferred_element_type=jnp.float32)
                results.append((window, part))
            for window, part in results:
                rows = pl.ds(pl.multiple_of(window * WIN, WIN), WIN)
                acc[rows, :] += part
            return carry

        lax.fori_loop(0, trips, body, 0)

    run(start, UNROLL, (stop - start + UNROLL - 1) // UNROLL)

    if first_window == 0:

        @pl.when(step == pl.num_programs(0) - 1)
        def _():
            cell_sum = outs[0]
            cell_sum[...] = jnp.zeros_like(cell_sum)
            cell_windows = cell_sum.shape[0] // WIN

            def gather_body(u, carry):
                results = []
                for t in range(WIN_UNROLL):
                    w = u * WIN_UNROLL + t
                    window = jnp.minimum(cw_ref[w], cell_windows - 1)
                    cells = cells_ref[pl.ds(w, 1), :]
                    inside = jnp.where(cells < C_DEV, cells - window * WIN, -1)
                    entries = acc[pl.ds(pl.multiple_of(w * WIN, WIN), WIN), :].astype(jnp.bfloat16)
                    rows = pl.ds(pl.multiple_of(window * WIN, WIN), WIN)
                    results.append((rows, jnp.dot(one_hot_rows(inside), entries, preferred_element_type=jnp.float32)))
                for rows, value in results:
                    cell_sum[rows, :] += value
                return carry

            lax.fori_loop(0, SELF_CAP // WIN // WIN_UNROLL, gather_body, 0)

    else:

        @pl.when(step == pl.num_programs(0) - 1)
        def _():
            size = outs[0].shape[0]
            for g, out in enumerate(outs):
                out[...] = acc[g * size : (g + 1) * size, :].astype(out.dtype)


def coarse_kernel(cw_ref, cells_ref, bias_ref, partial_ref, *refs):
    n_groups = len(step_table)
    sources = refs[:n_groups]
    outs = refs[n_groups : 1 + 2 * n_groups]
    acc, coarse = refs[1 + 2 * n_groups :]
    cell_windows = acc.shape[0] // WIN
    acc[...] = partial_ref[...]

    def pick_of(w):
        window = jnp.minimum(cw_ref[w], cell_windows - 1)
        cells = cells_ref[pl.ds(w, 1), :]
        inside = jnp.where(cells < C_DEV, cells - window * WIN, -1)
        rows = pl.ds(pl.multiple_of(window * WIN, WIN), WIN)
        return one_hot_rows(inside), rows

    base = SELF_CAP // WIN
    for src in sources:
        count = src.shape[0] // WIN
        unroll = min(WIN_UNROLL, count)

        def gather_body(u, carry, src=src, base=base, unroll=unroll):
            results = []
            for t in range(unroll):
                j = u * unroll + t
                pick, rows = pick_of(base + j)
                entries = src[pl.ds(pl.multiple_of(j * WIN, WIN), WIN), :]
                results.append((rows, jnp.dot(pick, entries, preferred_element_type=jnp.float32)))
            for rows, value in results:
                acc[rows, :] += value
            return carry

        lax.fori_loop(0, count // unroll, gather_body, 0)
        base += count

    coarse[...] = jnp.maximum(acc[...] + bias_ref[...], 0.0).astype(jnp.bfloat16)

    base = 0
    for out in outs:
        count = out.shape[1] // WIN
        unroll = min(WIN_UNROLL, count)

        def scatter_body(u, carry, out=out, base=base, unroll=unroll):
            for t in range(unroll):
                j = u * unroll + t
                pick, rows = pick_of(base + j)
                chosen = lax.dot_general(coarse[rows, :], pick, TN, preferred_element_type=jnp.float32)
                out[:, pl.ds(pl.multiple_of(j * WIN, WIN), WIN)] = chosen.astype(jnp.bfloat16)
            return carry

        lax.fori_loop(0, count // unroll, scatter_body, 0)
        base += count


def up_kernel(win_ref, off_ref, xt_ref, e_ref, wt_ref, *refs):
    n_groups = len(step_table)
    sources = refs[: 1 + n_groups]
    out_ref = refs[1 + n_groups]
    stack, sems = refs[2 + n_groups :]
    step = pl.program_id(0)
    per_step = e_ref.shape[0]

    @pl.when(step == 0)
    def _():
        copies = []
        start = 0
        for index, src in enumerate(sources):
            size = src.shape[1]
            copy = pltpu.make_async_copy(src, stack.at[:, pl.ds(start, size)], sems.at[index])
            copy.start()
            copies.append(copy)
            start += size
        for copy in copies:
            copy.wait()

    def body(u, carry):
        for t in range(UP_UNROLL):
            j = u * UP_UNROLL + t
            brick = step * per_step + j
            window = win_ref[brick]
            offset = off_ref[brick]
            inside = jnp.bitwise_and(e_ref[pl.ds(j, 1), :], WIN - 1)
            pick = one_hot_rows(inside)
            parents = stack[:, pl.ds(pl.multiple_of(window * WIN, WIN), WIN)]
            rows_t = jnp.dot(parents, pick, preferred_element_type=jnp.float32).astype(jnp.bfloat16)
            lifted = jnp.dot(wt_ref[offset], rows_t, preferred_element_type=jnp.float32)
            cols = pl.ds(pl.multiple_of(j * BLK, BLK), BLK)
            out_ref[:, cols] = (xt_ref[:, cols].astype(jnp.float32) + lifted).astype(out_ref.dtype)
        return carry

    lax.fori_loop(0, per_step // UP_UNROLL, body, 0)


def group_route(g, sign):
    n_outer = lax.axis_size("outer")
    n_inner = lax.axis_size("inner")
    a, b = step_table[g]
    route = []
    for s in range(n_outer * n_inner):
        row, col = divmod(s, n_inner)
        owner = ((row + a) % n_outer) * n_inner + (col + b) % n_inner
        route.append((s, owner) if sign > 0 else (owner, s))
    return route


def local(features, block_offset, parent_entry, owner_cell, w_down, b_down, w_up):
    n_groups = len(step_table)
    fine_rows, in_width = features.shape
    out_width = w_down.shape[2]
    entries = owner_cell.shape[1]
    cap = (entries - SELF_CAP) // n_groups
    blocks = fine_rows // BLK
    steps = blocks // BRICKS_PER_STEP

    xt = features.T
    entry_rows = parent_entry.reshape(blocks, BLK)
    brick_window = entry_rows[:, 0] // WIN
    cells = owner_cell.reshape(entries // WIN, WIN)
    cell_window = jnp.min(cells, axis=1) // WIN
    w_up_t = jnp.swapaxes(w_up, 1, 2)

    part_shapes = [jax.ShapeDtypeStruct((SELF_CAP, out_width), jnp.bfloat16)] + [
        jax.ShapeDtypeStruct((cap, out_width), jnp.bfloat16)
    ] * n_groups
    answer_shapes = [jax.ShapeDtypeStruct((s.shape[1], s.shape[0]), s.dtype) for s in part_shapes]
    whole = lambda shape: pl.BlockSpec(shape, lambda *idx: (0,) * len(shape))

    is_far = (brick_window >= SELF_CAP // WIN).astype(jnp.int32).reshape(steps, BRICKS_PER_STEP)
    far_count = jnp.sum(is_far, axis=1)
    far_rank = jnp.cumsum(is_far, axis=1) - is_far
    own_rank = jnp.cumsum(1 - is_far, axis=1) - (1 - is_far)
    position = jnp.where(is_far == 1, far_rank, far_count[:, None] + own_rank)
    local_ids = jnp.arange(BRICKS_PER_STEP, dtype=jnp.int32)
    order = jnp.sum(
        jnp.where(position[:, None, :] == local_ids[None, :, None], local_ids[None, None, :], 0), axis=2
    )
    order = order.reshape(blocks).astype(jnp.int32)
    counts = far_count.astype(jnp.int32)

    def down_call(first_window, shapes):
        rows = sum(s.shape[0] for s in shapes)
        return pl.pallas_call(
            functools.partial(down_kernel, first_window),
            out_shape=shapes,
            grid_spec=pltpu.PrefetchScalarGridSpec(
                num_scalar_prefetch=5,
                grid=(steps,),
                in_specs=[
                    pl.BlockSpec((in_width, BRICKS_PER_STEP * BLK), lambda i, *_: (0, i)),
                    pl.BlockSpec((BRICKS_PER_STEP, BLK), lambda i, *_: (i, 0)),
                    whole(w_down.shape),
                    whole(cells.shape),
                ],
                out_specs=[whole(s.shape) for s in shapes],
                scratch_shapes=[pltpu.VMEM((rows + WIN, out_width), jnp.float32)],
            ),
            compiler_params=pltpu.CompilerParams(dimension_semantics=("arbitrary",)),
            cost_estimate=pl.CostEstimate(
                flops=2 * fine_rows * in_width * out_width,
                transcendentals=0,
                bytes_accessed=fine_rows * (in_width * 2 + 4) + rows * out_width * 2,
            ),
        )(counts, order, brick_window, block_offset, cell_window, xt, entry_rows, w_down, cells)

    parts = [None] + list(down_call(SELF_CAP // WIN, part_shapes[1:]))
    cell_partial = down_call(0, [jax.ShapeDtypeStruct((C_DEV, out_width), jnp.float32)])[0]

    arrived = [
        lax.ppermute(parts[1 + g], ("outer", "inner"), group_route(g, 1)) for g in range(n_groups)
    ]

    coarse = pl.pallas_call(
        coarse_kernel,
        out_shape=answer_shapes,
        grid_spec=pltpu.PrefetchScalarGridSpec(
            num_scalar_prefetch=1,
            grid=(1,),
            in_specs=[whole(cells.shape), whole((1, out_width)), whole((C_DEV, out_width))]
            + [whole(s.shape) for s in part_shapes[1:]],
            out_specs=[whole(s.shape) for s in answer_shapes],
            scratch_shapes=[
                pltpu.VMEM((C_DEV, out_width), jnp.float32),
                pltpu.VMEM((C_DEV, out_width), jnp.bfloat16),
            ],
        ),
        cost_estimate=pl.CostEstimate(
            flops=4 * entries * WIN * out_width,
            transcendentals=0,
            bytes_accessed=4 * entries * out_width,
        ),
    )
    answers = coarse(cell_window, cells, b_down.reshape(1, out_width), cell_partial, *arrived)

    returned = [
        lax.ppermute(answers[1 + g], ("outer", "inner"), group_route(g, -1)) for g in range(n_groups)
    ]

    up = pl.pallas_call(
        up_kernel,
        out_shape=jax.ShapeDtypeStruct((in_width, fine_rows), features.dtype),
        grid_spec=pltpu.PrefetchScalarGridSpec(
            num_scalar_prefetch=2,
            grid=(steps,),
            in_specs=[
                pl.BlockSpec((in_width, BRICKS_PER_STEP * BLK), lambda i, *_: (0, i)),
                pl.BlockSpec((BRICKS_PER_STEP, BLK), lambda i, *_: (i, 0)),
                whole(w_up_t.shape),
            ]
            + [pl.BlockSpec(memory_space=pl.ANY)] * (1 + n_groups),
            out_specs=pl.BlockSpec((in_width, BRICKS_PER_STEP * BLK), lambda i, *_: (0, i)),
            scratch_shapes=[
                pltpu.VMEM((out_width, entries), jnp.bfloat16),
                pltpu.SemaphoreType.DMA((1 + n_groups,)),
            ],
        ),
        compiler_params=pltpu.CompilerParams(dimension_semantics=("arbitrary",)),
        cost_estimate=pl.CostEstimate(
            flops=6 * fine_rows * in_width * out_width,
            transcendentals=0,
            bytes_accessed=fine_rows * (in_width * 4 + 4) + entries * out_width * 2,
        ),
    )
    out_t = up(brick_window, block_offset, xt, entry_rows, w_up_t, answers[0], *returned)
    return out_t.T


def solution(mesh):
    in_specs = (
        P(("outer", "inner"), None),
        P(("outer", "inner")),
        P(("outer", "inner")),
        P(("outer", "inner"), None),
        P(),
        P(),
        P(),
    )
    out_specs = P(("outer", "inner"), None)
    return jax.shard_map(local, mesh=mesh, in_specs=in_specs, out_specs=out_specs, check_vma=False)
```

```python
import functools

import jax
import jax.numpy as jnp
from jax import lax
from jax.experimental import pallas as pl
from jax.experimental.pallas import tpu as pltpu
from jax.sharding import PartitionSpec as P

BLK = 128
C_DEV = 4096
SELF_CAP = 4096
WIN = 128
BRICKS_PER_STEP = 64
UNROLL = 16
UP_UNROLL = 64
WIN_UNROLL = 32

step_table = ((-1, -1), (-1, 0), (-1, 1), (0, -1), (0, 1), (1, -1), (1, 0), (1, 1))

NT = (((1,), (1,)), ((), ()))
TN = (((0,), (0,)), ((), ()))


def split_parts(data):
    high = data.astype(jnp.bfloat16)
    low = (data - high.astype(jnp.float32)).astype(jnp.bfloat16)
    return high, low


def one_hot_rows(index_row):
    span = lax.broadcasted_iota(jnp.int32, (WIN, index_row.shape[1]), 0)
    return (span == index_row).astype(jnp.bfloat16)


def down_kernel(first_window, count_ref, order_ref, win_ref, off_ref, xt_ref, e_ref, w_ref, *refs):
    outs = refs[:-1]
    acc = refs[-1]
    step = pl.program_id(0)
    per_step = e_ref.shape[0]
    trash = acc.shape[0] // WIN - 1

    @pl.when(step == 0)
    def _():
        acc[...] = jnp.zeros_like(acc)

    neighbours = count_ref[step]
    if first_window == 0:
        start, stop = neighbours, per_step
    else:
        start, stop = 0, neighbours

    def run(first, width, trips):
        def body(u, carry):
            results = []
            for t in range(width):
                position = first + u * width + t
                j = order_ref[step * per_step + jnp.minimum(position, per_step - 1)]
                brick = step * per_step + j
                window = jnp.where(position < stop, jnp.right_shift(win_ref[brick], 7) - first_window, trash)
                offset = off_ref[brick]
                inside = jnp.bitwise_and(e_ref[pl.ds(j, 1), :], WIN - 1)
                pick = one_hot_rows(inside)
                cols = pl.ds(pl.multiple_of(j * BLK, BLK), BLK)
                summed = lax.dot_general(pick, xt_ref[:, cols], NT, preferred_element_type=jnp.float32)
                part = jnp.dot(summed.astype(jnp.bfloat16), w_ref[offset], preferred_element_type=jnp.float32)
                results.append((window, part))
            for window, part in results:
                rows = pl.ds(pl.multiple_of(window * WIN, WIN), WIN)
                acc[rows, :] += part
            return carry

        lax.fori_loop(0, trips, body, 0)

    run(start, UNROLL, (stop - start + UNROLL - 1) // UNROLL)

    @pl.when(step == pl.num_programs(0) - 1)
    def _():
        size = outs[0].shape[0]
        for g, out in enumerate(outs):
            out[...] = acc[g * size : (g + 1) * size, :].astype(out.dtype)


def coarse_kernel(cw_ref, cells_ref, bias_ref, *refs):
    n_groups = len(step_table)
    sources = refs[: 1 + n_groups]
    outs = refs[1 + n_groups : 2 + 2 * n_groups]
    acc, coarse = refs[2 + 2 * n_groups :]
    cell_windows = acc.shape[0] // WIN
    acc[...] = jnp.zeros_like(acc)

    def pick_of(w):
        window = jnp.minimum(cw_ref[w], cell_windows - 1)
        cells = cells_ref[pl.ds(w, 1), :]
        inside = jnp.where(cells < C_DEV, cells - window * WIN, -1)
        rows = pl.ds(pl.multiple_of(window * WIN, WIN), WIN)
        return one_hot_rows(inside), rows

    base = 0
    for src in sources:
        count = src.shape[0] // WIN
        unroll = min(WIN_UNROLL, count)

        def gather_body(u, carry, src=src, base=base, unroll=unroll):
            results = []
            for t in range(unroll):
                j = u * unroll + t
                pick, rows = pick_of(base + j)
                entries = src[pl.ds(pl.multiple_of(j * WIN, WIN), WIN), :]
                results.append((rows, jnp.dot(pick, entries, preferred_element_type=jnp.float32)))
            for rows, value in results:
                acc[rows, :] += value
            return carry

        lax.fori_loop(0, count // unroll, gather_body, 0)
        base += count

    coarse[...] = jnp.maximum(acc[...] + bias_ref[...], 0.0).astype(jnp.bfloat16)

    base = 0
    for out in outs:
        count = out.shape[1] // WIN
        unroll = min(WIN_UNROLL, count)

        def scatter_body(u, carry, out=out, base=base, unroll=unroll):
            for t in range(unroll):
                j = u * unroll + t
                pick, rows = pick_of(base + j)
                chosen = lax.dot_general(coarse[rows, :], pick, TN, preferred_element_type=jnp.float32)
                out[:, pl.ds(pl.multiple_of(j * WIN, WIN), WIN)] = chosen.astype(jnp.bfloat16)
            return carry

        lax.fori_loop(0, count // unroll, scatter_body, 0)
        base += count


def up_kernel(win_ref, off_ref, xt_ref, e_ref, wt_ref, *refs):
    n_groups = len(step_table)
    sources = refs[: 1 + n_groups]
    out_ref = refs[1 + n_groups]
    stack, sems = refs[2 + n_groups :]
    step = pl.program_id(0)
    per_step = e_ref.shape[0]

    @pl.when(step == 0)
    def _():
        copies = []
        start = 0
        for index, src in enumerate(sources):
            size = src.shape[1]
            copy = pltpu.make_async_copy(src, stack.at[:, pl.ds(start, size)], sems.at[index])
            copy.start()
            copies.append(copy)
            start += size
        for copy in copies:
            copy.wait()

    def body(u, carry):
        for t in range(UP_UNROLL):
            j = u * UP_UNROLL + t
            brick = step * per_step + j
            window = jnp.right_shift(win_ref[brick], 7)
            offset = off_ref[brick]
            inside = jnp.bitwise_and(e_ref[pl.ds(j, 1), :], WIN - 1)
            pick = one_hot_rows(inside)
            parents = stack[:, pl.ds(pl.multiple_of(window * WIN, WIN), WIN)]
            rows_t = jnp.dot(parents, pick, preferred_element_type=jnp.float32).astype(jnp.bfloat16)
            lifted = jnp.dot(wt_ref[offset], rows_t, preferred_element_type=jnp.float32)
            cols = pl.ds(pl.multiple_of(j * BLK, BLK), BLK)
            out_ref[:, cols] = (xt_ref[:, cols].astype(jnp.float32) + lifted).astype(out_ref.dtype)
        return carry

    lax.fori_loop(0, per_step // UP_UNROLL, body, 0)


def group_route(g, sign):
    n_outer = lax.axis_size("outer")
    n_inner = lax.axis_size("inner")
    a, b = step_table[g]
    route = []
    for s in range(n_outer * n_inner):
        row, col = divmod(s, n_inner)
        owner = ((row + a) % n_outer) * n_inner + (col + b) % n_inner
        route.append((s, owner) if sign > 0 else (owner, s))
    return route


def local(features, block_offset, parent_entry, owner_cell, w_down, b_down, w_up):
    n_groups = len(step_table)
    fine_rows, in_width = features.shape
    out_width = w_down.shape[2]
    entries = owner_cell.shape[1]
    cap = (entries - SELF_CAP) // n_groups
    blocks = fine_rows // BLK
    steps = blocks // BRICKS_PER_STEP

    xt = features.T
    entry_rows = parent_entry.reshape(blocks, BLK)
    brick_first = entry_rows[:, 0]
    cells = owner_cell.reshape(entries // WIN, WIN)
    cell_window = jnp.min(cells, axis=1) // WIN
    w_up_t = jnp.swapaxes(w_up, 1, 2)

    part_shapes = [jax.ShapeDtypeStruct((SELF_CAP, out_width), jnp.bfloat16)] + [
        jax.ShapeDtypeStruct((cap, out_width), jnp.bfloat16)
    ] * n_groups
    answer_shapes = [jax.ShapeDtypeStruct((s.shape[1], s.shape[0]), s.dtype) for s in part_shapes]
    whole = lambda shape: pl.BlockSpec(shape, lambda *idx: (0,) * len(shape))

    is_far = (brick_first >= SELF_CAP).astype(jnp.int32).reshape(steps, BRICKS_PER_STEP)
    far_count = jnp.sum(is_far, axis=1)
    far_rank = jnp.cumsum(is_far, axis=1) - is_far
    own_rank = jnp.cumsum(1 - is_far, axis=1) - (1 - is_far)
    position = jnp.where(is_far == 1, far_rank, far_count[:, None] + own_rank)
    local_ids = jnp.arange(BRICKS_PER_STEP, dtype=jnp.int32)
    order = jnp.sum(
        jnp.where(position[:, None, :] == local_ids[None, :, None], local_ids[None, None, :], 0), axis=2
    )
    order = order.reshape(blocks).astype(jnp.int32)
    counts = far_count.astype(jnp.int32)

    def down_call(first_window, shapes):
        rows = sum(s.shape[0] for s in shapes)
        return pl.pallas_call(
            functools.partial(down_kernel, first_window),
            out_shape=shapes,
            grid_spec=pltpu.PrefetchScalarGridSpec(
                num_scalar_prefetch=4,
                grid=(steps,),
                in_specs=[
                    pl.BlockSpec((in_width, BRICKS_PER_STEP * BLK), lambda i, *_: (0, i)),
                    pl.BlockSpec((BRICKS_PER_STEP, BLK), lambda i, *_: (i, 0)),
                    whole(w_down.shape),
                ],
                out_specs=[whole(s.shape) for s in shapes],
                scratch_shapes=[pltpu.VMEM((rows + WIN, out_width), jnp.float32)],
            ),
            compiler_params=pltpu.CompilerParams(dimension_semantics=("arbitrary",)),
            cost_estimate=pl.CostEstimate(
                flops=2 * fine_rows * in_width * out_width,
                transcendentals=0,
                bytes_accessed=fine_rows * (in_width * 2 + 4) + rows * out_width * 2,
            ),
        )(counts, order, brick_first, block_offset, xt, entry_rows, w_down)

    parts = [None] + list(down_call(SELF_CAP // WIN, part_shapes[1:]))
    parts[0] = down_call(0, part_shapes[:1])[0]

    arrived = [
        lax.ppermute(parts[1 + g], ("outer", "inner"), group_route(g, 1)) for g in range(n_groups)
    ]

    coarse = pl.pallas_call(
        coarse_kernel,
        out_shape=answer_shapes,
        grid_spec=pltpu.PrefetchScalarGridSpec(
            num_scalar_prefetch=1,
            grid=(1,),
            in_specs=[whole(cells.shape), whole((1, out_width))]
            + [whole(s.shape) for s in part_shapes],
            out_specs=[whole(s.shape) for s in answer_shapes],
            scratch_shapes=[
                pltpu.VMEM((C_DEV, out_width), jnp.float32),
                pltpu.VMEM((C_DEV, out_width), jnp.bfloat16),
            ],
        ),
        cost_estimate=pl.CostEstimate(
            flops=4 * entries * WIN * out_width,
            transcendentals=0,
            bytes_accessed=4 * entries * out_width,
        ),
    )
    answers = coarse(cell_window, cells, b_down.reshape(1, out_width), parts[0], *arrived)

    returned = [
        lax.ppermute(answers[1 + g], ("outer", "inner"), group_route(g, -1)) for g in range(n_groups)
    ]

    up = pl.pallas_call(
        up_kernel,
        out_shape=jax.ShapeDtypeStruct((in_width, fine_rows), features.dtype),
        grid_spec=pltpu.PrefetchScalarGridSpec(
            num_scalar_prefetch=2,
            grid=(steps,),
            in_specs=[
                pl.BlockSpec((in_width, BRICKS_PER_STEP * BLK), lambda i, *_: (0, i)),
                pl.BlockSpec((BRICKS_PER_STEP, BLK), lambda i, *_: (i, 0)),
                whole(w_up_t.shape),
            ]
            + [pl.BlockSpec(memory_space=pl.ANY)] * (1 + n_groups),
            out_specs=pl.BlockSpec((in_width, BRICKS_PER_STEP * BLK), lambda i, *_: (0, i)),
            scratch_shapes=[
                pltpu.VMEM((out_width, entries), jnp.bfloat16),
                pltpu.SemaphoreType.DMA((1 + n_groups,)),
            ],
        ),
        compiler_params=pltpu.CompilerParams(dimension_semantics=("arbitrary",)),
        cost_estimate=pl.CostEstimate(
            flops=6 * fine_rows * in_width * out_width,
            transcendentals=0,
            bytes_accessed=fine_rows * (in_width * 4 + 4) + entries * out_width * 2,
        ),
    )
    out_t = up(brick_first, block_offset, xt, entry_rows, w_up_t, answers[0], *returned)
    return out_t.T


def solution(mesh):
    in_specs = (
        P(("outer", "inner"), None),
        P(("outer", "inner")),
        P(("outer", "inner")),
        P(("outer", "inner"), None),
        P(),
        P(),
        P(),
    )
    out_specs = P(("outer", "inner"), None)
    return jax.shard_map(local, mesh=mesh, in_specs=in_specs, out_specs=out_specs, check_vma=False)
```
